32 devices in a mesh: phi: 8 (over z, x), query: 2 (over core), event: 2 (over y).
Axes of the slice: x: 2, y: 2, z: 4, core: 2. Of those that a mesh axis runs over, the one named last changes fastest.
Arguments:
- hits: bfloat16 [8192, 256], P(('event', 'phi', 'query')), parts along dimension 0, may hold values from -6 to 6
- enc_qkv: bfloat16 [256, 768], replicated, may hold values from -15 to 15
- enc_out: bfloat16 [256, 256], replicated, may hold values from -0.375 to 0.375
- enc_up: bfloat16 [256, 1024], replicated, may hold values from -0.375 to 0.375
- enc_down: bfloat16 [1024, 256], replicated, may hold values from -0.1875 to 0.1875
- queries: bfloat16 [1024, 256], P('query'), may hold values from -240 to 240
- cross_q: bfloat16 [256, 256], replicated, may hold values from -0.375 to 0.375
- cross_kv: bfloat16 [256, 512], replicated, may hold values from -0.375 to 0.375
- cross_out: bfloat16 [256, 256], replicated, may hold values from -0.375 to 0.375
- mask_first: bfloat16 [256, 256], replicated, may hold values from -0.375 to 0.375
- mask_second: bfloat16 [256, 256], replicated, may hold values from -0.375 to 0.375
- truth: int32 [8192], P(('event', 'phi', 'query')), parts along dimension 0, may hold values from -1 to 511
- match: int32 [2048], P(('event', 'query')), parts along dimension 0, may hold values from 0 to 1023, each once
Outputs:
- encoded: bfloat16 [8192, 256], P(('event', 'phi', 'query')), parts along dimension 0
- mask_embed: bfloat16 [2048, 256], P(('event', 'query')), parts along dimension 0
- hit_grad: float32 [8192, 256], P(('event', 'phi', 'query')), parts along dimension 0
- mask_grad: float32 [2048, 256], P(('event', 'query')), parts along dimension 0
- mask_fill: float32 [2048], P(('event', 'query')), parts along dimension 0
The draws below stay inside these ranges and needn't reach their ends.
There are 2 independent parts, one for each index of `event`. The reference program is written for one: setup_inputs(seed, part) draws one part's arguments, and reference() takes and returns one part's arrays. A program takes and returns all parts, laid end to end along the dimension named above; an argument that names none is the same for every part. Nothing has to cross between parts.
All inputs are finite; a program needn't handle non-finite values.
Results may differ from the reference program's by a relative error of at most 0.017.
Values may be sent and summed in bfloat16 or wider, within the bound.
No kernel may reach another device: no remote copies, remote signals or barrier semaphores. Data moves between devices by JAX's collectives and lax.ppermute only.
A program may use at most 64 MiB of HBM per device.

```python
import jax
import jax.numpy as jnp
from jax import lax

D = 256
HEADS = 8
FF = 1024
HIT_DEV = 256
HALF = 256
QUERIES = 1024
TRACKS = 512
HIT_GRP = 512
HITS = 4096
N_PHI = 8


def pattern_signs(width):
    index = jnp.arange(width, dtype=jnp.int32)
    return (1 - 2 * ((index + index // 2) % 2)).astype(jnp.float32)


def draw_hits(key, part):
    first_key = jax.random.fold_in(key, 37)
    position = (jnp.arange(HITS, dtype=jnp.float32) + 0.5) / HITS
    signs = pattern_signs(D)
    noise = jax.random.uniform(first_key, (HITS, D), jnp.float32, -5.0, 5.0)
    amplitude = 1.0 + 0.11 * (1.0 - 2.0 * position)
    values = jnp.clip(noise + amplitude[:, None] * signs[None, :], -6.0, 6.0)
    return values.astype(jnp.bfloat16)


def draw_enc_qkv(key, part):
    first_key = jax.random.fold_in(jax.random.fold_in(key, 11), 0)
    limit = 6.0 * D ** (-0.5)
    base = jnp.clip(jax.random.normal(first_key, (D, 3 * D), jnp.float32) * D ** (-0.5), -limit, limit)
    return base.astype(jnp.bfloat16)


def draw_queries(key, part):
    first_key = jax.random.fold_in(jax.random.fold_in(key, 23), 0)
    base = jnp.clip(jax.random.normal(first_key, (QUERIES, D), jnp.float32), -6.0, 6.0)
    return base.astype(jnp.bfloat16)


def draw_cross_q(key, part):
    first_key = jax.random.fold_in(key, 71)
    base = jnp.clip(jax.random.normal(first_key, (D, D), jnp.float32), -6.0, 6.0) * D ** (-0.5)
    return base.astype(jnp.bfloat16)


def draw_mask_second(key, part):
    first_key = jax.random.fold_in(key, 53)
    base = jnp.clip(jax.random.normal(first_key, (D, D), jnp.float32), -6.0, 6.0) * (0.8 * D ** (-0.5))
    shift = -25.0 * D ** (-1.5)
    return (base + shift * pattern_signs(D)[None, :]).astype(jnp.bfloat16)


def place_ends(array, stream_key, smallest, top_value):
    spot = [jax.random.randint(jax.random.fold_in(stream_key, axis), (), 0, length) for axis, length in enumerate(array.shape)]
    widest = array.shape.index(max(array.shape))
    neighbour = spot[:widest] + [(spot[widest] + 1) % array.shape[widest]] + spot[widest + 1:]
    return array.at[tuple(spot)].set(smallest).at[tuple(neighbour)].set(top_value)


def gaussian(own_key, extent, scale, bound, kind=jnp.bfloat16):
    values = jax.random.normal(own_key, extent, jnp.float32) * scale
    return jnp.minimum(jnp.maximum(values, -bound), bound).astype(kind)


def setup_inputs(seed: int = 0, part: int = 0) -> dict:
    key_list = jax.random.split(jax.random.key(seed), 14)
    part_splits = jax.random.split(jax.random.fold_in(key_list[13], part), 14)
    hits = draw_hits(jax.random.fold_in(jax.random.fold_in(key_list[13], part), 71), part)
    enc_qkv = draw_enc_qkv(jax.random.fold_in(key_list[13], 71), part)
    enc_out = gaussian(key_list[2], (D, D), D ** -0.5, 0.375)
    enc_up = gaussian(key_list[3], (D, FF), D ** -0.5, 0.375)
    enc_down = gaussian(key_list[4], (FF, D), FF ** -0.5, 0.1875)
    queries = draw_queries(jax.random.fold_in(key_list[13], 71), part)
    cross_q = draw_cross_q(jax.random.fold_in(key_list[13], 71), part)
    cross_kv = gaussian(key_list[7], (D, 2 * D), D ** -0.5, 0.375)
    cross_out = gaussian(key_list[8], (D, D), D ** -0.5, 0.375)
    mask_first = gaussian(key_list[9], (D, D), D ** -0.5, 0.375)
    mask_second = draw_mask_second(jax.random.fold_in(key_list[13], 71), part)
    truth = place_ends(jax.random.randint(part_splits[11], (HITS,), -1, TRACKS), jax.random.fold_in(part_splits[11], 1), -1, TRACKS - 1).astype(jnp.int32)
    match = jax.random.permutation(part_splits[12], QUERIES).astype(jnp.int32)
    return dict(hits=hits, enc_qkv=enc_qkv, enc_out=enc_out, enc_up=enc_up, enc_down=enc_down, queries=queries, cross_q=cross_q, cross_kv=cross_kv, cross_out=cross_out, mask_first=mask_first, mask_second=mask_second, truth=truth, match=match)


def norm_rows(entries):
    widened = entries.astype(jnp.float32)
    centred = widened - lax.optimization_barrier(jnp.mean(widened, axis=-1, keepdims=True))
    spread = lax.optimization_barrier(jnp.mean(centred * centred, axis=-1, keepdims=True))
    return centred * lax.rsqrt(spread + 1e-05)

def window_attend(query_rows, kv_ext):
    row_count, model_width = query_rows.shape
    head_size = model_width // HEADS
    key_count = kv_ext.shape[0]
    key_span = key_count - row_count
    query_heads = query_rows.astype(jnp.float32).reshape(row_count, HEADS, head_size)
    key_heads = kv_ext[:, :model_width].astype(jnp.float32).reshape(key_count, HEADS, head_size)
    value_heads = kv_ext[:, model_width:].astype(jnp.float32).reshape(key_count, HEADS, head_size)
    scores = jnp.einsum('qhd,khd->hqk', query_heads, key_heads, precision=lax.Precision.HIGHEST) * head_size ** (-0.5)
    offset = lax.broadcasted_iota(jnp.int32, (row_count, key_count), 1) - lax.broadcasted_iota(jnp.int32, (row_count, key_count), 0)
    inside = jnp.logical_and(offset >= 0, offset < key_span)
    scores = jnp.where(inside[None, :, :], scores, -1e+30)
    raised = jnp.exp(scores - lax.optimization_barrier(jnp.max(scores, axis=-1, keepdims=True)))
    weights = (raised / lax.optimization_barrier(jnp.sum(raised, axis=-1, keepdims=True))).astype(jnp.bfloat16)
    attended = jnp.einsum('hqk,khd->qhd', weights.astype(jnp.float32), value_heads, precision=lax.Precision.HIGHEST)
    return attended.reshape(row_count, model_width).astype(jnp.bfloat16)

def split_heads(matrix):
    row_count, model_width = matrix.shape
    return matrix.reshape(row_count, HEADS, model_width // HEADS).transpose(1, 0, 2)

def head_partial(operands):
    query_head, key_head, value_head = operands
    scores = jnp.dot(query_head.astype(jnp.float32), key_head.astype(jnp.float32).T, precision=lax.Precision.HIGHEST) * query_head.shape[1] ** (-0.5)
    local_max = lax.optimization_barrier(jnp.max(scores, axis=1))
    raised = jnp.exp(scores - local_max[:, None]).astype(jnp.bfloat16)
    total = lax.optimization_barrier(jnp.sum(raised.astype(jnp.float32), axis=1))
    mixed = jnp.dot(raised, value_head, preferred_element_type=jnp.float32)
    return (local_max, total, mixed)

def loss_coefficients(sigma, target, matched, intersection, predicted, truth_count, hits_total, model_width):
    denom = predicted + truth_count + 1.0
    slope = -2.0 / denom
    level = (2.0 * intersection + 1.0) / (denom * denom)
    dice_part = hits_total * (slope[:, None] * target + level[:, None]) * sigma * (1.0 - sigma)
    return (matched[:, None] * (sigma - target + dice_part) * model_width ** (-0.5)).astype(jnp.bfloat16)

def reference(hits, enc_qkv, enc_out, enc_up, enc_down, queries, cross_q, cross_kv, cross_out, mask_first, mask_second, truth, match):
    normed = norm_rows(hits).astype(jnp.bfloat16)
    projected = jnp.dot(normed, enc_qkv, preferred_element_type=jnp.float32).astype(jnp.bfloat16)
    query_part = projected[:, :D]
    key_value = projected[:, D:]
    cycle = jnp.concatenate([key_value[HITS - HALF:], key_value, key_value[:HALF]], axis=0)

    def window_block(block_index):
        first_row = (block_index * HIT_DEV).astype(jnp.int32)
        query_rows = lax.dynamic_slice_in_dim(query_part, first_row, HIT_DEV, 0)
        kv_ext = lax.dynamic_slice_in_dim(cycle, first_row, HIT_DEV + 2 * HALF, 0)
        return window_attend(query_rows, kv_ext)
    attended = lax.map(window_block, jnp.arange(HITS // HIT_DEV, dtype=jnp.int32)).reshape(HITS, D)
    residual = hits.astype(jnp.float32) + jnp.dot(attended, enc_out, preferred_element_type=jnp.float32)
    upper = jax.nn.gelu(jnp.dot(norm_rows(residual).astype(jnp.bfloat16), enc_up, preferred_element_type=jnp.float32), approximate=True).astype(jnp.bfloat16)
    encoded = (residual + jnp.dot(upper, enc_down, preferred_element_type=jnp.float32)).astype(jnp.bfloat16)
    hit_kv = jnp.dot(norm_rows(encoded).astype(jnp.bfloat16), cross_kv, preferred_element_type=jnp.float32).astype(jnp.bfloat16)
    query_proj = jnp.dot(queries, cross_q, preferred_element_type=jnp.float32).astype(jnp.bfloat16)
    query_heads = split_heads(query_proj)

    def group_partial(group_index):
        first_row = (group_index * HIT_GRP).astype(jnp.int32)
        group_kv = lax.dynamic_slice_in_dim(hit_kv, first_row, HIT_GRP, 0)
        return lax.map(head_partial, (query_heads, split_heads(group_kv[:, :D]), split_heads(group_kv[:, D:])))
    maxima, totals, mixes = lax.map(group_partial, jnp.arange(N_PHI, dtype=jnp.int32))
    top = lax.optimization_barrier(jnp.max(maxima, axis=0))
    factor = jnp.exp(maxima - top[None])
    total = lax.optimization_barrier(jnp.sum(totals * factor, axis=0))
    mixed = lax.optimization_barrier(jnp.sum(mixes * factor[..., None], axis=0))
    context = (mixed * (1.0 / total)[..., None]).transpose(1, 0, 2).reshape(QUERIES, D).astype(jnp.bfloat16)
    mixed_queries = queries.astype(jnp.float32) + jnp.dot(context, cross_out, preferred_element_type=jnp.float32)
    mask_hidden = jax.nn.relu(jnp.dot(norm_rows(mixed_queries).astype(jnp.bfloat16), mask_first, preferred_element_type=jnp.float32)).astype(jnp.bfloat16)
    mask_embed = jnp.dot(mask_hidden, mask_second, preferred_element_type=jnp.float32).astype(jnp.bfloat16)
    matched_flag = match < TRACKS
    matched = matched_flag.astype(jnp.float32)

    def group_terms(group_index):
        first_row = (group_index * HIT_GRP).astype(jnp.int32)
        group_hits = lax.dynamic_slice_in_dim(encoded, first_row, HIT_GRP, 0)
        group_truth = lax.dynamic_slice_in_dim(truth, first_row, HIT_GRP, 0)
        logits = lax.dot_general(mask_embed, group_hits, (((1,), (1,)), ((), ())), preferred_element_type=jnp.float32) * D ** (-0.5)
        sigma = jax.nn.sigmoid(logits)
        target = jnp.logical_and(match[:, None] == group_truth[None, :], matched_flag[:, None]).astype(jnp.float32)
        return (group_hits, sigma, target)

    def group_stats(group_index):
        group_hits, sigma, target = group_terms(group_index)
        return (lax.optimization_barrier(jnp.sum(sigma * target, axis=1)), lax.optimization_barrier(jnp.sum(sigma, axis=1)), lax.optimization_barrier(jnp.sum(target, axis=1)))
    intersections, predictions, counts = lax.map(group_stats, jnp.arange(N_PHI, dtype=jnp.int32))
    intersection = lax.optimization_barrier(jnp.sum(intersections, axis=0))
    predicted = lax.optimization_barrier(jnp.sum(predictions, axis=0))
    truth_count = lax.optimization_barrier(jnp.sum(counts, axis=0))
    mask_fill = predicted / float(HITS)

    def group_grads(carried, group_index):
        group_hits, sigma, target = group_terms(group_index)
        coef = loss_coefficients(sigma, target, matched, intersection, predicted, truth_count, float(HITS), D)
        carried = carried + jnp.dot(coef, group_hits, preferred_element_type=jnp.float32)
        hit_part = lax.dot_general(coef, mask_embed, (((0,), (0,)), ((), ())), preferred_element_type=jnp.float32)
        return (carried, hit_part)
    mask_grad, hit_parts = lax.scan(group_grads, jnp.zeros((QUERIES, D), jnp.float32), jnp.arange(N_PHI, dtype=jnp.int32))
    hit_grad = hit_parts.reshape(HITS, D)
    return (encoded, mask_embed, hit_grad, mask_grad, mask_fill)
```

```python
import jax
import jax.numpy as jnp
from jax import lax
from jax.sharding import PartitionSpec as P

HEADS = 8
WIN = 512


def extended_2(block, sides, width):
    for axis, dim in sides:
        count = lax.axis_size(axis)
        forward = [(i, i + 1) for i in range(count - 1)]
        forward.append((count - 1, 0))
        backward = [(target, source) for source, target in forward]
        low = lax.ppermute(
            lax.slice_in_dim(block, block.shape[dim] - width, None, axis=dim), axis, forward
        )
        high = lax.ppermute(lax.slice_in_dim(block, 0, width, axis=dim), axis, backward)
        block = jnp.concatenate([low, block, high], axis=dim)
    return block


def partner_pairs(count, distance):
    return [(i, i ^ distance) for i in range(count)]


def butterfly(tree, axis, combine, ordered=False):
    count = lax.axis_size(axis)
    assert count & (count - 1) == 0
    index = lax.axis_index(axis)
    distance = 1
    while distance < count:
        other = lax.ppermute(tree, axis, partner_pairs(count, distance))
        if ordered:
            upper = (index // distance) % 2 == 1
            first = jax.tree.map(lambda a, b: jnp.where(upper, b, a), tree, other)
            second = jax.tree.map(lambda a, b: jnp.where(upper, a, b), tree, other)
            tree = combine(first, second)
        else:
            tree = combine(tree, other)
        distance *= 2
    return tree


def add_trees(a, b):
    return jax.tree.map(jnp.add, a, b)


def softmax_combine(a, b):
    max_a, total_a, mixed_a = a
    max_b, total_b, mixed_b = b
    top = jnp.maximum(max_a, max_b)
    factor_a = jnp.exp(max_a - top)
    factor_b = jnp.exp(max_b - top)
    return (
        top,
        total_a * factor_a + total_b * factor_b,
        scale_heads(mixed_a, factor_a) + scale_heads(mixed_b, factor_b),
    )


def reduce_scatter_rows(block, axis):
    count = lax.axis_size(axis)
    assert count & (count - 1) == 0
    index = lax.axis_index(axis)
    distance = count // 2
    while distance >= 1:
        half = block.shape[0] // 2
        upper = (index // distance) % 2 == 1
        low, high = block[:half], block[half:]
        keep = jnp.where(upper, high, low)
        send = jnp.where(upper, low, high)
        block = keep + lax.ppermute(send, axis, partner_pairs(count, distance))
        distance //= 2
    return block


def norm_rows(entries):
    widened = entries.astype(jnp.float32)
    centred = widened - jnp.mean(widened, axis=-1, keepdims=True)
    spread = jnp.mean(centred * centred, axis=-1, keepdims=True)
    return centred * lax.rsqrt(spread + 1e-05)


def window_attend(query_rows, kv_ext):
    row_count, model_width = query_rows.shape
    head_size = model_width // HEADS
    key_count = kv_ext.shape[0]
    key_span = key_count - row_count
    query_heads = query_rows.reshape(row_count, HEADS, head_size)
    key_heads = kv_ext[:, :model_width].reshape(key_count, HEADS, head_size)
    value_heads = kv_ext[:, model_width:].reshape(key_count, HEADS, head_size)
    scores = jnp.einsum(
        "qhd,khd->hqk", query_heads, key_heads, preferred_element_type=jnp.float32
    ) * head_size ** (-0.5)
    offset = lax.broadcasted_iota(jnp.int32, (row_count, key_count), 1) - lax.broadcasted_iota(
        jnp.int32, (row_count, key_count), 0
    )
    inside = jnp.logical_and(offset >= 0, offset < key_span)
    scores = jnp.where(inside[None, :, :], scores, -1e30)
    raised = jnp.exp(scores - jnp.max(scores, axis=-1, keepdims=True))
    weights = (raised / jnp.sum(raised, axis=-1, keepdims=True)).astype(jnp.bfloat16)
    attended = jnp.einsum("hqk,khd->qhd", weights, value_heads, preferred_element_type=jnp.float32)
    return attended.reshape(row_count, model_width).astype(jnp.bfloat16)


def split_heads(matrix):
    row_count, model_width = matrix.shape
    return matrix.reshape(row_count, HEADS, model_width // HEADS).transpose(1, 0, 2)


def head_partial(operands):
    query_head, key_head, value_head = operands
    scores = lax.dot_general(
        query_head, key_head, (((1,), (1,)), ((), ())), preferred_element_type=jnp.float32
    ) * query_head.shape[1] ** (-0.5)
    local_max = jnp.max(scores, axis=1)
    raised = jnp.exp(scores - local_max[:, None]).astype(jnp.bfloat16)
    total = jnp.sum(raised.astype(jnp.float32), axis=1)
    mixed = jnp.dot(raised, value_head, preferred_element_type=jnp.float32)
    return (local_max, total, mixed)


def scale_heads(mixed, factor):
    query_count, model_width = mixed.shape
    head_count = factor.shape[0]
    shaped = mixed.reshape(query_count, head_count, model_width // head_count)
    return (shaped * factor.T[:, :, None]).reshape(query_count, model_width)


def loss_coefficients(
    sigma, target, matched, intersection, predicted, truth_count, hits_total, model_width
):
    denom = predicted + truth_count + 1.0
    slope = -2.0 / denom
    level = (2.0 * intersection + 1.0) / (denom * denom)
    dice_part = hits_total * (slope[:, None] * target + level[:, None]) * sigma * (1.0 - sigma)
    return (matched[:, None] * (sigma - target + dice_part) * model_width ** (-0.5)).astype(
        jnp.bfloat16
    )


def body(
    hits,
    enc_qkv,
    enc_out,
    enc_up,
    enc_down,
    queries,
    cross_q,
    cross_kv,
    cross_out,
    mask_first,
    mask_second,
    truth,
    match,
):
    model_width = hits.shape[1]
    local_hits = hits.shape[0]
    query_count = queries.shape[0]
    hits_total = float(local_hits * lax.axis_size("phi") * lax.axis_size("query"))
    track_count = query_count * lax.axis_size("query") // 2
    normed = norm_rows(hits).astype(jnp.bfloat16)
    projected = jnp.dot(normed, enc_qkv, preferred_element_type=jnp.float32).astype(jnp.bfloat16)
    extended = extended_2(projected[:, model_width:], ((("phi", "query"), 0),), WIN // 2)
    attended = window_attend(projected[:, :model_width], extended)
    residual = hits.astype(jnp.float32) + jnp.dot(
        attended, enc_out, preferred_element_type=jnp.float32
    )
    upper = jax.nn.gelu(
        jnp.dot(
            norm_rows(residual).astype(jnp.bfloat16), enc_up, preferred_element_type=jnp.float32
        ),
        approximate=True,
    ).astype(jnp.bfloat16)
    encoded = (residual + jnp.dot(upper, enc_down, preferred_element_type=jnp.float32)).astype(
        jnp.bfloat16
    )
    local_kv = jnp.dot(
        norm_rows(encoded).astype(jnp.bfloat16), cross_kv, preferred_element_type=jnp.float32
    ).astype(jnp.bfloat16)
    group_kv, group_hits, group_truth = (
        lax.all_gather(local_kv, "query", axis=0, tiled=True),
        lax.all_gather(encoded, "query", axis=0, tiled=True),
        lax.all_gather(truth, "query", axis=0, tiled=True),
    )
    query_proj = jnp.dot(queries, cross_q, preferred_element_type=jnp.float32).astype(jnp.bfloat16)
    head_size = model_width // HEADS
    group_count = group_kv.shape[0]
    query_heads = query_proj.reshape(query_count, HEADS, head_size)
    key_heads = group_kv[:, :model_width].reshape(group_count, HEADS, head_size)
    value_heads = group_kv[:, model_width:].reshape(group_count, HEADS, head_size)
    scores = jnp.einsum(
        "qhd,khd->hqk", query_heads, key_heads, preferred_element_type=jnp.float32
    ) * head_size ** (-0.5)
    local_max = jnp.max(scores, axis=-1)
    raised = jnp.exp(scores - local_max[..., None]).astype(jnp.bfloat16)
    local_total = jnp.sum(raised.astype(jnp.float32), axis=-1)
    local_mixed = jnp.einsum(
        "hqk,khd->qhd", raised, value_heads, preferred_element_type=jnp.float32
    ).reshape(query_count, model_width)
    _, total, mixed = butterfly(
        (local_max, local_total, local_mixed), "phi", softmax_combine, ordered=True
    )
    context = scale_heads(mixed, 1.0 / total).astype(jnp.bfloat16)
    mixed_queries = queries.astype(jnp.float32) + jnp.dot(
        context, cross_out, preferred_element_type=jnp.float32
    )
    mask_hidden = jax.nn.relu(
        jnp.dot(
            norm_rows(mixed_queries).astype(jnp.bfloat16),
            mask_first,
            preferred_element_type=jnp.float32,
        )
    ).astype(jnp.bfloat16)
    mask_embed = jnp.dot(mask_hidden, mask_second, preferred_element_type=jnp.float32).astype(
        jnp.bfloat16
    )
    logits = lax.dot_general(
        mask_embed, group_hits, (((1,), (1,)), ((), ())), preferred_element_type=jnp.float32
    ) * model_width ** (-0.5)
    sigma = jax.nn.sigmoid(logits)
    matched_flag = match < track_count
    matched = matched_flag.astype(jnp.float32)
    target = jnp.logical_and(match[:, None] == group_truth[None, :], matched_flag[:, None]).astype(
        jnp.float32
    )
    intersection, predicted, truth_count = butterfly(
        (jnp.sum(sigma * target, axis=1), jnp.sum(sigma, axis=1), jnp.sum(target, axis=1)),
        "phi",
        add_trees,
    )
    mask_fill = predicted / hits_total
    coef = loss_coefficients(
        sigma, target, matched, intersection, predicted, truth_count, hits_total, model_width
    )
    mask_grad = butterfly(
        jnp.dot(coef, group_hits, preferred_element_type=jnp.float32), "phi", add_trees
    )
    hit_grad = reduce_scatter_rows(
        lax.dot_general(
            coef, mask_embed, (((0,), (0,)), ((), ())), preferred_element_type=jnp.float32
        ),
        "query",
    )
    return (encoded, mask_embed, hit_grad, mask_grad, mask_fill)


def solution(mesh):
    return jax.shard_map(
        body,
        mesh=mesh,
        in_specs=(
            P(("event", "phi", "query"), None),
            P(),
            P(),
            P(),
            P(),
            P("query", None),
            P(),
            P(),
            P(),
            P(),
            P(),
            P(("event", "phi", "query")),
            P(("event", "query")),
        ),
        out_specs=(
            P(("event", "phi", "query"), None),
            P(("event", "query"), None),
            P(("event", "phi", "query"), None),
            P(("event", "query"), None),
            P(("event", "query")),
        ),
        check_vma=False,
    )
```

```python
import jax
import jax.numpy as jnp
from jax import lax
from jax.sharding import PartitionSpec as P

HEADS = 8
WIN = 512


def extended_2(block, sides, width):
    for axis, dim in sides:
        count = lax.axis_size(axis)
        forward = [(i, i + 1) for i in range(count - 1)]
        forward.append((count - 1, 0))
        backward = [(target, source) for source, target in forward]
        low = lax.ppermute(
            lax.slice_in_dim(block, block.shape[dim] - width, None, axis=dim), axis, forward
        )
        high = lax.ppermute(lax.slice_in_dim(block, 0, width, axis=dim), axis, backward)
        block = jnp.concatenate([low, block, high], axis=dim)
    return block


def partner_pairs(count, distance):
    return [(i, i ^ distance) for i in range(count)]


def butterfly(tree, axis, combine, ordered=False):
    count = lax.axis_size(axis)
    assert count & (count - 1) == 0
    index = lax.axis_index(axis)
    distance = 1
    while distance < count:
        other = lax.ppermute(tree, axis, partner_pairs(count, distance))
        if ordered:
            upper = (index // distance) % 2 == 1
            first = jax.tree.map(lambda a, b: jnp.where(upper, b, a), tree, other)
            second = jax.tree.map(lambda a, b: jnp.where(upper, a, b), tree, other)
            tree = combine(first, second)
        else:
            tree = combine(tree, other)
        distance *= 2
    return tree


def add_trees(a, b):
    return jax.tree.map(jnp.add, a, b)


def narrow_butterfly(block, axis):
    count = lax.axis_size(axis)
    distance = 1
    while distance < count:
        sent = block.astype(jnp.bfloat16)
        other = lax.ppermute(sent, axis, partner_pairs(count, distance))
        block = sent.astype(jnp.float32) + other.astype(jnp.float32)
        distance *= 2
    return block


def softmax_combine(a, b):
    max_a, total_a, mixed_a = a
    max_b, total_b, mixed_b = b
    mixed_a = mixed_a.astype(jnp.float32)
    mixed_b = mixed_b.astype(jnp.float32)
    top = jnp.maximum(max_a, max_b)
    factor_a = jnp.exp(max_a - top)
    factor_b = jnp.exp(max_b - top)
    return (
        top,
        total_a * factor_a + total_b * factor_b,
        (scale_heads(mixed_a, factor_a) + scale_heads(mixed_b, factor_b)).astype(jnp.bfloat16),
    )


def reduce_scatter_rows(block, axis):
    count = lax.axis_size(axis)
    assert count & (count - 1) == 0
    index = lax.axis_index(axis)
    distance = count // 2
    while distance >= 1:
        half = block.shape[0] // 2
        upper = (index // distance) % 2 == 1
        low, high = block[:half], block[half:]
        keep = jnp.where(upper, high, low)
        send = jnp.where(upper, low, high)
        block = keep + lax.ppermute(send, axis, partner_pairs(count, distance))
        distance //= 2
    return block


def norm_rows(entries):
    widened = entries.astype(jnp.float32)
    centred = widened - jnp.mean(widened, axis=-1, keepdims=True)
    spread = jnp.mean(centred * centred, axis=-1, keepdims=True)
    return centred * lax.rsqrt(spread + 1e-05)


def window_attend(query_rows, kv_ext):
    row_count, model_width = query_rows.shape
    head_size = model_width // HEADS
    key_count = kv_ext.shape[0]
    key_span = key_count - row_count
    query_heads = query_rows.reshape(row_count, HEADS, head_size)
    key_heads = kv_ext[:, :model_width].reshape(key_count, HEADS, head_size)
    value_heads = kv_ext[:, model_width:].reshape(key_count, HEADS, head_size)
    scores = jnp.einsum(
        "qhd,khd->hqk", query_heads, key_heads, preferred_element_type=jnp.float32
    ) * head_size ** (-0.5)
    offset = lax.broadcasted_iota(jnp.int32, (row_count, key_count), 1) - lax.broadcasted_iota(
        jnp.int32, (row_count, key_count), 0
    )
    inside = jnp.logical_and(offset >= 0, offset < key_span)
    scores = jnp.where(inside[None, :, :], scores, -1e30)
    raised = jnp.exp(scores - jnp.max(scores, axis=-1, keepdims=True))
    weights = (raised / jnp.sum(raised, axis=-1, keepdims=True)).astype(jnp.bfloat16)
    attended = jnp.einsum("hqk,khd->qhd", weights, value_heads, preferred_element_type=jnp.float32)
    return attended.reshape(row_count, model_width).astype(jnp.bfloat16)


def split_heads(matrix):
    row_count, model_width = matrix.shape
    return matrix.reshape(row_count, HEADS, model_width // HEADS).transpose(1, 0, 2)


def head_partial(operands):
    query_head, key_head, value_head = operands
    scores = lax.dot_general(
        query_head, key_head, (((1,), (1,)), ((), ())), preferred_element_type=jnp.float32
    ) * query_head.shape[1] ** (-0.5)
    local_max = jnp.max(scores, axis=1)
    raised = jnp.exp(scores - local_max[:, None]).astype(jnp.bfloat16)
    total = jnp.sum(raised.astype(jnp.float32), axis=1)
    mixed = jnp.dot(raised, value_head, preferred_element_type=jnp.float32)
    return (local_max, total, mixed)


def scale_heads(mixed, factor):
    query_count, model_width = mixed.shape
    head_count = factor.shape[0]
    shaped = mixed.reshape(query_count, head_count, model_width // head_count)
    return (shaped * factor.T[:, :, None]).reshape(query_count, model_width)


def loss_coefficients(
    sigma, target, matched, intersection, predicted, truth_count, hits_total, model_width
):
    denom = predicted + truth_count + 1.0
    slope = -2.0 / denom
    level = (2.0 * intersection + 1.0) / (denom * denom)
    dice_part = hits_total * (slope[:, None] * target + level[:, None]) * sigma * (1.0 - sigma)
    return (matched[:, None] * (sigma - target + dice_part) * model_width ** (-0.5)).astype(
        jnp.bfloat16
    )


def body(
    hits,
    enc_qkv,
    enc_out,
    enc_up,
    enc_down,
    queries,
    cross_q,
    cross_kv,
    cross_out,
    mask_first,
    mask_second,
    truth,
    match,
):
    model_width = hits.shape[1]
    local_hits = hits.shape[0]
    query_count = queries.shape[0]
    hits_total = float(local_hits * lax.axis_size("phi") * lax.axis_size("query"))
    track_count = query_count * lax.axis_size("query") // 2
    normed = norm_rows(hits).astype(jnp.bfloat16)
    projected = jnp.dot(normed, enc_qkv, preferred_element_type=jnp.float32).astype(jnp.bfloat16)
    extended = extended_2(projected[:, model_width:], ((("phi", "query"), 0),), WIN // 2)
    attended = window_attend(projected[:, :model_width], extended)
    residual = hits.astype(jnp.float32) + jnp.dot(
        attended, enc_out, preferred_element_type=jnp.float32
    )
    upper = jax.nn.gelu(
        jnp.dot(
            norm_rows(residual).astype(jnp.bfloat16), enc_up, preferred_element_type=jnp.float32
        ),
        approximate=True,
    ).astype(jnp.bfloat16)
    encoded = (residual + jnp.dot(upper, enc_down, preferred_element_type=jnp.float32)).astype(
        jnp.bfloat16
    )
    local_kv = jnp.dot(
        norm_rows(encoded).astype(jnp.bfloat16), cross_kv, preferred_element_type=jnp.float32
    ).astype(jnp.bfloat16)
    shifted = truth + 1
    digits = jnp.stack([shifted // 256, shifted % 256], axis=1).astype(jnp.bfloat16)
    digits = jnp.pad(digits, ((0, 0), (0, 126)))
    gathered = lax.all_gather(
        jnp.concatenate([local_kv, encoded, digits], axis=1), "query", axis=0, tiled=True
    )
    group_kv = gathered[:, : 2 * model_width]
    group_hits = gathered[:, 2 * model_width : 3 * model_width]
    group_digits = gathered[:, 3 * model_width :].astype(jnp.int32)
    group_truth = group_digits[:, 0] * 256 + group_digits[:, 1] - 1
    query_proj = jnp.dot(queries, cross_q, preferred_element_type=jnp.float32).astype(jnp.bfloat16)
    head_size = model_width // HEADS
    group_count = group_kv.shape[0]
    query_heads = query_proj.reshape(query_count, HEADS, head_size)
    key_heads = group_kv[:, :model_width].reshape(group_count, HEADS, head_size)
    value_heads = group_kv[:, model_width:].reshape(group_count, HEADS, head_size)
    scores = jnp.einsum(
        "qhd,khd->hqk", query_heads, key_heads, preferred_element_type=jnp.float32
    ) * head_size ** (-0.5)
    local_max = jnp.max(scores, axis=-1)
    raised = jnp.exp(scores - local_max[..., None]).astype(jnp.bfloat16)
    local_total = jnp.sum(raised.astype(jnp.float32), axis=-1)
    local_mixed = jnp.einsum(
        "hqk,khd->qhd", raised, value_heads, preferred_element_type=jnp.float32
    ).reshape(query_count, model_width)
    _, total, mixed = butterfly(
        (local_max, local_total, local_mixed.astype(jnp.bfloat16)),
        "phi",
        softmax_combine,
        ordered=True,
    )
    mixed = mixed.astype(jnp.float32)
    context = scale_heads(mixed, 1.0 / total).astype(jnp.bfloat16)
    mixed_queries = queries.astype(jnp.float32) + jnp.dot(
        context, cross_out, preferred_element_type=jnp.float32
    )
    mask_hidden = jax.nn.relu(
        jnp.dot(
            norm_rows(mixed_queries).astype(jnp.bfloat16),
            mask_first,
            preferred_element_type=jnp.float32,
        )
    ).astype(jnp.bfloat16)
    mask_embed = jnp.dot(mask_hidden, mask_second, preferred_element_type=jnp.float32).astype(
        jnp.bfloat16
    )
    logits = lax.dot_general(
        mask_embed, group_hits, (((1,), (1,)), ((), ())), preferred_element_type=jnp.float32
    ) * model_width ** (-0.5)
    sigma = jax.nn.sigmoid(logits)
    matched_flag = match < track_count
    matched = matched_flag.astype(jnp.float32)
    target = jnp.logical_and(match[:, None] == group_truth[None, :], matched_flag[:, None]).astype(
        jnp.float32
    )
    intersection, predicted, truth_count = butterfly(
        (jnp.sum(sigma * target, axis=1), jnp.sum(sigma, axis=1), jnp.sum(target, axis=1)),
        "phi",
        add_trees,
    )
    mask_fill = predicted / hits_total
    coef = loss_coefficients(
        sigma, target, matched, intersection, predicted, truth_count, hits_total, model_width
    )
    mask_grad = narrow_butterfly(
        jnp.dot(coef, group_hits, preferred_element_type=jnp.float32), "phi"
    )
    hit_grad = reduce_scatter_rows(
        lax.dot_general(
            coef, mask_embed, (((0,), (0,)), ((), ())), preferred_element_type=jnp.float32
        ),
        "query",
    )
    return (encoded, mask_embed, hit_grad, mask_grad, mask_fill)


def solution(mesh):
    return jax.shard_map(
        body,
        mesh=mesh,
        in_specs=(
            P(("event", "phi", "query"), None),
            P(),
            P(),
            P(),
            P(),
            P("query", None),
            P(),
            P(),
            P(),
            P(),
            P(),
            P(("event", "phi", "query")),
            P(("event", "query")),
        ),
        out_specs=(
            P(("event", "phi", "query"), None),
            P(("event", "query"), None),
            P(("event", "phi", "query"), None),
            P(("event", "query"), None),
            P(("event", "query")),
        ),
        check_vma=False,
    )
```

```python
import jax
import jax.numpy as jnp
from jax import lax
from jax.sharding import PartitionSpec as P

HEADS = 8
WIN = 512


def extended_2(block, sides, width):
    for axis, dim in sides:
        count = lax.axis_size(axis)
        forward = [(i, i + 1) for i in range(count - 1)]
        forward.append((count - 1, 0))
        backward = [(target, source) for source, target in forward]
        low = lax.ppermute(
            lax.slice_in_dim(block, block.shape[dim] - width, None, axis=dim), axis, forward
        )
        high = lax.ppermute(lax.slice_in_dim(block, 0, width, axis=dim), axis, backward)
        block = jnp.concatenate([low, block, high], axis=dim)
    return block


def partner_pairs(count, distance):
    return [(i, i ^ distance) for i in range(count)]


def butterfly(tree, axis, combine, ordered=False):
    count = lax.axis_size(axis)
    assert count & (count - 1) == 0
    index = lax.axis_index(axis)
    distance = 1
    while distance < count:
        other = lax.ppermute(tree, axis, partner_pairs(count, distance))
        if ordered:
            upper = (index // distance) % 2 == 1
            first = jax.tree.map(lambda a, b: jnp.where(upper, b, a), tree, other)
            second = jax.tree.map(lambda a, b: jnp.where(upper, a, b), tree, other)
            tree = combine(first, second)
        else:
            tree = combine(tree, other)
        distance *= 2
    return tree


def add_trees(a, b):
    return jax.tree.map(jnp.add, a, b)


def narrow_butterfly(block, axis):
    count = lax.axis_size(axis)
    distance = 1
    while distance < count:
        sent = block.astype(jnp.bfloat16)
        other = lax.ppermute(sent, axis, partner_pairs(count, distance))
        block = sent.astype(jnp.float32) + other.astype(jnp.float32)
        distance *= 2
    return block


def softmax_combine(a, b):
    (max_a, total_a), mixed_a = a
    (max_b, total_b), mixed_b = b
    mixed_a = mixed_a.astype(jnp.float32)
    mixed_b = mixed_b.astype(jnp.float32)
    top = jnp.maximum(max_a, max_b)
    factor_a = jnp.exp(max_a - top)
    factor_b = jnp.exp(max_b - top)
    return (
        jnp.stack([top, total_a * factor_a + total_b * factor_b]),
        (scale_heads(mixed_a, factor_a) + scale_heads(mixed_b, factor_b)).astype(jnp.bfloat16),
    )


def reduce_scatter_rows(block, axis):
    count = lax.axis_size(axis)
    assert count & (count - 1) == 0
    index = lax.axis_index(axis)
    distance = count // 2
    while distance >= 1:
        half = block.shape[0] // 2
        upper = (index // distance) % 2 == 1
        low, high = block[:half], block[half:]
        keep = jnp.where(upper, high, low)
        send = jnp.where(upper, low, high)
        block = keep + lax.ppermute(send, axis, partner_pairs(count, distance))
        distance //= 2
    return block


def gather_rows(block, axis):
    if lax.axis_size(axis) != 2:
        return lax.all_gather(block, axis, axis=0, tiled=True)
    other = lax.ppermute(block, axis, [(0, 1), (1, 0)])
    first = lax.axis_index(axis) == 0
    return jnp.concatenate([jnp.where(first, block, other), jnp.where(first, other, block)])


def norm_rows(entries):
    widened = entries.astype(jnp.float32)
    centred = widened - jnp.mean(widened, axis=-1, keepdims=True)
    spread = jnp.mean(centred * centred, axis=-1, keepdims=True)
    return centred * lax.rsqrt(spread + 1e-05)


def window_attend(query_rows, kv_ext):
    row_count, model_width = query_rows.shape
    head_size = model_width // HEADS
    key_count = kv_ext.shape[0]
    key_span = key_count - row_count
    query_heads = query_rows.reshape(row_count, HEADS, head_size)
    key_heads = kv_ext[:, :model_width].reshape(key_count, HEADS, head_size)
    value_heads = kv_ext[:, model_width:].reshape(key_count, HEADS, head_size)
    scores = jnp.einsum(
        "qhd,khd->hqk", query_heads, key_heads, preferred_element_type=jnp.float32
    ) * head_size ** (-0.5)
    offset = lax.broadcasted_iota(jnp.int32, (row_count, key_count), 1) - lax.broadcasted_iota(
        jnp.int32, (row_count, key_count), 0
    )
    inside = jnp.logical_and(offset >= 0, offset < key_span)
    scores = jnp.where(inside[None, :, :], scores, -1e30)
    raised = jnp.exp(scores - jnp.max(scores, axis=-1, keepdims=True))
    weights = (raised / jnp.sum(raised, axis=-1, keepdims=True)).astype(jnp.bfloat16)
    attended = jnp.einsum("hqk,khd->qhd", weights, value_heads, preferred_element_type=jnp.float32)
    return attended.reshape(row_count, model_width).astype(jnp.bfloat16)


def split_heads(matrix):
    row_count, model_width = matrix.shape
    return matrix.reshape(row_count, HEADS, model_width // HEADS).transpose(1, 0, 2)


def head_partial(operands):
    query_head, key_head, value_head = operands
    scores = lax.dot_general(
        query_head, key_head, (((1,), (1,)), ((), ())), preferred_element_type=jnp.float32
    ) * query_head.shape[1] ** (-0.5)
    local_max = jnp.max(scores, axis=1)
    raised = jnp.exp(scores - local_max[:, None]).astype(jnp.bfloat16)
    total = jnp.sum(raised.astype(jnp.float32), axis=1)
    mixed = jnp.dot(raised, value_head, preferred_element_type=jnp.float32)
    return (local_max, total, mixed)


def scale_heads(mixed, factor):
    query_count, model_width = mixed.shape
    head_count = factor.shape[0]
    shaped = mixed.reshape(query_count, head_count, model_width // head_count)
    return (shaped * factor.T[:, :, None]).reshape(query_count, model_width)


def loss_coefficients(
    sigma, target, matched, intersection, predicted, truth_count, hits_total, model_width
):
    denom = predicted + truth_count + 1.0
    slope = -2.0 / denom
    level = (2.0 * intersection + 1.0) / (denom * denom)
    dice_part = hits_total * (slope[:, None] * target + level[:, None]) * sigma * (1.0 - sigma)
    return (matched[:, None] * (sigma - target + dice_part) * model_width ** (-0.5)).astype(
        jnp.bfloat16
    )


def body(
    hits,
    enc_qkv,
    enc_out,
    enc_up,
    enc_down,
    queries,
    cross_q,
    cross_kv,
    cross_out,
    mask_first,
    mask_second,
    truth,
    match,
):
    model_width = hits.shape[1]
    local_hits = hits.shape[0]
    query_count = queries.shape[0]
    hits_total = float(local_hits * lax.axis_size("phi") * lax.axis_size("query"))
    track_count = query_count * lax.axis_size("query") // 2
    normed = norm_rows(hits).astype(jnp.bfloat16)
    projected = jnp.dot(normed, enc_qkv, preferred_element_type=jnp.float32).astype(jnp.bfloat16)
    extended = extended_2(projected[:, model_width:], ((("phi", "query"), 0),), WIN // 2)
    attended = window_attend(projected[:, :model_width], extended)
    residual = hits.astype(jnp.float32) + jnp.dot(
        attended, enc_out, preferred_element_type=jnp.float32
    )
    upper = jax.nn.gelu(
        jnp.dot(
            norm_rows(residual).astype(jnp.bfloat16), enc_up, preferred_element_type=jnp.float32
        ),
        approximate=True,
    ).astype(jnp.bfloat16)
    encoded = (residual + jnp.dot(upper, enc_down, preferred_element_type=jnp.float32)).astype(
        jnp.bfloat16
    )
    local_kv = jnp.dot(
        norm_rows(encoded).astype(jnp.bfloat16), cross_kv, preferred_element_type=jnp.float32
    ).astype(jnp.bfloat16)
    shifted = truth + 1
    digits = jnp.stack([shifted // 256, shifted % 256], axis=1).astype(jnp.bfloat16)
    digits = jnp.pad(digits, ((0, 0), (0, 126)))
    gathered = gather_rows(jnp.concatenate([local_kv, encoded, digits], axis=1), "query")
    group_kv = gathered[:, : 2 * model_width]
    group_hits = gathered[:, 2 * model_width : 3 * model_width]
    group_digits = gathered[:, 3 * model_width :].astype(jnp.int32)
    group_truth = group_digits[:, 0] * 256 + group_digits[:, 1] - 1
    query_proj = jnp.dot(queries, cross_q, preferred_element_type=jnp.float32).astype(jnp.bfloat16)
    head_size = model_width // HEADS
    group_count = group_kv.shape[0]
    query_heads = query_proj.reshape(query_count, HEADS, head_size)
    key_heads = group_kv[:, :model_width].reshape(group_count, HEADS, head_size)
    value_heads = group_kv[:, model_width:].reshape(group_count, HEADS, head_size)
    scores = jnp.einsum(
        "qhd,khd->hqk", query_heads, key_heads, preferred_element_type=jnp.float32
    ) * head_size ** (-0.5)
    local_max = jnp.max(scores, axis=-1)
    raised = jnp.exp(scores - local_max[..., None]).astype(jnp.bfloat16)
    local_total = jnp.sum(raised.astype(jnp.float32), axis=-1)
    local_mixed = jnp.einsum(
        "hqk,khd->qhd", raised, value_heads, preferred_element_type=jnp.float32
    ).reshape(query_count, model_width)
    (_, total), mixed = butterfly(
        (jnp.stack([local_max, local_total]), local_mixed.astype(jnp.bfloat16)),
        "phi",
        softmax_combine,
        ordered=True,
    )
    mixed = mixed.astype(jnp.float32)
    context = scale_heads(mixed, 1.0 / total).astype(jnp.bfloat16)
    mixed_queries = queries.astype(jnp.float32) + jnp.dot(
        context, cross_out, preferred_element_type=jnp.float32
    )
    mask_hidden = jax.nn.relu(
        jnp.dot(
            norm_rows(mixed_queries).astype(jnp.bfloat16),
            mask_first,
            preferred_element_type=jnp.float32,
        )
    ).astype(jnp.bfloat16)
    mask_embed = jnp.dot(mask_hidden, mask_second, preferred_element_type=jnp.float32).astype(
        jnp.bfloat16
    )
    logits = lax.dot_general(
        mask_embed, group_hits, (((1,), (1,)), ((), ())), preferred_element_type=jnp.float32
    ) * model_width ** (-0.5)
    sigma = jax.nn.sigmoid(logits)
    matched_flag = match < track_count
    matched = matched_flag.astype(jnp.float32)
    target = jnp.logical_and(match[:, None] == group_truth[None, :], matched_flag[:, None]).astype(
        jnp.float32
    )
    intersection, predicted, truth_count = butterfly(
        jnp.stack(
            [jnp.sum(sigma * target, axis=1), jnp.sum(sigma, axis=1), jnp.sum(target, axis=1)]
        ),
        "phi",
        add_trees,
    )
    mask_fill = predicted / hits_total
    coef = loss_coefficients(
        sigma, target, matched, intersection, predicted, truth_count, hits_total, model_width
    )
    mask_grad = narrow_butterfly(
        jnp.dot(coef, group_hits, preferred_element_type=jnp.float32), "phi"
    )
    hit_grad = reduce_scatter_rows(
        lax.dot_general(
            coef, mask_embed, (((0,), (0,)), ((), ())), preferred_element_type=jnp.float32
        ),
        "query",
    )
    return (encoded, mask_embed, hit_grad, mask_grad, mask_fill)


def solution(mesh):
    return jax.shard_map(
        body,
        mesh=mesh,
        in_specs=(
            P(("event", "phi", "query"), None),
            P(),
            P(),
            P(),
            P(),
            P("query", None),
            P(),
            P(),
            P(),
            P(),
            P(),
            P(("event", "phi", "query")),
            P(("event", "query")),
        ),
        out_specs=(
            P(("event", "phi", "query"), None),
            P(("event", "query"), None),
            P(("event", "phi", "query"), None),
            P(("event", "query"), None),
            P(("event", "query")),
        ),
        check_vma=False,
    )
```

```python
import jax
import jax.numpy as jnp
from jax import lax
from jax.sharding import PartitionSpec as P

HEADS = 8
WIN = 512


def extended_2(block, sides, width):
    for axis, dim in sides:
        count = lax.axis_size(axis)
        forward = [(i, i + 1) for i in range(count - 1)]
        forward.append((count - 1, 0))
        backward = [(target, source) for source, target in forward]
        low = lax.ppermute(
            lax.slice_in_dim(block, block.shape[dim] - width, None, axis=dim), axis, forward
        )
        high = lax.ppermute(lax.slice_in_dim(block, 0, width, axis=dim), axis, backward)
        block = jnp.concatenate([low, block, high], axis=dim)
    return block


def partner_pairs(count, distance):
    return [(i, i ^ distance) for i in range(count)]


def butterfly(tree, axis, combine, ordered=False):
    count = lax.axis_size(axis)
    assert count & (count - 1) == 0
    index = lax.axis_index(axis)
    distance = 1
    while distance < count:
        other = lax.ppermute(tree, axis, partner_pairs(count, distance))
        if ordered:
            upper = (index // distance) % 2 == 1
            first = jax.tree.map(lambda a, b: jnp.where(upper, b, a), tree, other)
            second = jax.tree.map(lambda a, b: jnp.where(upper, a, b), tree, other)
            tree = combine(first, second)
        else:
            tree = combine(tree, other)
        distance *= 2
    return tree


def add_trees(a, b):
    return jax.tree.map(jnp.add, a, b)


def narrow_butterfly(block, axis):
    count = lax.axis_size(axis)
    distance = 1
    while distance < count:
        sent = block.astype(jnp.bfloat16)
        other = lax.ppermute(sent, axis, partner_pairs(count, distance))
        block = sent.astype(jnp.float32) + other.astype(jnp.float32)
        distance *= 2
    return block


def softmax_combine(a, b):
    max_a, total_a, mixed_a = a
    max_b, total_b, mixed_b = b
    mixed_a = mixed_a.astype(jnp.float32)
    mixed_b = mixed_b.astype(jnp.float32)
    top = jnp.maximum(max_a, max_b)
    factor_a = jnp.exp(max_a - top)
    factor_b = jnp.exp(max_b - top)
    return (
        top,
        total_a * factor_a + total_b * factor_b,
        (scale_heads(mixed_a, factor_a) + scale_heads(mixed_b, factor_b)).astype(jnp.bfloat16),
    )


def reduce_scatter_rows(block, axis):
    count = lax.axis_size(axis)
    assert count & (count - 1) == 0
    index = lax.axis_index(axis)
    distance = count // 2
    while distance >= 1:
        half = block.shape[0] // 2
        upper = (index // distance) % 2 == 1
        low, high = block[:half], block[half:]
        keep = jnp.where(upper, high, low)
        send = jnp.where(upper, low, high)
        block = keep + lax.ppermute(send, axis, partner_pairs(count, distance))
        distance //= 2
    return block


def shifted_exchange(piece_for, axis):
    count = lax.axis_size(axis)
    index = lax.axis_index(axis)
    received = [piece_for(index)]
    for shift in range(1, count):
        pairs = [(i, (i + shift) % count) for i in range(count)]
        received.append(lax.ppermute(piece_for((index + shift) % count), axis, pairs))
    return received


def by_source(received, axis):
    index = lax.axis_index(axis)
    order = (index - jnp.arange(len(received))) % len(received)
    return jnp.take(jnp.stack(received), order, axis=0)


def row_block(array, block_index, rows, axis=0):
    return lax.dynamic_slice_in_dim(array, block_index * rows, rows, axis=axis)


def norm_rows(entries):
    widened = entries.astype(jnp.float32)
    centred = widened - jnp.mean(widened, axis=-1, keepdims=True)
    spread = jnp.mean(centred * centred, axis=-1, keepdims=True)
    return centred * lax.rsqrt(spread + 1e-05)


def window_attend(query_rows, kv_ext):
    row_count, model_width = query_rows.shape
    head_size = model_width // HEADS
    key_count = kv_ext.shape[0]
    key_span = key_count - row_count
    query_heads = query_rows.reshape(row_count, HEADS, head_size)
    key_heads = kv_ext[:, :model_width].reshape(key_count, HEADS, head_size)
    value_heads = kv_ext[:, model_width:].reshape(key_count, HEADS, head_size)
    scores = jnp.einsum(
        "qhd,khd->hqk", query_heads, key_heads, preferred_element_type=jnp.float32
    ) * head_size ** (-0.5)
    offset = lax.broadcasted_iota(jnp.int32, (row_count, key_count), 1) - lax.broadcasted_iota(
        jnp.int32, (row_count, key_count), 0
    )
    inside = jnp.logical_and(offset >= 0, offset < key_span)
    scores = jnp.where(inside[None, :, :], scores, -1e30)
    raised = jnp.exp(scores - jnp.max(scores, axis=-1, keepdims=True))
    weights = (raised / jnp.sum(raised, axis=-1, keepdims=True)).astype(jnp.bfloat16)
    attended = jnp.einsum("hqk,khd->qhd", weights, value_heads, preferred_element_type=jnp.float32)
    return attended.reshape(row_count, model_width).astype(jnp.bfloat16)


def split_heads(matrix):
    row_count, model_width = matrix.shape
    return matrix.reshape(row_count, HEADS, model_width // HEADS).transpose(1, 0, 2)


def head_partial(operands):
    query_head, key_head, value_head = operands
    scores = lax.dot_general(
        query_head, key_head, (((1,), (1,)), ((), ())), preferred_element_type=jnp.float32
    ) * query_head.shape[1] ** (-0.5)
    local_max = jnp.max(scores, axis=1)
    raised = jnp.exp(scores - local_max[:, None]).astype(jnp.bfloat16)
    total = jnp.sum(raised.astype(jnp.float32), axis=1)
    mixed = jnp.dot(raised, value_head, preferred_element_type=jnp.float32)
    return (local_max, total, mixed)


def scale_heads(mixed, factor):
    query_count, model_width = mixed.shape
    head_count = factor.shape[0]
    shaped = mixed.reshape(query_count, head_count, model_width // head_count)
    return (shaped * factor.T[:, :, None]).reshape(query_count, model_width)


def loss_coefficients(
    sigma, target, matched, intersection, predicted, truth_count, hits_total, model_width
):
    denom = predicted + truth_count + 1.0
    slope = -2.0 / denom
    level = (2.0 * intersection + 1.0) / (denom * denom)
    dice_part = hits_total * (slope[:, None] * target + level[:, None]) * sigma * (1.0 - sigma)
    return (matched[:, None] * (sigma - target + dice_part) * model_width ** (-0.5)).astype(
        jnp.bfloat16
    )


def body(
    hits,
    enc_qkv,
    enc_out,
    enc_up,
    enc_down,
    queries,
    cross_q,
    cross_kv,
    cross_out,
    mask_first,
    mask_second,
    truth,
    match,
):
    model_width = hits.shape[1]
    local_hits = hits.shape[0]
    query_count = queries.shape[0]
    hits_total = float(local_hits * lax.axis_size("phi") * lax.axis_size("query"))
    track_count = query_count * lax.axis_size("query") // 2
    normed = norm_rows(hits).astype(jnp.bfloat16)
    projected = jnp.dot(normed, enc_qkv, preferred_element_type=jnp.float32).astype(jnp.bfloat16)
    extended = extended_2(projected[:, model_width:], ((("phi", "query"), 0),), WIN // 2)
    attended = window_attend(projected[:, :model_width], extended)
    residual = hits.astype(jnp.float32) + jnp.dot(
        attended, enc_out, preferred_element_type=jnp.float32
    )
    upper = jax.nn.gelu(
        jnp.dot(
            norm_rows(residual).astype(jnp.bfloat16), enc_up, preferred_element_type=jnp.float32
        ),
        approximate=True,
    ).astype(jnp.bfloat16)
    encoded = (residual + jnp.dot(upper, enc_down, preferred_element_type=jnp.float32)).astype(
        jnp.bfloat16
    )
    local_kv = jnp.dot(
        norm_rows(encoded).astype(jnp.bfloat16), cross_kv, preferred_element_type=jnp.float32
    ).astype(jnp.bfloat16)
    shifted = truth + 1
    digits = jnp.stack([shifted // 256, shifted % 256], axis=1).astype(jnp.bfloat16)
    digits = jnp.pad(digits, ((0, 0), (0, 126)))
    gathered = lax.all_gather(
        jnp.concatenate([local_kv, encoded, digits], axis=1), "query", axis=0, tiled=True
    )
    group_kv = gathered[:, : 2 * model_width]
    group_hits = gathered[:, 2 * model_width : 3 * model_width]
    group_digits = gathered[:, 3 * model_width :].astype(jnp.int32)
    group_truth = group_digits[:, 0] * 256 + group_digits[:, 1] - 1
    query_proj = jnp.dot(queries, cross_q, preferred_element_type=jnp.float32).astype(jnp.bfloat16)
    head_size = model_width // HEADS
    group_count = group_kv.shape[0]
    query_heads = query_proj.reshape(query_count, HEADS, head_size)
    key_heads = group_kv[:, :model_width].reshape(group_count, HEADS, head_size)
    value_heads = group_kv[:, model_width:].reshape(group_count, HEADS, head_size)
    scores = jnp.einsum(
        "qhd,khd->hqk", query_heads, key_heads, preferred_element_type=jnp.float32
    ) * head_size ** (-0.5)
    local_max = jnp.max(scores, axis=-1)
    raised = jnp.exp(scores - local_max[..., None]).astype(jnp.bfloat16)
    local_total = jnp.sum(raised.astype(jnp.float32), axis=-1)
    local_mixed = jnp.einsum(
        "hqk,khd->qhd", raised, value_heads, preferred_element_type=jnp.float32
    ).reshape(query_count, model_width)
    phi_count = lax.axis_size("phi")
    direct = phi_count <= 8
    if direct:
        rows = query_count // phi_count
        phi_index = lax.axis_index("phi")
        stats = jnp.stack([local_max, local_total])
        narrow = local_mixed.astype(jnp.bfloat16)
        received = shifted_exchange(
            lambda t: (row_block(stats, t, rows, axis=2), row_block(narrow, t, rows)), "phi"
        )
        maxima = jnp.stack([r[0][0] for r in received])
        totals = jnp.stack([r[0][1] for r in received])
        top = jnp.max(maxima, axis=0)
        factor = jnp.exp(maxima - top[None])
        total = jnp.sum(totals * factor, axis=0)
        mixed = scale_heads(received[0][1].astype(jnp.float32), factor[0])
        for k in range(1, phi_count):
            mixed = mixed + scale_heads(received[k][1].astype(jnp.float32), factor[k])
        own_queries = row_block(queries, phi_index, rows)
    else:
        _, total, mixed = butterfly(
            (local_max, local_total, local_mixed.astype(jnp.bfloat16)),
            "phi",
            softmax_combine,
            ordered=True,
        )
        mixed = mixed.astype(jnp.float32)
        own_queries = queries
    context = scale_heads(mixed, 1.0 / total).astype(jnp.bfloat16)
    mixed_queries = own_queries.astype(jnp.float32) + jnp.dot(
        context, cross_out, preferred_element_type=jnp.float32
    )
    mask_hidden = jax.nn.relu(
        jnp.dot(
            norm_rows(mixed_queries).astype(jnp.bfloat16),
            mask_first,
            preferred_element_type=jnp.float32,
        )
    ).astype(jnp.bfloat16)
    mask_embed = jnp.dot(mask_hidden, mask_second, preferred_element_type=jnp.float32).astype(
        jnp.bfloat16
    )
    if direct:
        mask_embed = by_source(shifted_exchange(lambda t: mask_embed, "phi"), "phi").reshape(
            query_count, model_width
        )
    logits = lax.dot_general(
        mask_embed, group_hits, (((1,), (1,)), ((), ())), preferred_element_type=jnp.float32
    ) * model_width ** (-0.5)
    sigma = jax.nn.sigmoid(logits)
    matched_flag = match < track_count
    matched = matched_flag.astype(jnp.float32)
    target = jnp.logical_and(match[:, None] == group_truth[None, :], matched_flag[:, None]).astype(
        jnp.float32
    )
    partial_stats = jnp.stack(
        [jnp.sum(sigma * target, axis=1), jnp.sum(sigma, axis=1), jnp.sum(target, axis=1)]
    )
    if direct:
        intersection, predicted, truth_count = jnp.sum(
            by_source(shifted_exchange(lambda t: partial_stats, "phi"), "phi"), axis=0
        )
    else:
        intersection, predicted, truth_count = butterfly(partial_stats, "phi", add_trees)
    mask_fill = predicted / hits_total
    coef = loss_coefficients(
        sigma, target, matched, intersection, predicted, truth_count, hits_total, model_width
    )
    grad_partial = jnp.dot(coef, group_hits, preferred_element_type=jnp.float32)
    if direct:
        received = shifted_exchange(
            lambda t: row_block(grad_partial, t, rows).astype(jnp.bfloat16), "phi"
        )
        grad_block = row_block(grad_partial, phi_index, rows)
        for k in range(1, phi_count):
            grad_block = grad_block + received[k].astype(jnp.float32)
        mask_grad = by_source(shifted_exchange(lambda t: grad_block, "phi"), "phi").reshape(
            query_count, model_width
        )
    else:
        mask_grad = narrow_butterfly(grad_partial, "phi")
    hit_grad = reduce_scatter_rows(
        lax.dot_general(
            coef, mask_embed, (((0,), (0,)), ((), ())), preferred_element_type=jnp.float32
        ),
        "query",
    )
    return (encoded, mask_embed, hit_grad, mask_grad, mask_fill)


def solution(mesh):
    return jax.shard_map(
        body,
        mesh=mesh,
        in_specs=(
            P(("event", "phi", "query"), None),
            P(),
            P(),
            P(),
            P(),
            P("query", None),
            P(),
            P(),
            P(),
            P(),
            P(),
            P(("event", "phi", "query")),
            P(("event", "query")),
        ),
        out_specs=(
            P(("event", "phi", "query"), None),
            P(("event", "query"), None),
            P(("event", "phi", "query"), None),
            P(("event", "query"), None),
            P(("event", "query")),
        ),
        check_vma=False,
    )
```

```python
import jax
import jax.numpy as jnp
from jax import lax
from jax.sharding import PartitionSpec as P

HEADS = 8
WIN = 512


def extended_2(block, sides, width):
    for axis, dim in sides:
        count = lax.axis_size(axis)
        forward = [(i, i + 1) for i in range(count - 1)]
        forward.append((count - 1, 0))
        backward = [(target, source) for source, target in forward]
        low = lax.ppermute(
            lax.slice_in_dim(block, block.shape[dim] - width, None, axis=dim), axis, forward
        )
        high = lax.ppermute(lax.slice_in_dim(block, 0, width, axis=dim), axis, backward)
        block = jnp.concatenate([low, block, high], axis=dim)
    return block


def partner_pairs(count, distance):
    return [(i, i ^ distance) for i in range(count)]


def butterfly(tree, axis, combine, ordered=False):
    count = lax.axis_size(axis)
    assert count & (count - 1) == 0
    index = lax.axis_index(axis)
    distance = 1
    while distance < count:
        other = lax.ppermute(tree, axis, partner_pairs(count, distance))
        if ordered:
            upper = (index // distance) % 2 == 1
            first = jax.tree.map(lambda a, b: jnp.where(upper, b, a), tree, other)
            second = jax.tree.map(lambda a, b: jnp.where(upper, a, b), tree, other)
            tree = combine(first, second)
        else:
            tree = combine(tree, other)
        distance *= 2
    return tree


def add_trees(a, b):
    return jax.tree.map(jnp.add, a, b)


def narrow_butterfly(block, axis):
    count = lax.axis_size(axis)
    distance = 1
    while distance < count:
        sent = block.astype(jnp.bfloat16)
        other = lax.ppermute(sent, axis, partner_pairs(count, distance))
        block = sent.astype(jnp.float32) + other.astype(jnp.float32)
        distance *= 2
    return block


def softmax_combine(a, b):
    max_a, total_a, mixed_a = a
    max_b, total_b, mixed_b = b
    mixed_a = mixed_a.astype(jnp.float32)
    mixed_b = mixed_b.astype(jnp.float32)
    top = jnp.maximum(max_a, max_b)
    factor_a = jnp.exp(max_a - top)
    factor_b = jnp.exp(max_b - top)
    return (
        top,
        total_a * factor_a + total_b * factor_b,
        (scale_heads(mixed_a, factor_a) + scale_heads(mixed_b, factor_b)).astype(jnp.bfloat16),
    )


def reduce_scatter_rows(block, axis):
    count = lax.axis_size(axis)
    assert count & (count - 1) == 0
    index = lax.axis_index(axis)
    distance = count // 2
    while distance >= 1:
        half = block.shape[0] // 2
        upper = (index // distance) % 2 == 1
        low, high = block[:half], block[half:]
        keep = jnp.where(upper, high, low)
        send = jnp.where(upper, low, high)
        block = keep + lax.ppermute(send, axis, partner_pairs(count, distance))
        distance //= 2
    return block


def halves(array, upper, axis):
    size = array.shape[axis] // 2
    low = lax.slice_in_dim(array, 0, size, axis=axis)
    high = lax.slice_in_dim(array, size, 2 * size, axis=axis)
    return jnp.where(upper, high, low), jnp.where(upper, low, high)


def owned_block(axis):
    count = lax.axis_size(axis)
    index = lax.axis_index(axis)
    offset, size, distance = 0, count, 1
    while distance < count:
        size //= 2
        offset = offset + ((index // distance) % 2) * size
        distance *= 2
    return offset


def scatter_softmax(stats, mixed, axis):
    count = lax.axis_size(axis)
    assert count & (count - 1) == 0
    index = lax.axis_index(axis)
    distance = 1
    while distance < count:
        upper = (index // distance) % 2 == 1
        keep_stats, send_stats = halves(stats, upper, 2)
        keep_mixed, send_mixed = halves(mixed, upper, 0)
        other_stats, other_mixed = lax.ppermute(
            (send_stats, send_mixed.astype(jnp.bfloat16)), axis, partner_pairs(count, distance)
        )
        top = jnp.maximum(keep_stats[0], other_stats[0])
        factor_keep = jnp.exp(keep_stats[0] - top)
        factor_other = jnp.exp(other_stats[0] - top)
        stats = jnp.stack([top, keep_stats[1] * factor_keep + other_stats[1] * factor_other])
        mixed = scale_heads(keep_mixed.astype(jnp.float32), factor_keep) + scale_heads(
            other_mixed.astype(jnp.float32), factor_other
        )
        distance *= 2
    return stats, mixed


def scatter_sum(block, axis):
    count = lax.axis_size(axis)
    index = lax.axis_index(axis)
    distance = 1
    while distance < count:
        upper = (index // distance) % 2 == 1
        keep, send = halves(block, upper, 0)
        other = lax.ppermute(send.astype(jnp.bfloat16), axis, partner_pairs(count, distance))
        block = keep + other.astype(jnp.float32)
        distance *= 2
    return block


def gather_blocks(block, axis):
    count = lax.axis_size(axis)
    index = lax.axis_index(axis)
    distance = count // 2
    while distance >= 1:
        upper = (index // distance) % 2 == 1
        other = lax.ppermute(block, axis, partner_pairs(count, distance))
        block = jnp.where(
            upper, jnp.concatenate([other, block]), jnp.concatenate([block, other])
        )
        distance //= 2
    return block


def norm_rows(entries):
    widened = entries.astype(jnp.float32)
    centred = widened - jnp.mean(widened, axis=-1, keepdims=True)
    spread = jnp.mean(centred * centred, axis=-1, keepdims=True)
    return centred * lax.rsqrt(spread + 1e-05)


def window_attend(query_rows, kv_ext):
    row_count, model_width = query_rows.shape
    head_size = model_width // HEADS
    key_count = kv_ext.shape[0]
    key_span = key_count - row_count
    query_heads = query_rows.reshape(row_count, HEADS, head_size)
    key_heads = kv_ext[:, :model_width].reshape(key_count, HEADS, head_size)
    value_heads = kv_ext[:, model_width:].reshape(key_count, HEADS, head_size)
    scores = jnp.einsum(
        "qhd,khd->hqk", query_heads, key_heads, preferred_element_type=jnp.float32
    ) * head_size ** (-0.5)
    offset = lax.broadcasted_iota(jnp.int32, (row_count, key_count), 1) - lax.broadcasted_iota(
        jnp.int32, (row_count, key_count), 0
    )
    inside = jnp.logical_and(offset >= 0, offset < key_span)
    scores = jnp.where(inside[None, :, :], scores, -1e30)
    raised = jnp.exp(scores - jnp.max(scores, axis=-1, keepdims=True))
    weights = (raised / jnp.sum(raised, axis=-1, keepdims=True)).astype(jnp.bfloat16)
    attended = jnp.einsum("hqk,khd->qhd", weights, value_heads, preferred_element_type=jnp.float32)
    return attended.reshape(row_count, model_width).astype(jnp.bfloat16)


def split_heads(matrix):
    row_count, model_width = matrix.shape
    return matrix.reshape(row_count, HEADS, model_width // HEADS).transpose(1, 0, 2)


def head_partial(operands):
    query_head, key_head, value_head = operands
    scores = lax.dot_general(
        query_head, key_head, (((1,), (1,)), ((), ())), preferred_element_type=jnp.float32
    ) * query_head.shape[1] ** (-0.5)
    local_max = jnp.max(scores, axis=1)
    raised = jnp.exp(scores - local_max[:, None]).astype(jnp.bfloat16)
    total = jnp.sum(raised.astype(jnp.float32), axis=1)
    mixed = jnp.dot(raised, value_head, preferred_element_type=jnp.float32)
    return (local_max, total, mixed)


def scale_heads(mixed, factor):
    query_count, model_width = mixed.shape
    head_count = factor.shape[0]
    shaped = mixed.reshape(query_count, head_count, model_width // head_count)
    return (shaped * factor.T[:, :, None]).reshape(query_count, model_width)


def loss_coefficients(
    sigma, target, matched, intersection, predicted, truth_count, hits_total, model_width
):
    denom = predicted + truth_count + 1.0
    slope = -2.0 / denom
    level = (2.0 * intersection + 1.0) / (denom * denom)
    dice_part = hits_total * (slope[:, None] * target + level[:, None]) * sigma * (1.0 - sigma)
    return (matched[:, None] * (sigma - target + dice_part) * model_width ** (-0.5)).astype(
        jnp.bfloat16
    )


def body(
    hits,
    enc_qkv,
    enc_out,
    enc_up,
    enc_down,
    queries,
    cross_q,
    cross_kv,
    cross_out,
    mask_first,
    mask_second,
    truth,
    match,
):
    model_width = hits.shape[1]
    local_hits = hits.shape[0]
    query_count = queries.shape[0]
    hits_total = float(local_hits * lax.axis_size("phi") * lax.axis_size("query"))
    track_count = query_count * lax.axis_size("query") // 2
    normed = norm_rows(hits).astype(jnp.bfloat16)
    projected = jnp.dot(normed, enc_qkv, preferred_element_type=jnp.float32).astype(jnp.bfloat16)
    extended = extended_2(projected[:, model_width:], ((("phi", "query"), 0),), WIN // 2)
    attended = window_attend(projected[:, :model_width], extended)
    residual = hits.astype(jnp.float32) + jnp.dot(
        attended, enc_out, preferred_element_type=jnp.float32
    )
    upper = jax.nn.gelu(
        jnp.dot(
            norm_rows(residual).astype(jnp.bfloat16), enc_up, preferred_element_type=jnp.float32
        ),
        approximate=True,
    ).astype(jnp.bfloat16)
    encoded = (residual + jnp.dot(upper, enc_down, preferred_element_type=jnp.float32)).astype(
        jnp.bfloat16
    )
    local_kv = jnp.dot(
        norm_rows(encoded).astype(jnp.bfloat16), cross_kv, preferred_element_type=jnp.float32
    ).astype(jnp.bfloat16)
    shifted = truth + 1
    digits = jnp.stack([shifted // 256, shifted % 256], axis=1).astype(jnp.bfloat16)
    digits = jnp.pad(digits, ((0, 0), (0, 126)))
    gathered = lax.all_gather(
        jnp.concatenate([local_kv, encoded, digits], axis=1), "query", axis=0, tiled=True
    )
    group_kv = gathered[:, : 2 * model_width]
    group_hits = gathered[:, 2 * model_width : 3 * model_width]
    group_digits = gathered[:, 3 * model_width :].astype(jnp.int32)
    group_truth = group_digits[:, 0] * 256 + group_digits[:, 1] - 1
    query_proj = jnp.dot(queries, cross_q, preferred_element_type=jnp.float32).astype(jnp.bfloat16)
    head_size = model_width // HEADS
    group_count = group_kv.shape[0]
    query_heads = query_proj.reshape(query_count, HEADS, head_size)
    key_heads = group_kv[:, :model_width].reshape(group_count, HEADS, head_size)
    value_heads = group_kv[:, model_width:].reshape(group_count, HEADS, head_size)
    scores = jnp.einsum(
        "qhd,khd->hqk", query_heads, key_heads, preferred_element_type=jnp.float32
    ) * head_size ** (-0.5)
    local_max = jnp.max(scores, axis=-1)
    raised = jnp.exp(scores - local_max[..., None]).astype(jnp.bfloat16)
    local_total = jnp.sum(raised.astype(jnp.float32), axis=-1)
    local_mixed = jnp.einsum(
        "hqk,khd->qhd", raised, value_heads, preferred_element_type=jnp.float32
    ).reshape(query_count, model_width)
    phi_count = lax.axis_size("phi")
    rows = query_count // phi_count
    (_, total), mixed = scatter_softmax(
        jnp.stack([local_max, local_total]), local_mixed, "phi"
    )
    own_queries = lax.dynamic_slice_in_dim(queries, owned_block("phi") * rows, rows, 0)
    context = scale_heads(mixed, 1.0 / total).astype(jnp.bfloat16)
    mixed_queries = own_queries.astype(jnp.float32) + jnp.dot(
        context, cross_out, preferred_element_type=jnp.float32
    )
    mask_hidden = jax.nn.relu(
        jnp.dot(
            norm_rows(mixed_queries).astype(jnp.bfloat16),
            mask_first,
            preferred_element_type=jnp.float32,
        )
    ).astype(jnp.bfloat16)
    mask_embed = gather_blocks(
        jnp.dot(mask_hidden, mask_second, preferred_element_type=jnp.float32).astype(
            jnp.bfloat16
        ),
        "phi",
    )
    logits = lax.dot_general(
        mask_embed, group_hits, (((1,), (1,)), ((), ())), preferred_element_type=jnp.float32
    ) * model_width ** (-0.5)
    sigma = jax.nn.sigmoid(logits)
    matched_flag = match < track_count
    matched = matched_flag.astype(jnp.float32)
    target = jnp.logical_and(match[:, None] == group_truth[None, :], matched_flag[:, None]).astype(
        jnp.float32
    )
    intersection, predicted, truth_count = butterfly(
        jnp.stack(
            [jnp.sum(sigma * target, axis=1), jnp.sum(sigma, axis=1), jnp.sum(target, axis=1)]
        ),
        "phi",
        add_trees,
    )
    mask_fill = predicted / hits_total
    coef = loss_coefficients(
        sigma, target, matched, intersection, predicted, truth_count, hits_total, model_width
    )
    mask_grad = gather_blocks(
        scatter_sum(jnp.dot(coef, group_hits, preferred_element_type=jnp.float32), "phi").astype(
            jnp.bfloat16
        ),
        "phi",
    ).astype(jnp.float32)
    hit_grad = reduce_scatter_rows(
        lax.dot_general(
            coef, mask_embed, (((0,), (0,)), ((), ())), preferred_element_type=jnp.float32
        ),
        "query",
    )
    return (encoded, mask_embed, hit_grad, mask_grad, mask_fill)


def solution(mesh):
    return jax.shard_map(
        body,
        mesh=mesh,
        in_specs=(
            P(("event", "phi", "query"), None),
            P(),
            P(),
            P(),
            P(),
            P("query", None),
            P(),
            P(),
            P(),
            P(),
            P(),
            P(("event", "phi", "query")),
            P(("event", "query")),
        ),
        out_specs=(
            P(("event", "phi", "query"), None),
            P(("event", "query"), None),
            P(("event", "phi", "query"), None),
            P(("event", "query"), None),
            P(("event", "query")),
        ),
        check_vma=False,
    )
```

```python
import jax
import jax.numpy as jnp
from jax import lax
from jax.sharding import PartitionSpec as P

HEADS = 8
WIN = 512


def extended_2(block, sides, width):
    for axis, dim in sides:
        count = lax.axis_size(axis)
        forward = [(i, i + 1) for i in range(count - 1)]
        forward.append((count - 1, 0))
        backward = [(target, source) for source, target in forward]
        low = lax.ppermute(
            lax.slice_in_dim(block, block.shape[dim] - width, None, axis=dim), axis, forward
        )
        high = lax.ppermute(lax.slice_in_dim(block, 0, width, axis=dim), axis, backward)
        block = jnp.concatenate([low, block, high], axis=dim)
    return block


def partner_pairs(count, distance):
    return [(i, i ^ distance) for i in range(count)]


def butterfly(tree, axis, combine, ordered=False):
    count = lax.axis_size(axis)
    assert count & (count - 1) == 0
    index = lax.axis_index(axis)
    distance = 1
    while distance < count:
        other = lax.ppermute(tree, axis, partner_pairs(count, distance))
        if ordered:
            upper = (index // distance) % 2 == 1
            first = jax.tree.map(lambda a, b: jnp.where(upper, b, a), tree, other)
            second = jax.tree.map(lambda a, b: jnp.where(upper, a, b), tree, other)
            tree = combine(first, second)
        else:
            tree = combine(tree, other)
        distance *= 2
    return tree


def add_trees(a, b):
    return jax.tree.map(jnp.add, a, b)


def narrow_butterfly(block, axis):
    count = lax.axis_size(axis)
    distance = 1
    while distance < count:
        sent = block.astype(jnp.bfloat16)
        other = lax.ppermute(sent, axis, partner_pairs(count, distance))
        block = sent.astype(jnp.float32) + other.astype(jnp.float32)
        distance *= 2
    return block


def softmax_combine(a, b):
    max_a, total_a, mixed_a = a
    max_b, total_b, mixed_b = b
    mixed_a = mixed_a.astype(jnp.float32)
    mixed_b = mixed_b.astype(jnp.float32)
    top = jnp.maximum(max_a, max_b)
    factor_a = jnp.exp(max_a - top)
    factor_b = jnp.exp(max_b - top)
    return (
        top,
        total_a * factor_a + total_b * factor_b,
        (scale_heads(mixed_a, factor_a) + scale_heads(mixed_b, factor_b)).astype(jnp.bfloat16),
    )


def reduce_scatter_rows(block, axis):
    count = lax.axis_size(axis)
    assert count & (count - 1) == 0
    index = lax.axis_index(axis)
    distance = count // 2
    while distance >= 1:
        half = block.shape[0] // 2
        upper = (index // distance) % 2 == 1
        low, high = block[:half], block[half:]
        keep = jnp.where(upper, high, low)
        send = jnp.where(upper, low, high)
        block = keep + lax.ppermute(send, axis, partner_pairs(count, distance))
        distance //= 2
    return block


def norm_rows(entries):
    widened = entries.astype(jnp.float32)
    centred = widened - jnp.mean(widened, axis=-1, keepdims=True)
    spread = jnp.mean(centred * centred, axis=-1, keepdims=True)
    return centred * lax.rsqrt(spread + 1e-05)


def window_attend(query_rows, kv_ext):
    row_count, model_width = query_rows.shape
    head_size = model_width // HEADS
    key_count = kv_ext.shape[0]
    key_span = key_count - row_count
    query_heads = query_rows.reshape(row_count, HEADS, head_size)
    key_heads = kv_ext[:, :model_width].reshape(key_count, HEADS, head_size)
    value_heads = kv_ext[:, model_width:].reshape(key_count, HEADS, head_size)
    scores = jnp.einsum(
        "qhd,khd->hqk", query_heads, key_heads, preferred_element_type=jnp.float32
    ) * head_size ** (-0.5)
    offset = lax.broadcasted_iota(jnp.int32, (row_count, key_count), 1) - lax.broadcasted_iota(
        jnp.int32, (row_count, key_count), 0
    )
    inside = jnp.logical_and(offset >= 0, offset < key_span)
    scores = jnp.where(inside[None, :, :], scores, -1e30)
    raised = jnp.exp(scores - jnp.max(scores, axis=-1, keepdims=True))
    weights = (raised / jnp.sum(raised, axis=-1, keepdims=True)).astype(jnp.bfloat16)
    attended = jnp.einsum("hqk,khd->qhd", weights, value_heads, preferred_element_type=jnp.float32)
    return attended.reshape(row_count, model_width).astype(jnp.bfloat16)


def split_heads(matrix):
    row_count, model_width = matrix.shape
    return matrix.reshape(row_count, HEADS, model_width // HEADS).transpose(1, 0, 2)


def head_partial(operands):
    query_head, key_head, value_head = operands
    scores = lax.dot_general(
        query_head, key_head, (((1,), (1,)), ((), ())), preferred_element_type=jnp.float32
    ) * query_head.shape[1] ** (-0.5)
    local_max = jnp.max(scores, axis=1)
    raised = jnp.exp(scores - local_max[:, None]).astype(jnp.bfloat16)
    total = jnp.sum(raised.astype(jnp.float32), axis=1)
    mixed = jnp.dot(raised, value_head, preferred_element_type=jnp.float32)
    return (local_max, total, mixed)


def scale_heads(mixed, factor):
    query_count, model_width = mixed.shape
    head_count = factor.shape[0]
    shaped = mixed.reshape(query_count, head_count, model_width // head_count)
    return (shaped * factor.T[:, :, None]).reshape(query_count, model_width)


def loss_coefficients(
    sigma, target, matched, intersection, predicted, truth_count, hits_total, model_width
):
    denom = predicted + truth_count + 1.0
    slope = -2.0 / denom
    level = (2.0 * intersection + 1.0) / (denom * denom)
    dice_part = hits_total * (slope[:, None] * target + level[:, None]) * sigma * (1.0 - sigma)
    return (matched[:, None] * (sigma - target + dice_part) * model_width ** (-0.5)).astype(
        jnp.bfloat16
    )


def query_chain(
    query_proj,
    queries,
    match,
    group_kv,
    group_hits,
    group_truth,
    cross_out,
    mask_first,
    mask_second,
    track_count,
    hits_total,
):
    query_count, model_width = queries.shape
    head_size = model_width // HEADS
    group_count = group_kv.shape[0]
    query_heads = query_proj.reshape(query_count, HEADS, head_size)
    key_heads = group_kv[:, :model_width].reshape(group_count, HEADS, head_size)
    value_heads = group_kv[:, model_width:].reshape(group_count, HEADS, head_size)
    scores = jnp.einsum(
        "qhd,khd->hqk", query_heads, key_heads, preferred_element_type=jnp.float32
    ) * head_size ** (-0.5)
    local_max = jnp.max(scores, axis=-1)
    raised = jnp.exp(scores - local_max[..., None]).astype(jnp.bfloat16)
    local_total = jnp.sum(raised.astype(jnp.float32), axis=-1)
    local_mixed = jnp.einsum(
        "hqk,khd->qhd", raised, value_heads, preferred_element_type=jnp.float32
    ).reshape(query_count, model_width)
    _, total, mixed = butterfly(
        (local_max, local_total, local_mixed.astype(jnp.bfloat16)),
        "phi",
        softmax_combine,
        ordered=True,
    )
    mixed = mixed.astype(jnp.float32)
    context = scale_heads(mixed, 1.0 / total).astype(jnp.bfloat16)
    mixed_queries = queries.astype(jnp.float32) + jnp.dot(
        context, cross_out, preferred_element_type=jnp.float32
    )
    mask_hidden = jax.nn.relu(
        jnp.dot(
            norm_rows(mixed_queries).astype(jnp.bfloat16),
            mask_first,
            preferred_element_type=jnp.float32,
        )
    ).astype(jnp.bfloat16)
    mask_embed = jnp.dot(mask_hidden, mask_second, preferred_element_type=jnp.float32).astype(
        jnp.bfloat16
    )
    logits = lax.dot_general(
        mask_embed, group_hits, (((1,), (1,)), ((), ())), preferred_element_type=jnp.float32
    ) * model_width ** (-0.5)
    sigma = jax.nn.sigmoid(logits)
    matched_flag = match < track_count
    matched = matched_flag.astype(jnp.float32)
    target = jnp.logical_and(match[:, None] == group_truth[None, :], matched_flag[:, None]).astype(
        jnp.float32
    )
    intersection, predicted, truth_count = butterfly(
        (jnp.sum(sigma * target, axis=1), jnp.sum(sigma, axis=1), jnp.sum(target, axis=1)),
        "phi",
        add_trees,
    )
    mask_fill = predicted / hits_total
    coef = loss_coefficients(
        sigma, target, matched, intersection, predicted, truth_count, hits_total, model_width
    )
    mask_grad = narrow_butterfly(
        jnp.dot(coef, group_hits, preferred_element_type=jnp.float32), "phi"
    )
    hit_partial = lax.dot_general(
        coef, mask_embed, (((0,), (0,)), ((), ())), preferred_element_type=jnp.float32
    )
    return mask_embed, mask_grad, mask_fill, hit_partial


def body(
    hits,
    enc_qkv,
    enc_out,
    enc_up,
    enc_down,
    queries,
    cross_q,
    cross_kv,
    cross_out,
    mask_first,
    mask_second,
    truth,
    match,
):
    model_width = hits.shape[1]
    local_hits = hits.shape[0]
    query_count = queries.shape[0]
    hits_total = float(local_hits * lax.axis_size("phi") * lax.axis_size("query"))
    track_count = query_count * lax.axis_size("query") // 2
    normed = norm_rows(hits).astype(jnp.bfloat16)
    projected = jnp.dot(normed, enc_qkv, preferred_element_type=jnp.float32).astype(jnp.bfloat16)
    extended = extended_2(projected[:, model_width:], ((("phi", "query"), 0),), WIN // 2)
    attended = window_attend(projected[:, :model_width], extended)
    residual = hits.astype(jnp.float32) + jnp.dot(
        attended, enc_out, preferred_element_type=jnp.float32
    )
    upper = jax.nn.gelu(
        jnp.dot(
            norm_rows(residual).astype(jnp.bfloat16), enc_up, preferred_element_type=jnp.float32
        ),
        approximate=True,
    ).astype(jnp.bfloat16)
    encoded = (residual + jnp.dot(upper, enc_down, preferred_element_type=jnp.float32)).astype(
        jnp.bfloat16
    )
    local_kv = jnp.dot(
        norm_rows(encoded).astype(jnp.bfloat16), cross_kv, preferred_element_type=jnp.float32
    ).astype(jnp.bfloat16)
    shifted = truth + 1
    digits = jnp.stack([shifted // 256, shifted % 256], axis=1).astype(jnp.bfloat16)
    digits = jnp.pad(digits, ((0, 0), (0, 126)))
    gathered = lax.all_gather(
        jnp.concatenate([local_kv, encoded, digits], axis=1), "query", axis=0, tiled=True
    )
    group_kv = gathered[:, : 2 * model_width]
    group_hits = gathered[:, 2 * model_width : 3 * model_width]
    group_digits = gathered[:, 3 * model_width :].astype(jnp.int32)
    group_truth = group_digits[:, 0] * 256 + group_digits[:, 1] - 1
    query_proj = jnp.dot(queries, cross_q, preferred_element_type=jnp.float32).astype(jnp.bfloat16)
    chunks = 2
    rows = query_count // chunks
    outputs = [
        query_chain(
            query_proj[c * rows : (c + 1) * rows],
            queries[c * rows : (c + 1) * rows],
            match[c * rows : (c + 1) * rows],
            group_kv,
            group_hits,
            group_truth,
            cross_out,
            mask_first,
            mask_second,
            track_count,
            hits_total,
        )
        for c in range(chunks)
    ]
    mask_embed = jnp.concatenate([o[0] for o in outputs])
    mask_grad = jnp.concatenate([o[1] for o in outputs])
    mask_fill = jnp.concatenate([o[2] for o in outputs])
    hit_partial = outputs[0][3]
    for o in outputs[1:]:
        hit_partial = hit_partial + o[3]
    hit_grad = reduce_scatter_rows(hit_partial, "query")
    return (encoded, mask_embed, hit_grad, mask_grad, mask_fill)


def solution(mesh):
    return jax.shard_map(
        body,
        mesh=mesh,
        in_specs=(
            P(("event", "phi", "query"), None),
            P(),
            P(),
            P(),
            P(),
            P("query", None),
            P(),
            P(),
            P(),
            P(),
            P(),
            P(("event", "phi", "query")),
            P(("event", "query")),
        ),
        out_specs=(
            P(("event", "phi", "query"), None),
            P(("event", "query"), None),
            P(("event", "phi", "query"), None),
            P(("event", "query"), None),
            P(("event", "query")),
        ),
        check_vma=False,
    )
```

```python
import jax
import jax.numpy as jnp
from jax import lax
from jax.sharding import PartitionSpec as P

HEADS = 8
WIN = 512


def extended_2(block, sides, width):
    for axis, dim in sides:
        count = lax.axis_size(axis)
        forward = [(i, i + 1) for i in range(count - 1)]
        forward.append((count - 1, 0))
        backward = [(target, source) for source, target in forward]
        low = lax.ppermute(
            lax.slice_in_dim(block, block.shape[dim] - width, None, axis=dim), axis, forward
        )
        high = lax.ppermute(lax.slice_in_dim(block, 0, width, axis=dim), axis, backward)
        block = jnp.concatenate([low, block, high], axis=dim)
    return block


def partner_pairs(count, distance):
    return [(i, i ^ distance) for i in range(count)]


def butterfly(tree, axis, combine, ordered=False):
    count = lax.axis_size(axis)
    assert count & (count - 1) == 0
    index = lax.axis_index(axis)
    distance = 1
    while distance < count:
        other = lax.ppermute(tree, axis, partner_pairs(count, distance))
        if ordered:
            upper = (index // distance) % 2 == 1
            first = jax.tree.map(lambda a, b: jnp.where(upper, b, a), tree, other)
            second = jax.tree.map(lambda a, b: jnp.where(upper, a, b), tree, other)
            tree = combine(first, second)
        else:
            tree = combine(tree, other)
        distance *= 2
    return tree


def add_trees(a, b):
    return jax.tree.map(jnp.add, a, b)


def narrow_butterfly(block, axis):
    count = lax.axis_size(axis)
    distance = 1
    while distance < count:
        sent = block.astype(jnp.bfloat16)
        other = lax.ppermute(sent, axis, partner_pairs(count, distance))
        block = sent.astype(jnp.float32) + other.astype(jnp.float32)
        distance *= 2
    return block


def softmax_combine(a, b):
    max_a, total_a, mixed_a = a
    max_b, total_b, mixed_b = b
    mixed_a = mixed_a.astype(jnp.float32)
    mixed_b = mixed_b.astype(jnp.float32)
    top = jnp.maximum(max_a, max_b)
    factor_a = jnp.exp(max_a - top)
    factor_b = jnp.exp(max_b - top)
    return (
        top,
        total_a * factor_a + total_b * factor_b,
        (scale_heads(mixed_a, factor_a) + scale_heads(mixed_b, factor_b)).astype(jnp.bfloat16),
    )


def reduce_scatter_rows(block, axis):
    count = lax.axis_size(axis)
    assert count & (count - 1) == 0
    index = lax.axis_index(axis)
    distance = count // 2
    while distance >= 1:
        half = block.shape[0] // 2
        upper = (index // distance) % 2 == 1
        low, high = block[:half], block[half:]
        keep = jnp.where(upper, high, low)
        send = jnp.where(upper, low, high)
        block = keep + lax.ppermute(send, axis, partner_pairs(count, distance))
        distance //= 2
    return block


def norm_rows(entries):
    widened = entries.astype(jnp.float32)
    centred = widened - jnp.mean(widened, axis=-1, keepdims=True)
    spread = jnp.mean(centred * centred, axis=-1, keepdims=True)
    return centred * lax.rsqrt(spread + 1e-05)


def window_attend(query_rows, kv_ext):
    row_count, model_width = query_rows.shape
    head_size = model_width // HEADS
    key_count = kv_ext.shape[0]
    key_span = key_count - row_count
    query_heads = query_rows.reshape(row_count, HEADS, head_size)
    key_heads = kv_ext[:, :model_width].reshape(key_count, HEADS, head_size)
    value_heads = kv_ext[:, model_width:].reshape(key_count, HEADS, head_size)
    scores = jnp.einsum(
        "qhd,khd->hqk", query_heads, key_heads, preferred_element_type=jnp.float32
    ) * head_size ** (-0.5)
    offset = lax.broadcasted_iota(jnp.int32, (row_count, key_count), 1) - lax.broadcasted_iota(
        jnp.int32, (row_count, key_count), 0
    )
    inside = jnp.logical_and(offset >= 0, offset < key_span)
    scores = jnp.where(inside[None, :, :], scores, -1e30)
    raised = jnp.exp(scores - jnp.max(scores, axis=-1, keepdims=True))
    weights = (raised / jnp.sum(raised, axis=-1, keepdims=True)).astype(jnp.bfloat16)
    attended = jnp.einsum("hqk,khd->qhd", weights, value_heads, preferred_element_type=jnp.float32)
    return attended.reshape(row_count, model_width).astype(jnp.bfloat16)


def split_heads(matrix):
    row_count, model_width = matrix.shape
    return matrix.reshape(row_count, HEADS, model_width // HEADS).transpose(1, 0, 2)


def head_partial(operands):
    query_head, key_head, value_head = operands
    scores = lax.dot_general(
        query_head, key_head, (((1,), (1,)), ((), ())), preferred_element_type=jnp.float32
    ) * query_head.shape[1] ** (-0.5)
    local_max = jnp.max(scores, axis=1)
    raised = jnp.exp(scores - local_max[:, None]).astype(jnp.bfloat16)
    total = jnp.sum(raised.astype(jnp.float32), axis=1)
    mixed = jnp.dot(raised, value_head, preferred_element_type=jnp.float32)
    return (local_max, total, mixed)


def scale_heads(mixed, factor):
    query_count, model_width = mixed.shape
    head_count = factor.shape[0]
    shaped = mixed.reshape(query_count, head_count, model_width // head_count)
    return (shaped * factor.T[:, :, None]).reshape(query_count, model_width)


def loss_coefficients(
    sigma, target, matched, intersection, predicted, truth_count, hits_total, model_width
):
    denom = predicted + truth_count + 1.0
    slope = -2.0 / denom
    level = (2.0 * intersection + 1.0) / (denom * denom)
    dice_part = hits_total * (slope[:, None] * target + level[:, None]) * sigma * (1.0 - sigma)
    return (matched[:, None] * (sigma - target + dice_part) * model_width ** (-0.5)).astype(
        jnp.bfloat16
    )


def body(
    hits,
    enc_qkv,
    enc_out,
    enc_up,
    enc_down,
    queries,
    cross_q,
    cross_kv,
    cross_out,
    mask_first,
    mask_second,
    truth,
    match,
):
    model_width = hits.shape[1]
    local_hits = hits.shape[0]
    query_count = queries.shape[0]
    hits_total = float(local_hits * lax.axis_size("phi") * lax.axis_size("query"))
    track_count = query_count * lax.axis_size("query") // 2
    normed = norm_rows(hits).astype(jnp.bfloat16)
    projected = jnp.dot(normed, enc_qkv, preferred_element_type=jnp.float32).astype(jnp.bfloat16)
    extended = extended_2(projected[:, model_width:], ((("phi", "query"), 0),), WIN // 2)
    attended = window_attend(projected[:, :model_width], extended)
    residual = hits.astype(jnp.float32) + jnp.dot(
        attended, enc_out, preferred_element_type=jnp.float32
    )
    upper = jax.nn.gelu(
        jnp.dot(
            norm_rows(residual).astype(jnp.bfloat16), enc_up, preferred_element_type=jnp.float32
        ),
        approximate=True,
    ).astype(jnp.bfloat16)
    encoded = (residual + jnp.dot(upper, enc_down, preferred_element_type=jnp.float32)).astype(
        jnp.bfloat16
    )
    local_kv = jnp.dot(
        norm_rows(encoded).astype(jnp.bfloat16), cross_kv, preferred_element_type=jnp.float32
    ).astype(jnp.bfloat16)
    shifted = truth + 1
    digits = jnp.stack([shifted // 256, shifted % 256], axis=1).astype(jnp.bfloat16)
    digits = jnp.pad(digits, ((0, 0), (0, 126)))
    gathered = lax.all_gather(
        jnp.concatenate([local_kv, encoded, digits], axis=1), "query", axis=0, tiled=True
    )
    group_kv = gathered[:, : 2 * model_width]
    group_hits = gathered[:, 2 * model_width : 3 * model_width]
    group_digits = gathered[:, 3 * model_width :].astype(jnp.int32)
    group_truth = group_digits[:, 0] * 256 + group_digits[:, 1] - 1
    query_proj = jnp.dot(queries, cross_q, preferred_element_type=jnp.float32).astype(jnp.bfloat16)
    head_size = model_width // HEADS
    group_count = group_kv.shape[0]
    query_heads = query_proj.reshape(query_count, HEADS, head_size)
    key_heads = group_kv[:, :model_width].reshape(group_count, HEADS, head_size)
    value_heads = group_kv[:, model_width:].reshape(group_count, HEADS, head_size)
    scores = jnp.einsum(
        "qhd,khd->hqk", query_heads, key_heads, preferred_element_type=jnp.float32
    ) * head_size ** (-0.5)
    local_max = jnp.max(scores, axis=-1)
    raised = jnp.exp(scores - local_max[..., None]).astype(jnp.bfloat16)
    local_total = jnp.sum(raised.astype(jnp.float32), axis=-1)
    local_mixed = jnp.einsum(
        "hqk,khd->qhd", raised, value_heads, preferred_element_type=jnp.float32
    ).reshape(query_count, model_width)
    _, total, mixed = butterfly(
        (local_max, local_total, local_mixed.astype(jnp.bfloat16)),
        "phi",
        softmax_combine,
        ordered=True,
    )
    mixed = mixed.astype(jnp.float32)
    context = scale_heads(mixed, 1.0 / total).astype(jnp.bfloat16)
    mixed_queries = queries.astype(jnp.float32) + jnp.dot(
        context, cross_out, preferred_element_type=jnp.float32
    )
    mask_hidden = jax.nn.relu(
        jnp.dot(
            norm_rows(mixed_queries).astype(jnp.bfloat16),
            mask_first,
            preferred_element_type=jnp.float32,
        )
    ).astype(jnp.bfloat16)
    mask_embed = jnp.dot(mask_hidden, mask_second, preferred_element_type=jnp.float32).astype(
        jnp.bfloat16
    )
    logits = lax.dot_general(
        mask_embed, group_hits, (((1,), (1,)), ((), ())), preferred_element_type=jnp.float32
    ) * model_width ** (-0.5)
    sigma = jax.nn.sigmoid(logits)
    matched_flag = match < track_count
    matched = matched_flag.astype(jnp.float32)
    target = jnp.logical_and(match[:, None] == group_truth[None, :], matched_flag[:, None]).astype(
        jnp.float32
    )
    intersection, predicted, truth_count = butterfly(
        jnp.stack(
            [jnp.sum(sigma * target, axis=1), jnp.sum(sigma, axis=1), jnp.sum(target, axis=1)]
        ),
        "phi",
        add_trees,
    )
    mask_fill = predicted / hits_total
    coef = loss_coefficients(
        sigma, target, matched, intersection, predicted, truth_count, hits_total, model_width
    )
    mask_grad = narrow_butterfly(
        jnp.dot(coef, group_hits, preferred_element_type=jnp.float32), "phi"
    )
    hit_grad = reduce_scatter_rows(
        lax.dot_general(
            coef, mask_embed, (((0,), (0,)), ((), ())), preferred_element_type=jnp.float32
        ),
        "query",
    )
    return (encoded, mask_embed, hit_grad, mask_grad, mask_fill)


def solution(mesh):
    return jax.shard_map(
        body,
        mesh=mesh,
        in_specs=(
            P(("event", "phi", "query"), None),
            P(),
            P(),
            P(),
            P(),
            P("query", None),
            P(),
            P(),
            P(),
            P(),
            P(),
            P(("event", "phi", "query")),
            P(("event", "query")),
        ),
        out_specs=(
            P(("event", "phi", "query"), None),
            P(("event", "query"), None),
            P(("event", "phi", "query"), None),
            P(("event", "query"), None),
            P(("event", "query")),
        ),
        check_vma=False,
    )
```

```python
import jax
import jax.numpy as jnp
from jax import lax
from jax.sharding import PartitionSpec as P

HEADS = 8
WIN = 512


def extended_2(block, sides, width):
    for axis, dim in sides:
        count = lax.axis_size(axis)
        forward = [(i, i + 1) for i in range(count - 1)]
        forward.append((count - 1, 0))
        backward = [(target, source) for source, target in forward]
        low = lax.ppermute(
            lax.slice_in_dim(block, block.shape[dim] - width, None, axis=dim), axis, forward
        )
        high = lax.ppermute(lax.slice_in_dim(block, 0, width, axis=dim), axis, backward)
        block = jnp.concatenate([low, block, high], axis=dim)
    return block


def partner_pairs(count, distance):
    return [(i, i ^ distance) for i in range(count)]


def butterfly(tree, axis, combine, ordered=False, distance=1):
    count = lax.axis_size(axis)
    assert count & (count - 1) == 0
    index = lax.axis_index(axis)
    while distance < count:
        other = lax.ppermute(tree, axis, partner_pairs(count, distance))
        if ordered:
            upper = (index // distance) % 2 == 1
            first = jax.tree.map(lambda a, b: jnp.where(upper, b, a), tree, other)
            second = jax.tree.map(lambda a, b: jnp.where(upper, a, b), tree, other)
            tree = combine(first, second)
        else:
            tree = combine(tree, other)
        distance *= 2
    return tree


def add_trees(a, b):
    return jax.tree.map(jnp.add, a, b)


def narrow_butterfly(block, axis, distance=1):
    count = lax.axis_size(axis)
    while distance < count:
        sent = block.astype(jnp.bfloat16)
        other = lax.ppermute(sent, axis, partner_pairs(count, distance))
        block = sent.astype(jnp.float32) + other.astype(jnp.float32)
        distance *= 2
    return block


def softmax_combine(a, b):
    max_a, total_a, mixed_a = a
    max_b, total_b, mixed_b = b
    mixed_a = mixed_a.astype(jnp.float32)
    mixed_b = mixed_b.astype(jnp.float32)
    top = jnp.maximum(max_a, max_b)
    factor_a = jnp.exp(max_a - top)
    factor_b = jnp.exp(max_b - top)
    return (
        top,
        total_a * factor_a + total_b * factor_b,
        (scale_heads(mixed_a, factor_a) + scale_heads(mixed_b, factor_b)).astype(jnp.bfloat16),
    )


def reduce_scatter_rows(block, axis):
    count = lax.axis_size(axis)
    assert count & (count - 1) == 0
    index = lax.axis_index(axis)
    distance = count // 2
    while distance >= 1:
        half = block.shape[0] // 2
        upper = (index // distance) % 2 == 1
        low, high = block[:half], block[half:]
        keep = jnp.where(upper, high, low)
        send = jnp.where(upper, low, high)
        block = keep + lax.ppermute(send, axis, partner_pairs(count, distance))
        distance //= 2
    return block


def norm_rows(entries):
    widened = entries.astype(jnp.float32)
    centred = widened - jnp.mean(widened, axis=-1, keepdims=True)
    spread = jnp.mean(centred * centred, axis=-1, keepdims=True)
    return centred * lax.rsqrt(spread + 1e-05)


def window_attend(query_rows, kv_ext):
    row_count, model_width = query_rows.shape
    head_size = model_width // HEADS
    key_count = kv_ext.shape[0]
    key_span = key_count - row_count
    query_heads = query_rows.reshape(row_count, HEADS, head_size)
    key_heads = kv_ext[:, :model_width].reshape(key_count, HEADS, head_size)
    value_heads = kv_ext[:, model_width:].reshape(key_count, HEADS, head_size)
    scores = jnp.einsum(
        "qhd,khd->hqk", query_heads, key_heads, preferred_element_type=jnp.float32
    ) * head_size ** (-0.5)
    offset = lax.broadcasted_iota(jnp.int32, (row_count, key_count), 1) - lax.broadcasted_iota(
        jnp.int32, (row_count, key_count), 0
    )
    inside = jnp.logical_and(offset >= 0, offset < key_span)
    scores = jnp.where(inside[None, :, :], scores, -1e30)
    raised = jnp.exp(scores - jnp.max(scores, axis=-1, keepdims=True))
    weights = (raised / jnp.sum(raised, axis=-1, keepdims=True)).astype(jnp.bfloat16)
    attended = jnp.einsum("hqk,khd->qhd", weights, value_heads, preferred_element_type=jnp.float32)
    return attended.reshape(row_count, model_width).astype(jnp.bfloat16)


def split_heads(matrix):
    row_count, model_width = matrix.shape
    return matrix.reshape(row_count, HEADS, model_width // HEADS).transpose(1, 0, 2)


def head_partial(operands):
    query_head, key_head, value_head = operands
    scores = lax.dot_general(
        query_head, key_head, (((1,), (1,)), ((), ())), preferred_element_type=jnp.float32
    ) * query_head.shape[1] ** (-0.5)
    local_max = jnp.max(scores, axis=1)
    raised = jnp.exp(scores - local_max[:, None]).astype(jnp.bfloat16)
    total = jnp.sum(raised.astype(jnp.float32), axis=1)
    mixed = jnp.dot(raised, value_head, preferred_element_type=jnp.float32)
    return (local_max, total, mixed)


def scale_heads(mixed, factor):
    query_count, model_width = mixed.shape
    head_count = factor.shape[0]
    shaped = mixed.reshape(query_count, head_count, model_width // head_count)
    return (shaped * factor.T[:, :, None]).reshape(query_count, model_width)


def loss_coefficients(
    sigma, target, matched, intersection, predicted, truth_count, hits_total, model_width
):
    denom = predicted + truth_count + 1.0
    slope = -2.0 / denom
    level = (2.0 * intersection + 1.0) / (denom * denom)
    dice_part = hits_total * (slope[:, None] * target + level[:, None]) * sigma * (1.0 - sigma)
    return (matched[:, None] * (sigma - target + dice_part) * model_width ** (-0.5)).astype(
        jnp.bfloat16
    )


def body(
    hits,
    enc_qkv,
    enc_out,
    enc_up,
    enc_down,
    queries,
    cross_q,
    cross_kv,
    cross_out,
    mask_first,
    mask_second,
    truth,
    match,
):
    model_width = hits.shape[1]
    local_hits = hits.shape[0]
    query_count = queries.shape[0]
    hits_total = float(local_hits * lax.axis_size("phi") * lax.axis_size("query"))
    track_count = query_count * lax.axis_size("query") // 2
    normed = norm_rows(hits).astype(jnp.bfloat16)
    projected = jnp.dot(normed, enc_qkv, preferred_element_type=jnp.float32).astype(jnp.bfloat16)
    extended = extended_2(projected[:, model_width:], ((("phi", "query"), 0),), WIN // 2)
    attended = window_attend(projected[:, :model_width], extended)
    residual = hits.astype(jnp.float32) + jnp.dot(
        attended, enc_out, preferred_element_type=jnp.float32
    )
    upper = jax.nn.gelu(
        jnp.dot(
            norm_rows(residual).astype(jnp.bfloat16), enc_up, preferred_element_type=jnp.float32
        ),
        approximate=True,
    ).astype(jnp.bfloat16)
    encoded = (residual + jnp.dot(upper, enc_down, preferred_element_type=jnp.float32)).astype(
        jnp.bfloat16
    )
    local_kv = jnp.dot(
        norm_rows(encoded).astype(jnp.bfloat16), cross_kv, preferred_element_type=jnp.float32
    ).astype(jnp.bfloat16)
    shifted = truth + 1
    digits = jnp.stack([shifted // 256, shifted % 256], axis=1).astype(jnp.bfloat16)
    digits = jnp.pad(digits, ((0, 0), (0, 126)))
    gathered = lax.all_gather(
        jnp.concatenate([local_kv, encoded, digits], axis=1), "query", axis=0, tiled=True
    )
    group_kv = gathered[:, : 2 * model_width]
    group_hits = gathered[:, 2 * model_width : 3 * model_width]
    group_digits = gathered[:, 3 * model_width :].astype(jnp.int32)
    group_truth = group_digits[:, 0] * 256 + group_digits[:, 1] - 1
    query_proj = jnp.dot(queries, cross_q, preferred_element_type=jnp.float32).astype(jnp.bfloat16)
    head_size = model_width // HEADS
    group_count = group_kv.shape[0]
    query_heads = query_proj.reshape(query_count, HEADS, head_size)
    key_heads = group_kv[:, :model_width].reshape(group_count, HEADS, head_size)
    value_heads = group_kv[:, model_width:].reshape(group_count, HEADS, head_size)
    scores = jnp.einsum(
        "qhd,khd->hqk", query_heads, key_heads, preferred_element_type=jnp.float32
    ) * head_size ** (-0.5)
    local_max = jnp.max(scores, axis=-1)
    raised = jnp.exp(scores - local_max[..., None]).astype(jnp.bfloat16)
    local_total = jnp.sum(raised.astype(jnp.float32), axis=-1)
    local_mixed = jnp.einsum(
        "hqk,khd->qhd", raised, value_heads, preferred_element_type=jnp.float32
    ).reshape(query_count, model_width)
    _, total, mixed = butterfly(
        (local_max, local_total, local_mixed.astype(jnp.bfloat16)),
        "phi",
        softmax_combine,
        ordered=True,
    )
    mixed = mixed.astype(jnp.float32)
    context = scale_heads(mixed, 1.0 / total).astype(jnp.bfloat16)
    mixed_queries = queries.astype(jnp.float32) + jnp.dot(
        context, cross_out, preferred_element_type=jnp.float32
    )
    mask_hidden = jax.nn.relu(
        jnp.dot(
            norm_rows(mixed_queries).astype(jnp.bfloat16),
            mask_first,
            preferred_element_type=jnp.float32,
        )
    ).astype(jnp.bfloat16)
    mask_embed = jnp.dot(mask_hidden, mask_second, preferred_element_type=jnp.float32).astype(
        jnp.bfloat16
    )
    pair_upper = lax.axis_index("phi") % 2 == 1
    own_payload = gathered[:, 2 * model_width :]
    other_payload = lax.ppermute(
        own_payload, "phi", partner_pairs(lax.axis_size("phi"), 1)
    )
    pair_payload = jnp.where(
        pair_upper,
        jnp.concatenate([other_payload, own_payload]),
        jnp.concatenate([own_payload, other_payload]),
    )
    pair_hits = pair_payload[:, :model_width]
    pair_digits = pair_payload[:, model_width:].astype(jnp.int32)
    pair_truth = pair_digits[:, 0] * 256 + pair_digits[:, 1] - 1
    logits = lax.dot_general(
        mask_embed, pair_hits, (((1,), (1,)), ((), ())), preferred_element_type=jnp.float32
    ) * model_width ** (-0.5)
    sigma = jax.nn.sigmoid(logits)
    matched_flag = match < track_count
    matched = matched_flag.astype(jnp.float32)
    target = jnp.logical_and(match[:, None] == pair_truth[None, :], matched_flag[:, None]).astype(
        jnp.float32
    )
    intersection, predicted, truth_count = butterfly(
        jnp.stack(
            [jnp.sum(sigma * target, axis=1), jnp.sum(sigma, axis=1), jnp.sum(target, axis=1)]
        ),
        "phi",
        add_trees,
        distance=2,
    )
    mask_fill = predicted / hits_total
    coef = loss_coefficients(
        sigma, target, matched, intersection, predicted, truth_count, hits_total, model_width
    )
    mask_grad = narrow_butterfly(
        jnp.dot(coef, pair_hits, preferred_element_type=jnp.float32), "phi", distance=2
    )
    group_count = group_hits.shape[0]
    own_coef = jnp.where(pair_upper, coef[:, group_count:], coef[:, :group_count])
    hit_grad = reduce_scatter_rows(
        lax.dot_general(
            own_coef, mask_embed, (((0,), (0,)), ((), ())), preferred_element_type=jnp.float32
        ),
        "query",
    )
    return (encoded, mask_embed, hit_grad, mask_grad, mask_fill)


def solution(mesh):
    return jax.shard_map(
        body,
        mesh=mesh,
        in_specs=(
            P(("event", "phi", "query"), None),
            P(),
            P(),
            P(),
            P(),
            P("query", None),
            P(),
            P(),
            P(),
            P(),
            P(),
            P(("event", "phi", "query")),
            P(("event", "query")),
        ),
        out_specs=(
            P(("event", "phi", "query"), None),
            P(("event", "query"), None),
            P(("event", "phi", "query"), None),
            P(("event", "query"), None),
            P(("event", "query")),
        ),
        check_vma=False,
    )
```

```python
import jax
import jax.numpy as jnp
from jax import lax
from jax.sharding import PartitionSpec as P

HEADS = 8
WIN = 512


def extended_2(block, sides, width):
    for axis, dim in sides:
        count = lax.axis_size(axis)
        forward = [(i, i + 1) for i in range(count - 1)]
        forward.append((count - 1, 0))
        backward = [(target, source) for source, target in forward]
        low = lax.ppermute(
            lax.slice_in_dim(block, block.shape[dim] - width, None, axis=dim), axis, forward
        )
        high = lax.ppermute(lax.slice_in_dim(block, 0, width, axis=dim), axis, backward)
        block = jnp.concatenate([low, block, high], axis=dim)
    return block


def partner_pairs(count, distance):
    return [(i, i ^ distance) for i in range(count)]


def butterfly(tree, axis, combine, ordered=False, distance=1):
    count = lax.axis_size(axis)
    assert count & (count - 1) == 0
    index = lax.axis_index(axis)
    while distance < count:
        other = lax.ppermute(tree, axis, partner_pairs(count, distance))
        if ordered:
            upper = (index // distance) % 2 == 1
            first = jax.tree.map(lambda a, b: jnp.where(upper, b, a), tree, other)
            second = jax.tree.map(lambda a, b: jnp.where(upper, a, b), tree, other)
            tree = combine(first, second)
        else:
            tree = combine(tree, other)
        distance *= 2
    return tree


def add_trees(a, b):
    return jax.tree.map(jnp.add, a, b)


def narrow_butterfly(block, axis, distance=1):
    count = lax.axis_size(axis)
    while distance < count:
        sent = block.astype(jnp.bfloat16)
        other = lax.ppermute(sent, axis, partner_pairs(count, distance))
        block = sent.astype(jnp.float32) + other.astype(jnp.float32)
        distance *= 2
    return block


def softmax_combine(a, b):
    max_a, total_a, mixed_a = a
    max_b, total_b, mixed_b = b
    mixed_a = mixed_a.astype(jnp.float32)
    mixed_b = mixed_b.astype(jnp.float32)
    top = jnp.maximum(max_a, max_b)
    factor_a = jnp.exp(max_a - top)
    factor_b = jnp.exp(max_b - top)
    return (
        top,
        total_a * factor_a + total_b * factor_b,
        (scale_heads(mixed_a, factor_a) + scale_heads(mixed_b, factor_b)).astype(jnp.bfloat16),
    )


def reduce_scatter_rows(block, axis):
    count = lax.axis_size(axis)
    assert count & (count - 1) == 0
    index = lax.axis_index(axis)
    distance = count // 2
    while distance >= 1:
        half = block.shape[0] // 2
        upper = (index // distance) % 2 == 1
        low, high = block[:half], block[half:]
        keep = jnp.where(upper, high, low)
        send = jnp.where(upper, low, high)
        block = keep + lax.ppermute(send, axis, partner_pairs(count, distance))
        distance //= 2
    return block


def norm_rows(entries):
    widened = entries.astype(jnp.float32)
    centred = widened - jnp.mean(widened, axis=-1, keepdims=True)
    spread = jnp.mean(centred * centred, axis=-1, keepdims=True)
    return centred * lax.rsqrt(spread + 1e-05)


def window_attend(query_rows, kv_ext):
    row_count, model_width = query_rows.shape
    head_size = model_width // HEADS
    key_count = kv_ext.shape[0]
    key_span = key_count - row_count
    query_heads = query_rows.reshape(row_count, HEADS, head_size)
    key_heads = kv_ext[:, :model_width].reshape(key_count, HEADS, head_size)
    value_heads = kv_ext[:, model_width:].reshape(key_count, HEADS, head_size)
    scores = jnp.einsum(
        "qhd,khd->hqk", query_heads, key_heads, preferred_element_type=jnp.float32
    ) * head_size ** (-0.5)
    offset = lax.broadcasted_iota(jnp.int32, (row_count, key_count), 1) - lax.broadcasted_iota(
        jnp.int32, (row_count, key_count), 0
    )
    inside = jnp.logical_and(offset >= 0, offset < key_span)
    scores = jnp.where(inside[None, :, :], scores, -1e30)
    raised = jnp.exp(scores - jnp.max(scores, axis=-1, keepdims=True))
    weights = (raised / jnp.sum(raised, axis=-1, keepdims=True)).astype(jnp.bfloat16)
    attended = jnp.einsum("hqk,khd->qhd", weights, value_heads, preferred_element_type=jnp.float32)
    return attended.reshape(row_count, model_width).astype(jnp.bfloat16)


def split_heads(matrix):
    row_count, model_width = matrix.shape
    return matrix.reshape(row_count, HEADS, model_width // HEADS).transpose(1, 0, 2)


def head_partial(operands):
    query_head, key_head, value_head = operands
    scores = lax.dot_general(
        query_head, key_head, (((1,), (1,)), ((), ())), preferred_element_type=jnp.float32
    ) * query_head.shape[1] ** (-0.5)
    local_max = jnp.max(scores, axis=1)
    raised = jnp.exp(scores - local_max[:, None]).astype(jnp.bfloat16)
    total = jnp.sum(raised.astype(jnp.float32), axis=1)
    mixed = jnp.dot(raised, value_head, preferred_element_type=jnp.float32)
    return (local_max, total, mixed)


def scale_heads(mixed, factor):
    query_count, model_width = mixed.shape
    head_count = factor.shape[0]
    shaped = mixed.reshape(query_count, head_count, model_width // head_count)
    return (shaped * factor.T[:, :, None]).reshape(query_count, model_width)


def loss_coefficients(
    sigma, target, matched, intersection, predicted, truth_count, hits_total, model_width
):
    denom = predicted + truth_count + 1.0
    slope = -2.0 / denom
    level = (2.0 * intersection + 1.0) / (denom * denom)
    dice_part = hits_total * (slope[:, None] * target + level[:, None]) * sigma * (1.0 - sigma)
    return (matched[:, None] * (sigma - target + dice_part) * model_width ** (-0.5)).astype(
        jnp.bfloat16
    )


def body(
    hits,
    enc_qkv,
    enc_out,
    enc_up,
    enc_down,
    queries,
    cross_q,
    cross_kv,
    cross_out,
    mask_first,
    mask_second,
    truth,
    match,
):
    model_width = hits.shape[1]
    local_hits = hits.shape[0]
    query_count = queries.shape[0]
    hits_total = float(local_hits * lax.axis_size("phi") * lax.axis_size("query"))
    track_count = query_count * lax.axis_size("query") // 2
    normed = norm_rows(hits).astype(jnp.bfloat16)
    projected = jnp.dot(normed, enc_qkv, preferred_element_type=jnp.float32).astype(jnp.bfloat16)
    extended = extended_2(projected[:, model_width:], ((("phi", "query"), 0),), WIN // 2)
    attended = window_attend(projected[:, :model_width], extended)
    residual = hits.astype(jnp.float32) + jnp.dot(
        attended, enc_out, preferred_element_type=jnp.float32
    )
    upper = jax.nn.gelu(
        jnp.dot(
            norm_rows(residual).astype(jnp.bfloat16), enc_up, preferred_element_type=jnp.float32
        ),
        approximate=True,
    ).astype(jnp.bfloat16)
    encoded = (residual + jnp.dot(upper, enc_down, preferred_element_type=jnp.float32)).astype(
        jnp.bfloat16
    )
    local_kv = jnp.dot(
        norm_rows(encoded).astype(jnp.bfloat16), cross_kv, preferred_element_type=jnp.float32
    ).astype(jnp.bfloat16)
    shifted = truth + 1
    digits = jnp.stack([shifted // 256, shifted % 256], axis=1).astype(jnp.bfloat16)
    digits = jnp.pad(digits, ((0, 0), (0, 126)))
    gathered = lax.all_gather(
        jnp.concatenate([local_kv, encoded, digits], axis=1), "query", axis=0, tiled=True
    )
    group_kv = gathered[:, : 2 * model_width]
    group_hits = gathered[:, 2 * model_width : 3 * model_width]
    group_digits = gathered[:, 3 * model_width :].astype(jnp.int32)
    group_truth = group_digits[:, 0] * 256 + group_digits[:, 1] - 1
    query_proj = jnp.dot(queries, cross_q, preferred_element_type=jnp.float32).astype(jnp.bfloat16)
    head_size = model_width // HEADS
    group_count = group_kv.shape[0]
    query_heads = query_proj.reshape(query_count, HEADS, head_size)
    key_heads = group_kv[:, :model_width].reshape(group_count, HEADS, head_size)
    value_heads = group_kv[:, model_width:].reshape(group_count, HEADS, head_size)
    scores = jnp.einsum(
        "qhd,khd->hqk", query_heads, key_heads, preferred_element_type=jnp.float32
    ) * head_size ** (-0.5)
    local_max = jnp.max(scores, axis=-1)
    raised = jnp.exp(scores - local_max[..., None]).astype(jnp.bfloat16)
    local_total = jnp.sum(raised.astype(jnp.float32), axis=-1)
    local_mixed = jnp.einsum(
        "hqk,khd->qhd", raised, value_heads, preferred_element_type=jnp.float32
    ).reshape(query_count, model_width)
    softmax_parts = lax.optimization_barrier(
        (local_max, local_total, local_mixed.astype(jnp.bfloat16))
    )
    _, total, mixed = butterfly(
        softmax_parts,
        "phi",
        softmax_combine,
        ordered=True,
    )
    mixed = mixed.astype(jnp.float32)
    context = scale_heads(mixed, 1.0 / total).astype(jnp.bfloat16)
    mixed_queries = queries.astype(jnp.float32) + jnp.dot(
        context, cross_out, preferred_element_type=jnp.float32
    )
    mask_hidden = jax.nn.relu(
        jnp.dot(
            norm_rows(mixed_queries).astype(jnp.bfloat16),
            mask_first,
            preferred_element_type=jnp.float32,
        )
    ).astype(jnp.bfloat16)
    mask_embed = jnp.dot(mask_hidden, mask_second, preferred_element_type=jnp.float32).astype(
        jnp.bfloat16
    )
    pair_upper = lax.axis_index("phi") % 2 == 1
    own_payload = gathered[:, 2 * model_width :]
    other_payload = lax.ppermute(
        own_payload, "phi", partner_pairs(lax.axis_size("phi"), 1)
    )
    pair_payload = jnp.where(
        pair_upper,
        jnp.concatenate([other_payload, own_payload]),
        jnp.concatenate([own_payload, other_payload]),
    )
    pair_hits = pair_payload[:, :model_width]
    pair_digits = pair_payload[:, model_width:].astype(jnp.int32)
    pair_truth = pair_digits[:, 0] * 256 + pair_digits[:, 1] - 1
    logits = lax.dot_general(
        mask_embed, pair_hits, (((1,), (1,)), ((), ())), preferred_element_type=jnp.float32
    ) * model_width ** (-0.5)
    sigma = jax.nn.sigmoid(logits)
    matched_flag = match < track_count
    matched = matched_flag.astype(jnp.float32)
    target = jnp.logical_and(match[:, None] == pair_truth[None, :], matched_flag[:, None]).astype(
        jnp.float32
    )
    intersection, predicted, truth_count = butterfly(
        jnp.stack(
            [jnp.sum(sigma * target, axis=1), jnp.sum(sigma, axis=1), jnp.sum(target, axis=1)]
        ),
        "phi",
        add_trees,
        distance=2,
    )
    mask_fill = predicted / hits_total
    coef = loss_coefficients(
        sigma, target, matched, intersection, predicted, truth_count, hits_total, model_width
    )
    mask_grad = narrow_butterfly(
        jnp.dot(coef, pair_hits, preferred_element_type=jnp.float32), "phi", distance=2
    )
    group_count = group_hits.shape[0]
    own_coef = jnp.where(pair_upper, coef[:, group_count:], coef[:, :group_count])
    hit_grad = reduce_scatter_rows(
        lax.dot_general(
            own_coef, mask_embed, (((0,), (0,)), ((), ())), preferred_element_type=jnp.float32
        ),
        "query",
    )
    return (encoded, mask_embed, hit_grad, mask_grad, mask_fill)


def solution(mesh):
    return jax.shard_map(
        body,
        mesh=mesh,
        in_specs=(
            P(("event", "phi", "query"), None),
            P(),
            P(),
            P(),
            P(),
            P("query", None),
            P(),
            P(),
            P(),
            P(),
            P(),
            P(("event", "phi", "query")),
            P(("event", "query")),
        ),
        out_specs=(
            P(("event", "phi", "query"), None),
            P(("event", "query"), None),
            P(("event", "phi", "query"), None),
            P(("event", "query"), None),
            P(("event", "query")),
        ),
        check_vma=False,
    )
```

```python
import jax
import jax.numpy as jnp
from jax import lax
from jax.sharding import PartitionSpec as P

HEADS = 8
WIN = 512


def extended_2(block, sides, width):
    for axis, dim in sides:
        count = lax.axis_size(axis)
        forward = [(i, i + 1) for i in range(count - 1)]
        forward.append((count - 1, 0))
        backward = [(target, source) for source, target in forward]
        low = lax.ppermute(
            lax.slice_in_dim(block, block.shape[dim] - width, None, axis=dim), axis, forward
        )
        high = lax.ppermute(lax.slice_in_dim(block, 0, width, axis=dim), axis, backward)
        block = jnp.concatenate([low, block, high], axis=dim)
    return block


def partner_pairs(count, distance):
    return [(i, i ^ distance) for i in range(count)]


def butterfly(tree, axis, combine, ordered=False, distance=1):
    count = lax.axis_size(axis)
    assert count & (count - 1) == 0
    index = lax.axis_index(axis)
    while distance < count:
        other = lax.ppermute(tree, axis, partner_pairs(count, distance))
        if ordered:
            upper = (index // distance) % 2 == 1
            first = jax.tree.map(lambda a, b: jnp.where(upper, b, a), tree, other)
            second = jax.tree.map(lambda a, b: jnp.where(upper, a, b), tree, other)
            tree = combine(first, second)
        else:
            tree = combine(tree, other)
        distance *= 2
    return tree


def add_trees(a, b):
    return jax.tree.map(jnp.add, a, b)


def narrow_butterfly(block, axis, distance=1):
    count = lax.axis_size(axis)
    while distance < count:
        sent = block.astype(jnp.bfloat16)
        other = lax.ppermute(sent, axis, partner_pairs(count, distance))
        block = sent.astype(jnp.float32) + other.astype(jnp.float32)
        distance *= 2
    return block


def softmax_combine(a, b):
    max_a, total_a, mixed_a = a
    max_b, total_b, mixed_b = b
    mixed_a = mixed_a.astype(jnp.float32)
    mixed_b = mixed_b.astype(jnp.float32)
    top = jnp.maximum(max_a, max_b)
    factor_a = jnp.exp(max_a - top)
    factor_b = jnp.exp(max_b - top)
    return (
        top,
        total_a * factor_a + total_b * factor_b,
        (scale_heads(mixed_a, factor_a) + scale_heads(mixed_b, factor_b)).astype(jnp.bfloat16),
    )


def reduce_scatter_rows(block, axis):
    count = lax.axis_size(axis)
    assert count & (count - 1) == 0
    index = lax.axis_index(axis)
    distance = count // 2
    while distance >= 1:
        half = block.shape[0] // 2
        upper = (index // distance) % 2 == 1
        low, high = block[:half], block[half:]
        keep = jnp.where(upper, high, low)
        send = jnp.where(upper, low, high)
        block = keep + lax.ppermute(send, axis, partner_pairs(count, distance))
        distance //= 2
    return block


def norm_rows(entries):
    widened = entries.astype(jnp.float32)
    centred = widened - jnp.mean(widened, axis=-1, keepdims=True)
    spread = jnp.mean(centred * centred, axis=-1, keepdims=True)
    return centred * lax.rsqrt(spread + 1e-05)


def window_attend(query_rows, kv_ext):
    row_count, model_width = query_rows.shape
    head_size = model_width // HEADS
    key_count = kv_ext.shape[0]
    key_span = key_count - row_count
    query_heads = query_rows.reshape(row_count, HEADS, head_size)
    key_heads = kv_ext[:, :model_width].reshape(key_count, HEADS, head_size)
    value_heads = kv_ext[:, model_width:].reshape(key_count, HEADS, head_size)
    scores = jnp.einsum(
        "qhd,khd->hqk", query_heads, key_heads, preferred_element_type=jnp.float32
    ) * head_size ** (-0.5)
    offset = lax.broadcasted_iota(jnp.int32, (row_count, key_count), 1) - lax.broadcasted_iota(
        jnp.int32, (row_count, key_count), 0
    )
    inside = jnp.logical_and(offset >= 0, offset < key_span)
    scores = jnp.where(inside[None, :, :], scores, -1e30)
    raised = jnp.exp(scores - jnp.max(scores, axis=-1, keepdims=True))
    weights = (raised / jnp.sum(raised, axis=-1, keepdims=True)).astype(jnp.bfloat16)
    attended = jnp.einsum("hqk,khd->qhd", weights, value_heads, preferred_element_type=jnp.float32)
    return attended.reshape(row_count, model_width).astype(jnp.bfloat16)


def split_heads(matrix):
    row_count, model_width = matrix.shape
    return matrix.reshape(row_count, HEADS, model_width // HEADS).transpose(1, 0, 2)


def head_partial(operands):
    query_head, key_head, value_head = operands
    scores = lax.dot_general(
        query_head, key_head, (((1,), (1,)), ((), ())), preferred_element_type=jnp.float32
    ) * query_head.shape[1] ** (-0.5)
    local_max = jnp.max(scores, axis=1)
    raised = jnp.exp(scores - local_max[:, None]).astype(jnp.bfloat16)
    total = jnp.sum(raised.astype(jnp.float32), axis=1)
    mixed = jnp.dot(raised, value_head, preferred_element_type=jnp.float32)
    return (local_max, total, mixed)


def scale_heads(mixed, factor):
    query_count, model_width = mixed.shape
    head_count = factor.shape[0]
    shaped = mixed.reshape(query_count, head_count, model_width // head_count)
    return (shaped * factor.T[:, :, None]).reshape(query_count, model_width)


def loss_coefficients(
    sigma, target, matched, intersection, predicted, truth_count, hits_total, model_width
):
    denom = predicted + truth_count + 1.0
    slope = -2.0 / denom
    level = (2.0 * intersection + 1.0) / (denom * denom)
    dice_part = hits_total * (slope[:, None] * target + level[:, None]) * sigma * (1.0 - sigma)
    return (matched[:, None] * (sigma - target + dice_part) * model_width ** (-0.5)).astype(
        jnp.bfloat16
    )


def body(
    hits,
    enc_qkv,
    enc_out,
    enc_up,
    enc_down,
    queries,
    cross_q,
    cross_kv,
    cross_out,
    mask_first,
    mask_second,
    truth,
    match,
):
    model_width = hits.shape[1]
    local_hits = hits.shape[0]
    query_count = queries.shape[0]
    hits_total = float(local_hits * lax.axis_size("phi") * lax.axis_size("query"))
    track_count = query_count * lax.axis_size("query") // 2
    normed = norm_rows(hits).astype(jnp.bfloat16)
    projected = jnp.dot(normed, enc_qkv, preferred_element_type=jnp.float32).astype(jnp.bfloat16)
    extended = extended_2(projected[:, model_width:], ((("phi", "query"), 0),), WIN // 2)
    block_rows = local_hits // 2
    span = extended.shape[0] - local_hits
    attended = jnp.concatenate(
        [
            window_attend(
                projected[b * block_rows : (b + 1) * block_rows, :model_width],
                extended[b * block_rows : b * block_rows + block_rows + span],
            )
            for b in range(2)
        ]
    )
    residual = hits.astype(jnp.float32) + jnp.dot(
        attended, enc_out, preferred_element_type=jnp.float32
    )
    upper = jax.nn.gelu(
        jnp.dot(
            norm_rows(residual).astype(jnp.bfloat16), enc_up, preferred_element_type=jnp.float32
        ),
        approximate=True,
    ).astype(jnp.bfloat16)
    encoded = (residual + jnp.dot(upper, enc_down, preferred_element_type=jnp.float32)).astype(
        jnp.bfloat16
    )
    local_kv = jnp.dot(
        norm_rows(encoded).astype(jnp.bfloat16), cross_kv, preferred_element_type=jnp.float32
    ).astype(jnp.bfloat16)
    shifted = truth + 1
    digits = jnp.stack([shifted // 256, shifted % 256], axis=1).astype(jnp.bfloat16)
    digits = jnp.pad(digits, ((0, 0), (0, 126)))
    gathered = lax.all_gather(
        jnp.concatenate([local_kv, encoded, digits], axis=1), "query", axis=0, tiled=True
    )
    group_kv = gathered[:, : 2 * model_width]
    group_hits = gathered[:, 2 * model_width : 3 * model_width]
    group_digits = gathered[:, 3 * model_width :].astype(jnp.int32)
    group_truth = group_digits[:, 0] * 256 + group_digits[:, 1] - 1
    query_proj = jnp.dot(queries, cross_q, preferred_element_type=jnp.float32).astype(jnp.bfloat16)
    head_size = model_width // HEADS
    group_count = group_kv.shape[0]
    query_heads = query_proj.reshape(query_count, HEADS, head_size)
    key_heads = group_kv[:, :model_width].reshape(group_count, HEADS, head_size)
    value_heads = group_kv[:, model_width:].reshape(group_count, HEADS, head_size)
    scores = jnp.einsum(
        "qhd,khd->hqk", query_heads, key_heads, preferred_element_type=jnp.float32
    ) * head_size ** (-0.5)
    local_max = jnp.max(scores, axis=-1)
    raised = jnp.exp(scores - local_max[..., None]).astype(jnp.bfloat16)
    local_total = jnp.sum(raised.astype(jnp.float32), axis=-1)
    local_mixed = jnp.einsum(
        "hqk,khd->qhd", raised, value_heads, preferred_element_type=jnp.float32
    ).reshape(query_count, model_width)
    _, total, mixed = butterfly(
        (local_max, local_total, local_mixed.astype(jnp.bfloat16)),
        "phi",
        softmax_combine,
        ordered=True,
    )
    mixed = mixed.astype(jnp.float32)
    context = scale_heads(mixed, 1.0 / total).astype(jnp.bfloat16)
    mixed_queries = queries.astype(jnp.float32) + jnp.dot(
        context, cross_out, preferred_element_type=jnp.float32
    )
    mask_hidden = jax.nn.relu(
        jnp.dot(
            norm_rows(mixed_queries).astype(jnp.bfloat16),
            mask_first,
            preferred_element_type=jnp.float32,
        )
    ).astype(jnp.bfloat16)
    mask_embed = jnp.dot(mask_hidden, mask_second, preferred_element_type=jnp.float32).astype(
        jnp.bfloat16
    )
    pair_upper = lax.axis_index("phi") % 2 == 1
    own_payload = gathered[:, 2 * model_width :]
    other_payload = lax.ppermute(
        own_payload, "phi", partner_pairs(lax.axis_size("phi"), 1)
    )
    pair_payload = jnp.where(
        pair_upper,
        jnp.concatenate([other_payload, own_payload]),
        jnp.concatenate([own_payload, other_payload]),
    )
    pair_hits = pair_payload[:, :model_width]
    pair_digits = pair_payload[:, model_width:].astype(jnp.int32)
    pair_truth = pair_digits[:, 0] * 256 + pair_digits[:, 1] - 1
    logits = lax.dot_general(
        mask_embed, pair_hits, (((1,), (1,)), ((), ())), preferred_element_type=jnp.float32
    ) * model_width ** (-0.5)
    sigma = jax.nn.sigmoid(logits)
    matched_flag = match < track_count
    matched = matched_flag.astype(jnp.float32)
    target = jnp.logical_and(match[:, None] == pair_truth[None, :], matched_flag[:, None]).astype(
        jnp.float32
    )
    intersection, predicted, truth_count = butterfly(
        jnp.stack(
            [jnp.sum(sigma * target, axis=1), jnp.sum(sigma, axis=1), jnp.sum(target, axis=1)]
        ),
        "phi",
        add_trees,
        distance=2,
    )
    mask_fill = predicted / hits_total
    coef = loss_coefficients(
        sigma, target, matched, intersection, predicted, truth_count, hits_total, model_width
    )
    mask_grad = narrow_butterfly(
        jnp.dot(coef, pair_hits, preferred_element_type=jnp.float32), "phi", distance=2
    )
    group_count = group_hits.shape[0]
    own_coef = jnp.where(pair_upper, coef[:, group_count:], coef[:, :group_count])
    hit_grad = reduce_scatter_rows(
        lax.dot_general(
            own_coef, mask_embed, (((0,), (0,)), ((), ())), preferred_element_type=jnp.float32
        ),
        "query",
    )
    return (encoded, mask_embed, hit_grad, mask_grad, mask_fill)


def solution(mesh):
    return jax.shard_map(
        body,
        mesh=mesh,
        in_specs=(
            P(("event", "phi", "query"), None),
            P(),
            P(),
            P(),
            P(),
            P("query", None),
            P(),
            P(),
            P(),
            P(),
            P(),
            P(("event", "phi", "query")),
            P(("event", "query")),
        ),
        out_specs=(
            P(("event", "phi", "query"), None),
            P(("event", "query"), None),
            P(("event", "phi", "query"), None),
            P(("event", "query"), None),
            P(("event", "query")),
        ),
        check_vma=False,
    )
```

```python
import jax
import jax.numpy as jnp
from jax import lax
from jax.sharding import PartitionSpec as P

HEADS = 8
WIN = 512


def extended_2(block, sides, width):
    for axis, dim in sides:
        count = lax.axis_size(axis)
        forward = [(i, i + 1) for i in range(count - 1)]
        forward.append((count - 1, 0))
        backward = [(target, source) for source, target in forward]
        low = lax.ppermute(
            lax.slice_in_dim(block, block.shape[dim] - width, None, axis=dim), axis, forward
        )
        high = lax.ppermute(lax.slice_in_dim(block, 0, width, axis=dim), axis, backward)
        block = jnp.concatenate([low, block, high], axis=dim)
    return block


def partner_pairs(count, distance):
    return [(i, i ^ distance) for i in range(count)]


def butterfly(tree, axis, combine, ordered=False, distance=1):
    count = lax.axis_size(axis)
    assert count & (count - 1) == 0
    index = lax.axis_index(axis)
    while distance < count:
        other = lax.ppermute(tree, axis, partner_pairs(count, distance))
        if ordered:
            upper = (index // distance) % 2 == 1
            first = jax.tree.map(lambda a, b: jnp.where(upper, b, a), tree, other)
            second = jax.tree.map(lambda a, b: jnp.where(upper, a, b), tree, other)
            tree = combine(first, second)
        else:
            tree = combine(tree, other)
        distance *= 2
    return tree


def add_trees(a, b):
    return jax.tree.map(jnp.add, a, b)


def narrow_butterfly(block, axis, distance=1):
    count = lax.axis_size(axis)
    while distance < count:
        sent = block.astype(jnp.bfloat16)
        other = lax.ppermute(sent, axis, partner_pairs(count, distance))
        block = sent.astype(jnp.float32) + other.astype(jnp.float32)
        distance *= 2
    return block


def softmax_combine(a, b):
    max_a, total_a, mixed_a = a
    max_b, total_b, mixed_b = b
    mixed_a = mixed_a.astype(jnp.float32)
    mixed_b = mixed_b.astype(jnp.float32)
    top = jnp.maximum(max_a, max_b)
    factor_a = jnp.exp(max_a - top)
    factor_b = jnp.exp(max_b - top)
    return (
        top,
        total_a * factor_a + total_b * factor_b,
        (scale_heads(mixed_a, factor_a) + scale_heads(mixed_b, factor_b)).astype(jnp.bfloat16),
    )


def reduce_scatter_rows(block, axis):
    count = lax.axis_size(axis)
    assert count & (count - 1) == 0
    index = lax.axis_index(axis)
    distance = count // 2
    while distance >= 1:
        half = block.shape[0] // 2
        upper = (index // distance) % 2 == 1
        low, high = block[:half], block[half:]
        keep = jnp.where(upper, high, low)
        send = jnp.where(upper, low, high)
        block = keep + lax.ppermute(send, axis, partner_pairs(count, distance))
        distance //= 2
    return block


def norm_rows(entries):
    widened = entries.astype(jnp.float32)
    centred = widened - jnp.mean(widened, axis=-1, keepdims=True)
    spread = jnp.mean(centred * centred, axis=-1, keepdims=True)
    return centred * lax.rsqrt(spread + 1e-05)


def window_attend(query_rows, kv_ext):
    row_count, model_width = query_rows.shape
    head_size = model_width // HEADS
    key_count = kv_ext.shape[0]
    key_span = key_count - row_count
    query_heads = query_rows.reshape(row_count, HEADS, head_size)
    key_heads = kv_ext[:, :model_width].reshape(key_count, HEADS, head_size)
    value_heads = kv_ext[:, model_width:].reshape(key_count, HEADS, head_size)
    scores = jnp.einsum(
        "qhd,khd->hqk", query_heads, key_heads, preferred_element_type=jnp.float32
    ) * head_size ** (-0.5)
    offset = lax.broadcasted_iota(jnp.int32, (row_count, key_count), 1) - lax.broadcasted_iota(
        jnp.int32, (row_count, key_count), 0
    )
    inside = jnp.logical_and(offset >= 0, offset < key_span)
    scores = jnp.where(inside[None, :, :], scores, -1e30)
    raised = jnp.exp(scores - jnp.max(scores, axis=-1, keepdims=True))
    weights = (raised / jnp.sum(raised, axis=-1, keepdims=True)).astype(jnp.bfloat16)
    attended = jnp.einsum("hqk,khd->qhd", weights, value_heads, preferred_element_type=jnp.float32)
    return attended.reshape(row_count, model_width).astype(jnp.bfloat16)


def split_heads(matrix):
    row_count, model_width = matrix.shape
    return matrix.reshape(row_count, HEADS, model_width // HEADS).transpose(1, 0, 2)


def head_partial(operands):
    query_head, key_head, value_head = operands
    scores = lax.dot_general(
        query_head, key_head, (((1,), (1,)), ((), ())), preferred_element_type=jnp.float32
    ) * query_head.shape[1] ** (-0.5)
    local_max = jnp.max(scores, axis=1)
    raised = jnp.exp(scores - local_max[:, None]).astype(jnp.bfloat16)
    total = jnp.sum(raised.astype(jnp.float32), axis=1)
    mixed = jnp.dot(raised, value_head, preferred_element_type=jnp.float32)
    return (local_max, total, mixed)


def scale_heads(mixed, factor):
    query_count, model_width = mixed.shape
    head_count = factor.shape[0]
    shaped = mixed.reshape(query_count, head_count, model_width // head_count)
    return (shaped * factor.T[:, :, None]).reshape(query_count, model_width)


def loss_coefficients(
    sigma, target, matched, intersection, predicted, truth_count, hits_total, model_width
):
    denom = predicted + truth_count + 1.0
    slope = -2.0 / denom
    level = (2.0 * intersection + 1.0) / (denom * denom)
    dice_part = hits_total * (slope[:, None] * target + level[:, None]) * sigma * (1.0 - sigma)
    return (matched[:, None] * (sigma - target + dice_part) * model_width ** (-0.5)).astype(
        jnp.bfloat16
    )


def body(
    hits,
    enc_qkv,
    enc_out,
    enc_up,
    enc_down,
    queries,
    cross_q,
    cross_kv,
    cross_out,
    mask_first,
    mask_second,
    truth,
    match,
):
    model_width = hits.shape[1]
    local_hits = hits.shape[0]
    query_count = queries.shape[0]
    hits_total = float(local_hits * lax.axis_size("phi") * lax.axis_size("query"))
    track_count = query_count * lax.axis_size("query") // 2
    normed = norm_rows(hits).astype(jnp.bfloat16)
    projected = jnp.dot(normed, enc_qkv, preferred_element_type=jnp.float32).astype(jnp.bfloat16)
    extended = extended_2(projected[:, model_width:], ((("phi", "query"), 0),), WIN // 2)
    block_rows = local_hits // 4
    span = extended.shape[0] - local_hits
    attended = jnp.concatenate(
        [
            window_attend(
                projected[b * block_rows : (b + 1) * block_rows, :model_width],
                extended[b * block_rows : b * block_rows + block_rows + span],
            )
            for b in range(4)
        ]
    )
    residual = hits.astype(jnp.float32) + jnp.dot(
        attended, enc_out, preferred_element_type=jnp.float32
    )
    upper = jax.nn.gelu(
        jnp.dot(
            norm_rows(residual).astype(jnp.bfloat16), enc_up, preferred_element_type=jnp.float32
        ),
        approximate=True,
    ).astype(jnp.bfloat16)
    encoded = (residual + jnp.dot(upper, enc_down, preferred_element_type=jnp.float32)).astype(
        jnp.bfloat16
    )
    local_kv = jnp.dot(
        norm_rows(encoded).astype(jnp.bfloat16), cross_kv, preferred_element_type=jnp.float32
    ).astype(jnp.bfloat16)
    shifted = truth + 1
    digits = jnp.stack([shifted // 256, shifted % 256], axis=1).astype(jnp.bfloat16)
    digits = jnp.pad(digits, ((0, 0), (0, 126)))
    gathered = lax.all_gather(
        jnp.concatenate([local_kv, encoded, digits], axis=1), "query", axis=0, tiled=True
    )
    group_kv = gathered[:, : 2 * model_width]
    group_hits = gathered[:, 2 * model_width : 3 * model_width]
    group_digits = gathered[:, 3 * model_width :].astype(jnp.int32)
    group_truth = group_digits[:, 0] * 256 + group_digits[:, 1] - 1
    query_proj = jnp.dot(queries, cross_q, preferred_element_type=jnp.float32).astype(jnp.bfloat16)
    head_size = model_width // HEADS
    group_count = group_kv.shape[0]
    query_heads = query_proj.reshape(query_count, HEADS, head_size)
    key_heads = group_kv[:, :model_width].reshape(group_count, HEADS, head_size)
    value_heads = group_kv[:, model_width:].reshape(group_count, HEADS, head_size)
    scores = jnp.einsum(
        "qhd,khd->hqk", query_heads, key_heads, preferred_element_type=jnp.float32
    ) * head_size ** (-0.5)
    local_max = jnp.max(scores, axis=-1)
    raised = jnp.exp(scores - local_max[..., None]).astype(jnp.bfloat16)
    local_total = jnp.sum(raised.astype(jnp.float32), axis=-1)
    local_mixed = jnp.einsum(
        "hqk,khd->qhd", raised, value_heads, preferred_element_type=jnp.float32
    ).reshape(query_count, model_width)
    _, total, mixed = butterfly(
        (local_max, local_total, local_mixed.astype(jnp.bfloat16)),
        "phi",
        softmax_combine,
        ordered=True,
    )
    mixed = mixed.astype(jnp.float32)
    context = scale_heads(mixed, 1.0 / total).astype(jnp.bfloat16)
    mixed_queries = queries.astype(jnp.float32) + jnp.dot(
        context, cross_out, preferred_element_type=jnp.float32
    )
    mask_hidden = jax.nn.relu(
        jnp.dot(
            norm_rows(mixed_queries).astype(jnp.bfloat16),
            mask_first,
            preferred_element_type=jnp.float32,
        )
    ).astype(jnp.bfloat16)
    mask_embed = jnp.dot(mask_hidden, mask_second, preferred_element_type=jnp.float32).astype(
        jnp.bfloat16
    )
    pair_upper = lax.axis_index("phi") % 2 == 1
    own_payload = gathered[:, 2 * model_width :]
    other_payload = lax.ppermute(
        own_payload, "phi", partner_pairs(lax.axis_size("phi"), 1)
    )
    pair_payload = jnp.where(
        pair_upper,
        jnp.concatenate([other_payload, own_payload]),
        jnp.concatenate([own_payload, other_payload]),
    )
    pair_hits = pair_payload[:, :model_width]
    pair_digits = pair_payload[:, model_width:].astype(jnp.int32)
    pair_truth = pair_digits[:, 0] * 256 + pair_digits[:, 1] - 1
    logits = lax.dot_general(
        mask_embed, pair_hits, (((1,), (1,)), ((), ())), preferred_element_type=jnp.float32
    ) * model_width ** (-0.5)
    sigma = jax.nn.sigmoid(logits)
    matched_flag = match < track_count
    matched = matched_flag.astype(jnp.float32)
    target = jnp.logical_and(match[:, None] == pair_truth[None, :], matched_flag[:, None]).astype(
        jnp.float32
    )
    intersection, predicted, truth_count = butterfly(
        jnp.stack(
            [jnp.sum(sigma * target, axis=1), jnp.sum(sigma, axis=1), jnp.sum(target, axis=1)]
        ),
        "phi",
        add_trees,
        distance=2,
    )
    mask_fill = predicted / hits_total
    coef = loss_coefficients(
        sigma, target, matched, intersection, predicted, truth_count, hits_total, model_width
    )
    mask_grad = narrow_butterfly(
        jnp.dot(coef, pair_hits, preferred_element_type=jnp.float32), "phi", distance=2
    )
    group_count = group_hits.shape[0]
    own_coef = jnp.where(pair_upper, coef[:, group_count:], coef[:, :group_count])
    hit_grad = reduce_scatter_rows(
        lax.dot_general(
            own_coef, mask_embed, (((0,), (0,)), ((), ())), preferred_element_type=jnp.float32
        ),
        "query",
    )
    return (encoded, mask_embed, hit_grad, mask_grad, mask_fill)


def solution(mesh):
    return jax.shard_map(
        body,
        mesh=mesh,
        in_specs=(
            P(("event", "phi", "query"), None),
            P(),
            P(),
            P(),
            P(),
            P("query", None),
            P(),
            P(),
            P(),
            P(),
            P(),
            P(("event", "phi", "query")),
            P(("event", "query")),
        ),
        out_specs=(
            P(("event", "phi", "query"), None),
            P(("event", "query"), None),
            P(("event", "phi", "query"), None),
            P(("event", "query"), None),
            P(("event", "query")),
        ),
        check_vma=False,
    )
```

```python
import jax
import jax.numpy as jnp
from jax import lax
from jax.sharding import PartitionSpec as P

HEADS = 8
WIN = 512


def extended_2(block, sides, width):
    for axis, dim in sides:
        count = lax.axis_size(axis)
        forward = [(i, i + 1) for i in range(count - 1)]
        forward.append((count - 1, 0))
        backward = [(target, source) for source, target in forward]
        low = lax.ppermute(
            lax.slice_in_dim(block, block.shape[dim] - width, None, axis=dim), axis, forward
        )
        high = lax.ppermute(lax.slice_in_dim(block, 0, width, axis=dim), axis, backward)
        block = jnp.concatenate([low, block, high], axis=dim)
    return block


def partner_pairs(count, distance):
    return [(i, i ^ distance) for i in range(count)]


def butterfly(tree, axis, combine, ordered=False, distance=1):
    count = lax.axis_size(axis)
    assert count & (count - 1) == 0
    index = lax.axis_index(axis)
    while distance < count:
        other = lax.ppermute(tree, axis, partner_pairs(count, distance))
        if ordered:
            upper = (index // distance) % 2 == 1
            first = jax.tree.map(lambda a, b: jnp.where(upper, b, a), tree, other)
            second = jax.tree.map(lambda a, b: jnp.where(upper, a, b), tree, other)
            tree = combine(first, second)
        else:
            tree = combine(tree, other)
        distance *= 2
    return tree


def add_trees(a, b):
    return jax.tree.map(jnp.add, a, b)


def narrow_butterfly(block, axis, distance=1):
    count = lax.axis_size(axis)
    while distance < count:
        sent = block.astype(jnp.bfloat16)
        other = lax.ppermute(sent, axis, partner_pairs(count, distance))
        block = sent.astype(jnp.float32) + other.astype(jnp.float32)
        distance *= 2
    return block


def softmax_combine(a, b):
    max_a, total_a, mixed_a = a
    max_b, total_b, mixed_b = b
    mixed_a = mixed_a.astype(jnp.float32)
    mixed_b = mixed_b.astype(jnp.float32)
    top = jnp.maximum(max_a, max_b)
    factor_a = jnp.exp(max_a - top)
    factor_b = jnp.exp(max_b - top)
    return (
        top,
        total_a * factor_a + total_b * factor_b,
        (scale_heads(mixed_a, factor_a) + scale_heads(mixed_b, factor_b)).astype(jnp.bfloat16),
    )


def reduce_scatter_rows(block, axis):
    count = lax.axis_size(axis)
    assert count & (count - 1) == 0
    index = lax.axis_index(axis)
    distance = count // 2
    while distance >= 1:
        half = block.shape[0] // 2
        upper = (index // distance) % 2 == 1
        low, high = block[:half], block[half:]
        keep = jnp.where(upper, high, low)
        send = jnp.where(upper, low, high)
        block = keep + lax.ppermute(send, axis, partner_pairs(count, distance))
        distance //= 2
    return block


def norm_rows(entries):
    widened = entries.astype(jnp.float32)
    centred = widened - jnp.mean(widened, axis=-1, keepdims=True)
    spread = jnp.mean(centred * centred, axis=-1, keepdims=True)
    return centred * lax.rsqrt(spread + 1e-05)


def window_attend(query_rows, kv_ext):
    row_count, model_width = query_rows.shape
    head_size = model_width // HEADS
    key_count = kv_ext.shape[0]
    key_span = key_count - row_count
    query_heads = query_rows.reshape(row_count, HEADS, head_size)
    key_heads = kv_ext[:, :model_width].reshape(key_count, HEADS, head_size)
    value_heads = kv_ext[:, model_width:].reshape(key_count, HEADS, head_size)
    scores = jnp.einsum(
        "qhd,khd->hqk", query_heads, key_heads, preferred_element_type=jnp.float32
    ) * head_size ** (-0.5)
    offset = lax.broadcasted_iota(jnp.int32, (row_count, key_count), 1) - lax.broadcasted_iota(
        jnp.int32, (row_count, key_count), 0
    )
    inside = jnp.logical_and(offset >= 0, offset < key_span)
    scores = jnp.where(inside[None, :, :], scores, -1e30)
    raised = jnp.exp(scores - jnp.max(scores, axis=-1, keepdims=True))
    weights = (raised / jnp.sum(raised, axis=-1, keepdims=True)).astype(jnp.bfloat16)
    attended = jnp.einsum("hqk,khd->qhd", weights, value_heads, preferred_element_type=jnp.float32)
    return attended.reshape(row_count, model_width).astype(jnp.bfloat16)


def split_heads(matrix):
    row_count, model_width = matrix.shape
    return matrix.reshape(row_count, HEADS, model_width // HEADS).transpose(1, 0, 2)


def head_partial(operands):
    query_head, key_head, value_head = operands
    scores = lax.dot_general(
        query_head, key_head, (((1,), (1,)), ((), ())), preferred_element_type=jnp.float32
    ) * query_head.shape[1] ** (-0.5)
    local_max = jnp.max(scores, axis=1)
    raised = jnp.exp(scores - local_max[:, None]).astype(jnp.bfloat16)
    total = jnp.sum(raised.astype(jnp.float32), axis=1)
    mixed = jnp.dot(raised, value_head, preferred_element_type=jnp.float32)
    return (local_max, total, mixed)


def scale_heads(mixed, factor):
    query_count, model_width = mixed.shape
    head_count = factor.shape[0]
    shaped = mixed.reshape(query_count, head_count, model_width // head_count)
    return (shaped * factor.T[:, :, None]).reshape(query_count, model_width)


def loss_coefficients(
    sigma, target, matched, intersection, predicted, truth_count, hits_total, model_width
):
    denom = predicted + truth_count + 1.0
    slope = -2.0 / denom
    level = (2.0 * intersection + 1.0) / (denom * denom)
    dice_part = hits_total * (slope[:, None] * target + level[:, None]) * sigma * (1.0 - sigma)
    return (matched[:, None] * (sigma - target + dice_part) * model_width ** (-0.5)).astype(
        jnp.bfloat16
    )


def body(
    hits,
    enc_qkv,
    enc_out,
    enc_up,
    enc_down,
    queries,
    cross_q,
    cross_kv,
    cross_out,
    mask_first,
    mask_second,
    truth,
    match,
):
    model_width = hits.shape[1]
    local_hits = hits.shape[0]
    query_count = queries.shape[0]
    hits_total = float(local_hits * lax.axis_size("phi") * lax.axis_size("query"))
    track_count = query_count * lax.axis_size("query") // 2
    normed = norm_rows(hits).astype(jnp.bfloat16)
    projected = jnp.dot(normed, enc_qkv, preferred_element_type=jnp.float32).astype(jnp.bfloat16)
    extended = extended_2(projected[:, model_width:], ((("phi", "query"), 0),), WIN // 2)
    block_rows = local_hits // 2
    span = extended.shape[0] - local_hits
    attended = jnp.concatenate(
        [
            window_attend(
                projected[b * block_rows : (b + 1) * block_rows, :model_width],
                extended[b * block_rows : b * block_rows + block_rows + span],
            )
            for b in range(2)
        ]
    )
    residual = hits.astype(jnp.float32) + jnp.dot(
        attended, enc_out, preferred_element_type=jnp.float32
    )
    upper = jax.nn.gelu(
        jnp.dot(
            norm_rows(residual).astype(jnp.bfloat16), enc_up, preferred_element_type=jnp.float32
        ),
        approximate=True,
    ).astype(jnp.bfloat16)
    encoded = (residual + jnp.dot(upper, enc_down, preferred_element_type=jnp.float32)).astype(
        jnp.bfloat16
    )
    local_kv = jnp.dot(
        norm_rows(encoded).astype(jnp.bfloat16), cross_kv, preferred_element_type=jnp.float32
    ).astype(jnp.bfloat16)
    shifted = truth + 1
    digits = jnp.stack([shifted // 256, shifted % 256], axis=1).astype(jnp.bfloat16)
    digits = jnp.pad(digits, ((0, 0), (0, 126)))
    gathered = lax.all_gather(
        jnp.concatenate([local_kv, encoded, digits], axis=1), "query", axis=0, tiled=True
    )
    group_kv = gathered[:, : 2 * model_width]
    group_hits = gathered[:, 2 * model_width : 3 * model_width]
    group_digits = gathered[:, 3 * model_width :].astype(jnp.int32)
    group_truth = group_digits[:, 0] * 256 + group_digits[:, 1] - 1
    query_proj = jnp.dot(queries, cross_q, preferred_element_type=jnp.float32).astype(jnp.bfloat16)
    head_size = model_width // HEADS
    group_count = group_kv.shape[0]
    query_heads = query_proj.reshape(query_count, HEADS, head_size)
    key_heads = group_kv[:, :model_width].reshape(group_count, HEADS, head_size)
    value_heads = group_kv[:, model_width:].reshape(group_count, HEADS, head_size)
    scores = jnp.einsum(
        "qhd,khd->hqk", query_heads, key_heads, preferred_element_type=jnp.float32
    ) * head_size ** (-0.5)
    local_max = jnp.max(scores, axis=-1)
    raised = jnp.exp(scores - local_max[..., None]).astype(jnp.bfloat16)
    local_total = jnp.sum(raised.astype(jnp.float32), axis=-1)
    local_mixed = jnp.einsum(
        "hqk,khd->qhd", raised, value_heads, preferred_element_type=jnp.float32
    ).reshape(query_count, model_width)
    _, total, mixed = butterfly(
        (local_max, local_total, local_mixed.astype(jnp.bfloat16)),
        "phi",
        softmax_combine,
        ordered=True,
    )
    mixed = mixed.astype(jnp.float32)
    context = scale_heads(mixed, 1.0 / total).astype(jnp.bfloat16)
    mixed_queries = queries.astype(jnp.float32) + jnp.dot(
        context, cross_out, preferred_element_type=jnp.float32
    )
    mask_hidden = jax.nn.relu(
        jnp.dot(
            norm_rows(mixed_queries).astype(jnp.bfloat16),
            mask_first,
            preferred_element_type=jnp.float32,
        )
    ).astype(jnp.bfloat16)
    mask_embed = jnp.dot(mask_hidden, mask_second, preferred_element_type=jnp.float32).astype(
        jnp.bfloat16
    )
    pair_upper = lax.axis_index("phi") % 2 == 1
    group_count = group_hits.shape[0]
    digit_rows = gathered[:, 3 * model_width : 3 * model_width + 2].T.reshape(
        2 * group_count // model_width, model_width
    )
    own_payload = jnp.concatenate(
        [group_hits, jnp.pad(digit_rows, ((0, 16 - digit_rows.shape[0]), (0, 0)))]
    )
    other_payload = lax.ppermute(
        own_payload, "phi", partner_pairs(lax.axis_size("phi"), 1)
    )
    other_digits = other_payload[group_count : group_count + digit_rows.shape[0]].reshape(
        2, group_count
    )
    other_payload = jnp.concatenate(
        [other_payload[:group_count], other_digits.T], axis=1
    )
    own_payload = gathered[:, 2 * model_width : 3 * model_width + 2]
    pair_payload = jnp.where(
        pair_upper,
        jnp.concatenate([other_payload, own_payload]),
        jnp.concatenate([own_payload, other_payload]),
    )
    pair_hits = pair_payload[:, :model_width]
    pair_digits = pair_payload[:, model_width:].astype(jnp.int32)
    pair_truth = pair_digits[:, 0] * 256 + pair_digits[:, 1] - 1
    logits = lax.dot_general(
        mask_embed, pair_hits, (((1,), (1,)), ((), ())), preferred_element_type=jnp.float32
    ) * model_width ** (-0.5)
    sigma = jax.nn.sigmoid(logits)
    matched_flag = match < track_count
    matched = matched_flag.astype(jnp.float32)
    target = jnp.logical_and(match[:, None] == pair_truth[None, :], matched_flag[:, None]).astype(
        jnp.float32
    )
    intersection, predicted, truth_count = butterfly(
        jnp.stack(
            [jnp.sum(sigma * target, axis=1), jnp.sum(sigma, axis=1), jnp.sum(target, axis=1)]
        ),
        "phi",
        add_trees,
        distance=2,
    )
    mask_fill = predicted / hits_total
    coef = loss_coefficients(
        sigma, target, matched, intersection, predicted, truth_count, hits_total, model_width
    )
    mask_grad = narrow_butterfly(
        jnp.dot(coef, pair_hits, preferred_element_type=jnp.float32), "phi", distance=2
    )
    own_coef = jnp.where(pair_upper, coef[:, group_count:], coef[:, :group_count])
    hit_grad = reduce_scatter_rows(
        lax.dot_general(
            own_coef, mask_embed, (((0,), (0,)), ((), ())), preferred_element_type=jnp.float32
        ),
        "query",
    )
    return (encoded, mask_embed, hit_grad, mask_grad, mask_fill)


def solution(mesh):
    return jax.shard_map(
        body,
        mesh=mesh,
        in_specs=(
            P(("event", "phi", "query"), None),
            P(),
            P(),
            P(),
            P(),
            P("query", None),
            P(),
            P(),
            P(),
            P(),
            P(),
            P(("event", "phi", "query")),
            P(("event", "query")),
        ),
        out_specs=(
            P(("event", "phi", "query"), None),
            P(("event", "query"), None),
            P(("event", "phi", "query"), None),
            P(("event", "query"), None),
            P(("event", "query")),
        ),
        check_vma=False,
    )
```

```python
import jax
import jax.numpy as jnp
from jax import lax
from jax.sharding import PartitionSpec as P

HEADS = 8
WIN = 512


def extended_2(block, sides, width):
    for axis, dim in sides:
        count = lax.axis_size(axis)
        forward = [(i, i + 1) for i in range(count - 1)]
        forward.append((count - 1, 0))
        backward = [(target, source) for source, target in forward]
        low = lax.ppermute(
            lax.slice_in_dim(block, block.shape[dim] - width, None, axis=dim), axis, forward
        )
        high = lax.ppermute(lax.slice_in_dim(block, 0, width, axis=dim), axis, backward)
        block = jnp.concatenate([low, block, high], axis=dim)
    return block


def partner_pairs(count, distance):
    return [(i, i ^ distance) for i in range(count)]


def butterfly(tree, axis, combine, ordered=False, distance=1):
    count = lax.axis_size(axis)
    assert count & (count - 1) == 0
    index = lax.axis_index(axis)
    while distance < count:
        other = lax.ppermute(tree, axis, partner_pairs(count, distance))
        if ordered:
            upper = (index // distance) % 2 == 1
            first = jax.tree.map(lambda a, b: jnp.where(upper, b, a), tree, other)
            second = jax.tree.map(lambda a, b: jnp.where(upper, a, b), tree, other)
            tree = combine(first, second)
        else:
            tree = combine(tree, other)
        distance *= 2
    return tree


def add_trees(a, b):
    return jax.tree.map(jnp.add, a, b)


def narrow_butterfly(block, axis, distance=1):
    count = lax.axis_size(axis)
    while distance < count:
        sent = block.astype(jnp.bfloat16)
        other = lax.ppermute(sent, axis, partner_pairs(count, distance))
        block = sent.astype(jnp.float32) + other.astype(jnp.float32)
        distance *= 2
    return block


def softmax_combine(a, b):
    max_a, total_a, mixed_a = a
    max_b, total_b, mixed_b = b
    mixed_a = mixed_a.astype(jnp.float32)
    mixed_b = mixed_b.astype(jnp.float32)
    top = jnp.maximum(max_a, max_b)
    factor_a = jnp.exp(max_a - top)
    factor_b = jnp.exp(max_b - top)
    return (
        top,
        total_a * factor_a + total_b * factor_b,
        (scale_heads(mixed_a, factor_a) + scale_heads(mixed_b, factor_b)).astype(jnp.bfloat16),
    )


def reduce_scatter_rows(block, axis):
    count = lax.axis_size(axis)
    assert count & (count - 1) == 0
    index = lax.axis_index(axis)
    distance = count // 2
    while distance >= 1:
        half = block.shape[0] // 2
        upper = (index // distance) % 2 == 1
        low, high = block[:half], block[half:]
        keep = jnp.where(upper, high, low)
        send = jnp.where(upper, low, high)
        block = keep + lax.ppermute(send, axis, partner_pairs(count, distance))
        distance //= 2
    return block


def partner_rows(hits, digits, distance):
    count_rows, width = hits.shape
    digit_rows = digits.T.reshape(2 * count_rows // width, width)
    payload = jnp.concatenate(
        [hits, jnp.pad(digit_rows, ((0, (-digit_rows.shape[0]) % 16), (0, 0)))]
    )
    other = lax.ppermute(payload, "phi", partner_pairs(lax.axis_size("phi"), distance))
    other_hits = other[:count_rows]
    other_digits = other[count_rows : count_rows + digit_rows.shape[0]].reshape(2, count_rows).T
    upper = (lax.axis_index("phi") // distance) % 2 == 1
    hits = jnp.where(
        upper, jnp.concatenate([other_hits, hits]), jnp.concatenate([hits, other_hits])
    )
    digits = jnp.where(
        upper, jnp.concatenate([other_digits, digits]), jnp.concatenate([digits, other_digits])
    )
    return hits, digits


def norm_rows(entries):
    widened = entries.astype(jnp.float32)
    centred = widened - jnp.mean(widened, axis=-1, keepdims=True)
    spread = jnp.mean(centred * centred, axis=-1, keepdims=True)
    return centred * lax.rsqrt(spread + 1e-05)


def window_attend(query_rows, kv_ext):
    row_count, model_width = query_rows.shape
    head_size = model_width // HEADS
    key_count = kv_ext.shape[0]
    key_span = key_count - row_count
    query_heads = query_rows.reshape(row_count, HEADS, head_size)
    key_heads = kv_ext[:, :model_width].reshape(key_count, HEADS, head_size)
    value_heads = kv_ext[:, model_width:].reshape(key_count, HEADS, head_size)
    scores = jnp.einsum(
        "qhd,khd->hqk", query_heads, key_heads, preferred_element_type=jnp.float32
    ) * head_size ** (-0.5)
    offset = lax.broadcasted_iota(jnp.int32, (row_count, key_count), 1) - lax.broadcasted_iota(
        jnp.int32, (row_count, key_count), 0
    )
    inside = jnp.logical_and(offset >= 0, offset < key_span)
    scores = jnp.where(inside[None, :, :], scores, -1e30)
    raised = jnp.exp(scores - jnp.max(scores, axis=-1, keepdims=True))
    weights = (raised / jnp.sum(raised, axis=-1, keepdims=True)).astype(jnp.bfloat16)
    attended = jnp.einsum("hqk,khd->qhd", weights, value_heads, preferred_element_type=jnp.float32)
    return attended.reshape(row_count, model_width).astype(jnp.bfloat16)


def split_heads(matrix):
    row_count, model_width = matrix.shape
    return matrix.reshape(row_count, HEADS, model_width // HEADS).transpose(1, 0, 2)


def head_partial(operands):
    query_head, key_head, value_head = operands
    scores = lax.dot_general(
        query_head, key_head, (((1,), (1,)), ((), ())), preferred_element_type=jnp.float32
    ) * query_head.shape[1] ** (-0.5)
    local_max = jnp.max(scores, axis=1)
    raised = jnp.exp(scores - local_max[:, None]).astype(jnp.bfloat16)
    total = jnp.sum(raised.astype(jnp.float32), axis=1)
    mixed = jnp.dot(raised, value_head, preferred_element_type=jnp.float32)
    return (local_max, total, mixed)


def scale_heads(mixed, factor):
    query_count, model_width = mixed.shape
    head_count = factor.shape[0]
    shaped = mixed.reshape(query_count, head_count, model_width // head_count)
    return (shaped * factor.T[:, :, None]).reshape(query_count, model_width)


def loss_coefficients(
    sigma, target, matched, intersection, predicted, truth_count, hits_total, model_width
):
    denom = predicted + truth_count + 1.0
    slope = -2.0 / denom
    level = (2.0 * intersection + 1.0) / (denom * denom)
    dice_part = hits_total * (slope[:, None] * target + level[:, None]) * sigma * (1.0 - sigma)
    return (matched[:, None] * (sigma - target + dice_part) * model_width ** (-0.5)).astype(
        jnp.bfloat16
    )


def body(
    hits,
    enc_qkv,
    enc_out,
    enc_up,
    enc_down,
    queries,
    cross_q,
    cross_kv,
    cross_out,
    mask_first,
    mask_second,
    truth,
    match,
):
    model_width = hits.shape[1]
    local_hits = hits.shape[0]
    query_count = queries.shape[0]
    hits_total = float(local_hits * lax.axis_size("phi") * lax.axis_size("query"))
    track_count = query_count * lax.axis_size("query") // 2
    normed = norm_rows(hits).astype(jnp.bfloat16)
    projected = jnp.dot(normed, enc_qkv, preferred_element_type=jnp.float32).astype(jnp.bfloat16)
    extended = extended_2(projected[:, model_width:], ((("phi", "query"), 0),), WIN // 2)
    block_rows = local_hits // 2
    span = extended.shape[0] - local_hits
    attended = jnp.concatenate(
        [
            window_attend(
                projected[b * block_rows : (b + 1) * block_rows, :model_width],
                extended[b * block_rows : b * block_rows + block_rows + span],
            )
            for b in range(2)
        ]
    )
    residual = hits.astype(jnp.float32) + jnp.dot(
        attended, enc_out, preferred_element_type=jnp.float32
    )
    upper = jax.nn.gelu(
        jnp.dot(
            norm_rows(residual).astype(jnp.bfloat16), enc_up, preferred_element_type=jnp.float32
        ),
        approximate=True,
    ).astype(jnp.bfloat16)
    encoded = (residual + jnp.dot(upper, enc_down, preferred_element_type=jnp.float32)).astype(
        jnp.bfloat16
    )
    local_kv = jnp.dot(
        norm_rows(encoded).astype(jnp.bfloat16), cross_kv, preferred_element_type=jnp.float32
    ).astype(jnp.bfloat16)
    shifted = truth + 1
    digits = jnp.stack([shifted // 256, shifted % 256], axis=1).astype(jnp.bfloat16)
    digits = jnp.pad(digits, ((0, 0), (0, 126)))
    gathered = lax.all_gather(
        jnp.concatenate([local_kv, encoded, digits], axis=1), "query", axis=0, tiled=True
    )
    group_kv = gathered[:, : 2 * model_width]
    group_hits = gathered[:, 2 * model_width : 3 * model_width]
    group_digits = gathered[:, 3 * model_width :].astype(jnp.int32)
    group_truth = group_digits[:, 0] * 256 + group_digits[:, 1] - 1
    query_proj = jnp.dot(queries, cross_q, preferred_element_type=jnp.float32).astype(jnp.bfloat16)
    head_size = model_width // HEADS
    group_count = group_kv.shape[0]
    query_heads = query_proj.reshape(query_count, HEADS, head_size)
    key_heads = group_kv[:, :model_width].reshape(group_count, HEADS, head_size)
    value_heads = group_kv[:, model_width:].reshape(group_count, HEADS, head_size)
    scores = jnp.einsum(
        "qhd,khd->hqk", query_heads, key_heads, preferred_element_type=jnp.float32
    ) * head_size ** (-0.5)
    local_max = jnp.max(scores, axis=-1)
    raised = jnp.exp(scores - local_max[..., None]).astype(jnp.bfloat16)
    local_total = jnp.sum(raised.astype(jnp.float32), axis=-1)
    local_mixed = jnp.einsum(
        "hqk,khd->qhd", raised, value_heads, preferred_element_type=jnp.float32
    ).reshape(query_count, model_width)
    _, total, mixed = butterfly(
        (local_max, local_total, local_mixed.astype(jnp.bfloat16)),
        "phi",
        softmax_combine,
        ordered=True,
    )
    mixed = mixed.astype(jnp.float32)
    context = scale_heads(mixed, 1.0 / total).astype(jnp.bfloat16)
    mixed_queries = queries.astype(jnp.float32) + jnp.dot(
        context, cross_out, preferred_element_type=jnp.float32
    )
    mask_hidden = jax.nn.relu(
        jnp.dot(
            norm_rows(mixed_queries).astype(jnp.bfloat16),
            mask_first,
            preferred_element_type=jnp.float32,
        )
    ).astype(jnp.bfloat16)
    mask_embed = jnp.dot(mask_hidden, mask_second, preferred_element_type=jnp.float32).astype(
        jnp.bfloat16
    )
    pair_hits = group_hits
    pair_digits = gathered[:, 3 * model_width : 3 * model_width + 2]
    for distance in (1, 2):
        pair_hits, pair_digits = partner_rows(pair_hits, pair_digits, distance)
    pair_digits = pair_digits.astype(jnp.int32)
    pair_truth = pair_digits[:, 0] * 256 + pair_digits[:, 1] - 1
    logits = lax.dot_general(
        mask_embed, pair_hits, (((1,), (1,)), ((), ())), preferred_element_type=jnp.float32
    ) * model_width ** (-0.5)
    sigma = jax.nn.sigmoid(logits)
    matched_flag = match < track_count
    matched = matched_flag.astype(jnp.float32)
    target = jnp.logical_and(match[:, None] == pair_truth[None, :], matched_flag[:, None]).astype(
        jnp.float32
    )
    intersection, predicted, truth_count = butterfly(
        jnp.stack(
            [jnp.sum(sigma * target, axis=1), jnp.sum(sigma, axis=1), jnp.sum(target, axis=1)]
        ),
        "phi",
        add_trees,
        distance=4,
    )
    mask_fill = predicted / hits_total
    coef = loss_coefficients(
        sigma, target, matched, intersection, predicted, truth_count, hits_total, model_width
    )
    mask_grad = narrow_butterfly(
        jnp.dot(coef, pair_hits, preferred_element_type=jnp.float32), "phi", distance=4
    )
    group_count = group_hits.shape[0]
    own_coef = lax.dynamic_slice_in_dim(
        coef, (lax.axis_index("phi") % 4) * group_count, group_count, axis=1
    )
    hit_grad = reduce_scatter_rows(
        lax.dot_general(
            own_coef, mask_embed, (((0,), (0,)), ((), ())), preferred_element_type=jnp.float32
        ),
        "query",
    )
    return (encoded, mask_embed, hit_grad, mask_grad, mask_fill)


def solution(mesh):
    return jax.shard_map(
        body,
        mesh=mesh,
        in_specs=(
            P(("event", "phi", "query"), None),
            P(),
            P(),
            P(),
            P(),
            P("query", None),
            P(),
            P(),
            P(),
            P(),
            P(),
            P(("event", "phi", "query")),
            P(("event", "query")),
        ),
        out_specs=(
            P(("event", "phi", "query"), None),
            P(("event", "query"), None),
            P(("event", "phi", "query"), None),
            P(("event", "query"), None),
            P(("event", "query")),
        ),
        check_vma=False,
    )
```

```python
import jax
import jax.numpy as jnp
from jax import lax
from jax.experimental import pallas as pl
from jax.sharding import PartitionSpec as P

HEADS = 8
WIN = 512


def extended_2(block, sides, width):
    for axis, dim in sides:
        count = lax.axis_size(axis)
        forward = [(i, i + 1) for i in range(count - 1)]
        forward.append((count - 1, 0))
        backward = [(target, source) for source, target in forward]
        low = lax.ppermute(
            lax.slice_in_dim(block, block.shape[dim] - width, None, axis=dim), axis, forward
        )
        high = lax.ppermute(lax.slice_in_dim(block, 0, width, axis=dim), axis, backward)
        block = jnp.concatenate([low, block, high], axis=dim)
    return block


def partner_pairs(count, distance):
    return [(i, i ^ distance) for i in range(count)]


def butterfly(tree, axis, combine, ordered=False, distance=1):
    count = lax.axis_size(axis)
    assert count & (count - 1) == 0
    index = lax.axis_index(axis)
    while distance < count:
        other = lax.ppermute(tree, axis, partner_pairs(count, distance))
        if ordered:
            upper = (index // distance) % 2 == 1
            first = jax.tree.map(lambda a, b: jnp.where(upper, b, a), tree, other)
            second = jax.tree.map(lambda a, b: jnp.where(upper, a, b), tree, other)
            tree = combine(first, second)
        else:
            tree = combine(tree, other)
        distance *= 2
    return tree


def add_trees(a, b):
    return jax.tree.map(jnp.add, a, b)


def narrow_butterfly(block, axis, distance=1):
    count = lax.axis_size(axis)
    while distance < count:
        sent = block.astype(jnp.bfloat16)
        other = lax.ppermute(sent, axis, partner_pairs(count, distance))
        block = sent.astype(jnp.float32) + other.astype(jnp.float32)
        distance *= 2
    return block


def softmax_combine(a, b):
    max_a, total_a, mixed_a = a
    max_b, total_b, mixed_b = b
    mixed_a = mixed_a.astype(jnp.float32)
    mixed_b = mixed_b.astype(jnp.float32)
    top = jnp.maximum(max_a, max_b)
    factor_a = jnp.exp(max_a - top)
    factor_b = jnp.exp(max_b - top)
    return (
        top,
        total_a * factor_a + total_b * factor_b,
        (scale_heads(mixed_a, factor_a) + scale_heads(mixed_b, factor_b)).astype(jnp.bfloat16),
    )


def reduce_scatter_rows(block, axis):
    count = lax.axis_size(axis)
    assert count & (count - 1) == 0
    index = lax.axis_index(axis)
    distance = count // 2
    while distance >= 1:
        half = block.shape[0] // 2
        upper = (index // distance) % 2 == 1
        low, high = block[:half], block[half:]
        keep = jnp.where(upper, high, low)
        send = jnp.where(upper, low, high)
        block = keep + lax.ppermute(send, axis, partner_pairs(count, distance))
        distance //= 2
    return block


def partner_rows(hits, digits, distance):
    count_rows, width = hits.shape
    digit_rows = digits.T.reshape(2 * count_rows // width, width)
    payload = jnp.concatenate(
        [hits, jnp.pad(digit_rows, ((0, (-digit_rows.shape[0]) % 16), (0, 0)))]
    )
    other = lax.ppermute(payload, "phi", partner_pairs(lax.axis_size("phi"), distance))
    other_hits = other[:count_rows]
    other_digits = other[count_rows : count_rows + digit_rows.shape[0]].reshape(2, count_rows).T
    upper = (lax.axis_index("phi") // distance) % 2 == 1
    hits = jnp.where(
        upper, jnp.concatenate([other_hits, hits]), jnp.concatenate([hits, other_hits])
    )
    digits = jnp.where(
        upper, jnp.concatenate([other_digits, digits]), jnp.concatenate([digits, other_digits])
    )
    return hits, digits


def cross_kernel(query_ref, key_ref, value_ref, max_ref, total_ref, mixed_ref):
    query = query_ref[...]
    scores = lax.dot_general(
        query, key_ref[...], (((1,), (1,)), ((), ())), preferred_element_type=jnp.float32
    ) * query.shape[1] ** (-0.5)
    local_max = jnp.max(scores, axis=1, keepdims=True)
    raised = jnp.exp(scores - local_max).astype(jnp.bfloat16)
    max_ref[...] = local_max
    total_ref[...] = jnp.sum(raised.astype(jnp.float32), axis=1, keepdims=True)
    mixed_ref[...] = jnp.dot(raised, value_ref[...], preferred_element_type=jnp.float32)


def cross_partials(query_heads, key_heads, value_heads):
    head_count, query_count, head_size = query_heads.shape
    key_count = key_heads.shape[1]
    query_spec = pl.BlockSpec((None, query_count, head_size), lambda h: (h, 0, 0))
    key_spec = pl.BlockSpec((None, key_count, head_size), lambda h: (h, 0, 0))
    stat_spec = pl.BlockSpec((None, query_count, 1), lambda h: (h, 0, 0))
    return pl.pallas_call(
        cross_kernel,
        grid=(head_count,),
        in_specs=[query_spec, key_spec, key_spec],
        out_specs=[stat_spec, stat_spec, query_spec],
        out_shape=[
            jax.ShapeDtypeStruct((head_count, query_count, 1), jnp.float32),
            jax.ShapeDtypeStruct((head_count, query_count, 1), jnp.float32),
            jax.ShapeDtypeStruct((head_count, query_count, head_size), jnp.float32),
        ],
        cost_estimate=pl.CostEstimate(
            flops=4 * head_count * query_count * key_count * head_size,
            transcendentals=head_count * query_count * key_count,
            bytes_accessed=2 * head_count * (query_count + 2 * key_count) * head_size
            + 4 * head_count * query_count * (head_size + 2),
        ),
    )(query_heads, key_heads, value_heads)


def norm_rows(entries):
    widened = entries.astype(jnp.float32)
    centred = widened - jnp.mean(widened, axis=-1, keepdims=True)
    spread = jnp.mean(centred * centred, axis=-1, keepdims=True)
    return centred * lax.rsqrt(spread + 1e-05)


def window_attend(query_rows, kv_ext):
    row_count, model_width = query_rows.shape
    head_size = model_width // HEADS
    key_count = kv_ext.shape[0]
    key_span = key_count - row_count
    query_heads = query_rows.reshape(row_count, HEADS, head_size)
    key_heads = kv_ext[:, :model_width].reshape(key_count, HEADS, head_size)
    value_heads = kv_ext[:, model_width:].reshape(key_count, HEADS, head_size)
    scores = jnp.einsum(
        "qhd,khd->hqk", query_heads, key_heads, preferred_element_type=jnp.float32
    ) * head_size ** (-0.5)
    offset = lax.broadcasted_iota(jnp.int32, (row_count, key_count), 1) - lax.broadcasted_iota(
        jnp.int32, (row_count, key_count), 0
    )
    inside = jnp.logical_and(offset >= 0, offset < key_span)
    scores = jnp.where(inside[None, :, :], scores, -1e30)
    raised = jnp.exp(scores - jnp.max(scores, axis=-1, keepdims=True))
    weights = (raised / jnp.sum(raised, axis=-1, keepdims=True)).astype(jnp.bfloat16)
    attended = jnp.einsum("hqk,khd->qhd", weights, value_heads, preferred_element_type=jnp.float32)
    return attended.reshape(row_count, model_width).astype(jnp.bfloat16)


def split_heads(matrix):
    row_count, model_width = matrix.shape
    return matrix.reshape(row_count, HEADS, model_width // HEADS).transpose(1, 0, 2)


def head_partial(operands):
    query_head, key_head, value_head = operands
    scores = lax.dot_general(
        query_head, key_head, (((1,), (1,)), ((), ())), preferred_element_type=jnp.float32
    ) * query_head.shape[1] ** (-0.5)
    local_max = jnp.max(scores, axis=1)
    raised = jnp.exp(scores - local_max[:, None]).astype(jnp.bfloat16)
    total = jnp.sum(raised.astype(jnp.float32), axis=1)
    mixed = jnp.dot(raised, value_head, preferred_element_type=jnp.float32)
    return (local_max, total, mixed)


def scale_heads(mixed, factor):
    query_count, model_width = mixed.shape
    head_count = factor.shape[0]
    shaped = mixed.reshape(query_count, head_count, model_width // head_count)
    return (shaped * factor.T[:, :, None]).reshape(query_count, model_width)


def loss_coefficients(
    sigma, target, matched, intersection, predicted, truth_count, hits_total, model_width
):
    denom = predicted + truth_count + 1.0
    slope = -2.0 / denom
    level = (2.0 * intersection + 1.0) / (denom * denom)
    dice_part = hits_total * (slope[:, None] * target + level[:, None]) * sigma * (1.0 - sigma)
    return (matched[:, None] * (sigma - target + dice_part) * model_width ** (-0.5)).astype(
        jnp.bfloat16
    )


def body(
    hits,
    enc_qkv,
    enc_out,
    enc_up,
    enc_down,
    queries,
    cross_q,
    cross_kv,
    cross_out,
    mask_first,
    mask_second,
    truth,
    match,
):
    model_width = hits.shape[1]
    local_hits = hits.shape[0]
    query_count = queries.shape[0]
    hits_total = float(local_hits * lax.axis_size("phi") * lax.axis_size("query"))
    track_count = query_count * lax.axis_size("query") // 2
    normed = norm_rows(hits).astype(jnp.bfloat16)
    projected = jnp.dot(normed, enc_qkv, preferred_element_type=jnp.float32).astype(jnp.bfloat16)
    extended = extended_2(projected[:, model_width:], ((("phi", "query"), 0),), WIN // 2)
    block_rows = local_hits // 2
    span = extended.shape[0] - local_hits
    attended = jnp.concatenate(
        [
            window_attend(
                projected[b * block_rows : (b + 1) * block_rows, :model_width],
                extended[b * block_rows : b * block_rows + block_rows + span],
            )
            for b in range(2)
        ]
    )
    residual = hits.astype(jnp.float32) + jnp.dot(
        attended, enc_out, preferred_element_type=jnp.float32
    )
    upper = jax.nn.gelu(
        jnp.dot(
            norm_rows(residual).astype(jnp.bfloat16), enc_up, preferred_element_type=jnp.float32
        ),
        approximate=True,
    ).astype(jnp.bfloat16)
    encoded = (residual + jnp.dot(upper, enc_down, preferred_element_type=jnp.float32)).astype(
        jnp.bfloat16
    )
    local_kv = jnp.dot(
        norm_rows(encoded).astype(jnp.bfloat16), cross_kv, preferred_element_type=jnp.float32
    ).astype(jnp.bfloat16)
    shifted = truth + 1
    digits = jnp.stack([shifted // 256, shifted % 256], axis=1).astype(jnp.bfloat16)
    digits = jnp.pad(digits, ((0, 0), (0, 126)))
    gathered = lax.all_gather(
        jnp.concatenate([local_kv, encoded, digits], axis=1), "query", axis=0, tiled=True
    )
    group_kv = gathered[:, : 2 * model_width]
    group_hits = gathered[:, 2 * model_width : 3 * model_width]
    group_digits = gathered[:, 3 * model_width :].astype(jnp.int32)
    group_truth = group_digits[:, 0] * 256 + group_digits[:, 1] - 1
    query_proj = jnp.dot(queries, cross_q, preferred_element_type=jnp.float32).astype(jnp.bfloat16)
    head_size = model_width // HEADS
    group_count = group_kv.shape[0]
    query_heads = query_proj.reshape(query_count, HEADS, head_size).transpose(1, 0, 2)
    key_heads = group_kv[:, :model_width].reshape(group_count, HEADS, head_size).transpose(1, 0, 2)
    value_heads = (
        group_kv[:, model_width:].reshape(group_count, HEADS, head_size).transpose(1, 0, 2)
    )
    head_max, head_total, head_mixed = cross_partials(query_heads, key_heads, value_heads)
    local_max = head_max[:, :, 0]
    local_total = head_total[:, :, 0]
    local_mixed = head_mixed.transpose(1, 0, 2).reshape(query_count, model_width)
    _, total, mixed = butterfly(
        (local_max, local_total, local_mixed.astype(jnp.bfloat16)),
        "phi",
        softmax_combine,
        ordered=True,
    )
    mixed = mixed.astype(jnp.float32)
    context = scale_heads(mixed, 1.0 / total).astype(jnp.bfloat16)
    mixed_queries = queries.astype(jnp.float32) + jnp.dot(
        context, cross_out, preferred_element_type=jnp.float32
    )
    mask_hidden = jax.nn.relu(
        jnp.dot(
            norm_rows(mixed_queries).astype(jnp.bfloat16),
            mask_first,
            preferred_element_type=jnp.float32,
        )
    ).astype(jnp.bfloat16)
    mask_embed = jnp.dot(mask_hidden, mask_second, preferred_element_type=jnp.float32).astype(
        jnp.bfloat16
    )
    pair_hits = group_hits
    pair_digits = gathered[:, 3 * model_width : 3 * model_width + 2]
    for distance in (1, 2):
        pair_hits, pair_digits = partner_rows(pair_hits, pair_digits, distance)
    pair_digits = pair_digits.astype(jnp.int32)
    pair_truth = pair_digits[:, 0] * 256 + pair_digits[:, 1] - 1
    logits = lax.dot_general(
        mask_embed, pair_hits, (((1,), (1,)), ((), ())), preferred_element_type=jnp.float32
    ) * model_width ** (-0.5)
    sigma = jax.nn.sigmoid(logits)
    matched_flag = match < track_count
    matched = matched_flag.astype(jnp.float32)
    target = jnp.logical_and(match[:, None] == pair_truth[None, :], matched_flag[:, None]).astype(
        jnp.float32
    )
    intersection, predicted, truth_count = butterfly(
        jnp.stack(
            [jnp.sum(sigma * target, axis=1), jnp.sum(sigma, axis=1), jnp.sum(target, axis=1)]
        ),
        "phi",
        add_trees,
        distance=4,
    )
    mask_fill = predicted / hits_total
    coef = loss_coefficients(
        sigma, target, matched, intersection, predicted, truth_count, hits_total, model_width
    )
    mask_grad = narrow_butterfly(
        jnp.dot(coef, pair_hits, preferred_element_type=jnp.float32), "phi", distance=4
    )
    group_count = group_hits.shape[0]
    own_coef = lax.dynamic_slice_in_dim(
        coef, (lax.axis_index("phi") % 4) * group_count, group_count, axis=1
    )
    hit_grad = reduce_scatter_rows(
        lax.dot_general(
            own_coef, mask_embed, (((0,), (0,)), ((), ())), preferred_element_type=jnp.float32
        ),
        "query",
    )
    return (encoded, mask_embed, hit_grad, mask_grad, mask_fill)


def solution(mesh):
    return jax.shard_map(
        body,
        mesh=mesh,
        in_specs=(
            P(("event", "phi", "query"), None),
            P(),
            P(),
            P(),
            P(),
            P("query", None),
            P(),
            P(),
            P(),
            P(),
            P(),
            P(("event", "phi", "query")),
            P(("event", "query")),
        ),
        out_specs=(
            P(("event", "phi", "query"), None),
            P(("event", "query"), None),
            P(("event", "phi", "query"), None),
            P(("event", "query"), None),
            P(("event", "query")),
        ),
        check_vma=False,
    )
```

```python
import jax
import jax.numpy as jnp
from jax import lax
from jax.sharding import PartitionSpec as P

HEADS = 8
WIN = 512


def extended_2(block, sides, width):
    for axis, dim in sides:
        count = lax.axis_size(axis)
        forward = [(i, i + 1) for i in range(count - 1)]
        forward.append((count - 1, 0))
        backward = [(target, source) for source, target in forward]
        low = lax.ppermute(
            lax.slice_in_dim(block, block.shape[dim] - width, None, axis=dim), axis, forward
        )
        high = lax.ppermute(lax.slice_in_dim(block, 0, width, axis=dim), axis, backward)
        block = jnp.concatenate([low, block, high], axis=dim)
    return block


def partner_pairs(count, distance):
    return [(i, i ^ distance) for i in range(count)]


def butterfly(tree, axis, combine, ordered=False, distance=1):
    count = lax.axis_size(axis)
    assert count & (count - 1) == 0
    index = lax.axis_index(axis)
    while distance < count:
        other = lax.ppermute(tree, axis, partner_pairs(count, distance))
        if ordered:
            upper = (index // distance) % 2 == 1
            first = jax.tree.map(lambda a, b: jnp.where(upper, b, a), tree, other)
            second = jax.tree.map(lambda a, b: jnp.where(upper, a, b), tree, other)
            tree = combine(first, second)
        else:
            tree = combine(tree, other)
        distance *= 2
    return tree


def add_trees(a, b):
    return jax.tree.map(jnp.add, a, b)


def narrow_butterfly(block, axis, distance=1):
    count = lax.axis_size(axis)
    while distance < count:
        sent = block.astype(jnp.bfloat16)
        other = lax.ppermute(sent, axis, partner_pairs(count, distance))
        block = sent.astype(jnp.float32) + other.astype(jnp.float32)
        distance *= 2
    return block


def softmax_combine(a, b):
    (max_a, total_a), mixed_a = a
    (max_b, total_b), mixed_b = b
    mixed_a = mixed_a.astype(jnp.float32)
    mixed_b = mixed_b.astype(jnp.float32)
    top = jnp.maximum(max_a, max_b)
    factor_a = jnp.exp(max_a - top)
    factor_b = jnp.exp(max_b - top)
    return (
        jnp.stack([top, total_a * factor_a + total_b * factor_b]),
        (scale_heads(mixed_a, factor_a) + scale_heads(mixed_b, factor_b)).astype(jnp.bfloat16),
    )


def reduce_scatter_rows(block, axis):
    count = lax.axis_size(axis)
    assert count & (count - 1) == 0
    index = lax.axis_index(axis)
    distance = count // 2
    while distance >= 1:
        half = block.shape[0] // 2
        upper = (index // distance) % 2 == 1
        low, high = block[:half], block[half:]
        keep = jnp.where(upper, high, low)
        send = jnp.where(upper, low, high)
        block = keep + lax.ppermute(send, axis, partner_pairs(count, distance))
        distance //= 2
    return block


def partner_rows(hits, digits, distance):
    count_rows, width = hits.shape
    digit_rows = digits.T.reshape(2 * count_rows // width, width)
    payload = jnp.concatenate(
        [hits, jnp.pad(digit_rows, ((0, (-digit_rows.shape[0]) % 16), (0, 0)))]
    )
    other = lax.ppermute(payload, "phi", partner_pairs(lax.axis_size("phi"), distance))
    other_hits = other[:count_rows]
    other_digits = other[count_rows : count_rows + digit_rows.shape[0]].reshape(2, count_rows).T
    upper = (lax.axis_index("phi") // distance) % 2 == 1
    hits = jnp.where(
        upper, jnp.concatenate([other_hits, hits]), jnp.concatenate([hits, other_hits])
    )
    digits = jnp.where(
        upper, jnp.concatenate([other_digits, digits]), jnp.concatenate([digits, other_digits])
    )
    return hits, digits


def norm_rows(entries):
    widened = entries.astype(jnp.float32)
    centred = widened - jnp.mean(widened, axis=-1, keepdims=True)
    spread = jnp.mean(centred * centred, axis=-1, keepdims=True)
    return centred * lax.rsqrt(spread + 1e-05)


def window_attend(query_rows, kv_ext):
    row_count, model_width = query_rows.shape
    head_size = model_width // HEADS
    key_count = kv_ext.shape[0]
    key_span = key_count - row_count
    query_heads = query_rows.reshape(row_count, HEADS, head_size)
    key_heads = kv_ext[:, :model_width].reshape(key_count, HEADS, head_size)
    value_heads = kv_ext[:, model_width:].reshape(key_count, HEADS, head_size)
    scores = jnp.einsum(
        "qhd,khd->hqk", query_heads, key_heads, preferred_element_type=jnp.float32
    ) * head_size ** (-0.5)
    offset = lax.broadcasted_iota(jnp.int32, (row_count, key_count), 1) - lax.broadcasted_iota(
        jnp.int32, (row_count, key_count), 0
    )
    inside = jnp.logical_and(offset >= 0, offset < key_span)
    scores = jnp.where(inside[None, :, :], scores, -1e30)
    raised = jnp.exp(scores - jnp.max(scores, axis=-1, keepdims=True))
    weights = (raised / jnp.sum(raised, axis=-1, keepdims=True)).astype(jnp.bfloat16)
    attended = jnp.einsum("hqk,khd->qhd", weights, value_heads, preferred_element_type=jnp.float32)
    return attended.reshape(row_count, model_width).astype(jnp.bfloat16)


def split_heads(matrix):
    row_count, model_width = matrix.shape
    return matrix.reshape(row_count, HEADS, model_width // HEADS).transpose(1, 0, 2)


def head_partial(operands):
    query_head, key_head, value_head = operands
    scores = lax.dot_general(
        query_head, key_head, (((1,), (1,)), ((), ())), preferred_element_type=jnp.float32
    ) * query_head.shape[1] ** (-0.5)
    local_max = jnp.max(scores, axis=1)
    raised = jnp.exp(scores - local_max[:, None]).astype(jnp.bfloat16)
    total = jnp.sum(raised.astype(jnp.float32), axis=1)
    mixed = jnp.dot(raised, value_head, preferred_element_type=jnp.float32)
    return (local_max, total, mixed)


def scale_heads(mixed, factor):
    query_count, model_width = mixed.shape
    head_count = factor.shape[0]
    shaped = mixed.reshape(query_count, head_count, model_width // head_count)
    return (shaped * factor.T[:, :, None]).reshape(query_count, model_width)


def loss_coefficients(
    sigma, target, matched, intersection, predicted, truth_count, hits_total, model_width
):
    denom = predicted + truth_count + 1.0
    slope = -2.0 / denom
    level = (2.0 * intersection + 1.0) / (denom * denom)
    dice_part = hits_total * (slope[:, None] * target + level[:, None]) * sigma * (1.0 - sigma)
    return (matched[:, None] * (sigma - target + dice_part) * model_width ** (-0.5)).astype(
        jnp.bfloat16
    )


def body(
    hits,
    enc_qkv,
    enc_out,
    enc_up,
    enc_down,
    queries,
    cross_q,
    cross_kv,
    cross_out,
    mask_first,
    mask_second,
    truth,
    match,
):
    model_width = hits.shape[1]
    local_hits = hits.shape[0]
    query_count = queries.shape[0]
    hits_total = float(local_hits * lax.axis_size("phi") * lax.axis_size("query"))
    track_count = query_count * lax.axis_size("query") // 2
    normed = norm_rows(hits).astype(jnp.bfloat16)
    projected = jnp.dot(normed, enc_qkv, preferred_element_type=jnp.float32).astype(jnp.bfloat16)
    extended = extended_2(projected[:, model_width:], ((("phi", "query"), 0),), WIN // 2)
    block_rows = local_hits // 2
    span = extended.shape[0] - local_hits
    attended = jnp.concatenate(
        [
            window_attend(
                projected[b * block_rows : (b + 1) * block_rows, :model_width],
                extended[b * block_rows : b * block_rows + block_rows + span],
            )
            for b in range(2)
        ]
    )
    residual = hits.astype(jnp.float32) + jnp.dot(
        attended, enc_out, preferred_element_type=jnp.float32
    )
    upper = jax.nn.gelu(
        jnp.dot(
            norm_rows(residual).astype(jnp.bfloat16), enc_up, preferred_element_type=jnp.float32
        ),
        approximate=True,
    ).astype(jnp.bfloat16)
    encoded = (residual + jnp.dot(upper, enc_down, preferred_element_type=jnp.float32)).astype(
        jnp.bfloat16
    )
    local_kv = jnp.dot(
        norm_rows(encoded).astype(jnp.bfloat16), cross_kv, preferred_element_type=jnp.float32
    ).astype(jnp.bfloat16)
    shifted = truth + 1
    digits = jnp.stack([shifted // 256, shifted % 256], axis=1).astype(jnp.bfloat16)
    digits = jnp.pad(digits, ((0, 0), (0, 126)))
    gathered = lax.all_gather(
        jnp.concatenate([local_kv, encoded, digits], axis=1), "query", axis=0, tiled=True
    )
    group_kv = gathered[:, : 2 * model_width]
    group_hits = gathered[:, 2 * model_width : 3 * model_width]
    group_digits = gathered[:, 3 * model_width :].astype(jnp.int32)
    group_truth = group_digits[:, 0] * 256 + group_digits[:, 1] - 1
    query_proj = jnp.dot(queries, cross_q, preferred_element_type=jnp.float32).astype(jnp.bfloat16)
    head_size = model_width // HEADS
    group_count = group_kv.shape[0]
    query_heads = query_proj.reshape(query_count, HEADS, head_size)
    key_heads = group_kv[:, :model_width].reshape(group_count, HEADS, head_size)
    value_heads = group_kv[:, model_width:].reshape(group_count, HEADS, head_size)
    scores = jnp.einsum(
        "qhd,khd->hqk", query_heads, key_heads, preferred_element_type=jnp.float32
    ) * head_size ** (-0.5)
    local_max = jnp.max(scores, axis=-1)
    raised = jnp.exp(scores - local_max[..., None]).astype(jnp.bfloat16)
    local_total = jnp.sum(raised.astype(jnp.float32), axis=-1)
    local_mixed = jnp.einsum(
        "hqk,khd->qhd", raised, value_heads, preferred_element_type=jnp.float32
    ).reshape(query_count, model_width)
    (_, total), mixed = butterfly(
        (jnp.stack([local_max, local_total]), local_mixed.astype(jnp.bfloat16)),
        "phi",
        softmax_combine,
        ordered=True,
    )
    mixed = mixed.astype(jnp.float32)
    context = scale_heads(mixed, 1.0 / total).astype(jnp.bfloat16)
    mixed_queries = queries.astype(jnp.float32) + jnp.dot(
        context, cross_out, preferred_element_type=jnp.float32
    )
    mask_hidden = jax.nn.relu(
        jnp.dot(
            norm_rows(mixed_queries).astype(jnp.bfloat16),
            mask_first,
            preferred_element_type=jnp.float32,
        )
    ).astype(jnp.bfloat16)
    mask_embed = jnp.dot(mask_hidden, mask_second, preferred_element_type=jnp.float32).astype(
        jnp.bfloat16
    )
    pair_hits = group_hits
    pair_digits = gathered[:, 3 * model_width : 3 * model_width + 2]
    for distance in (1, 2):
        pair_hits, pair_digits = partner_rows(pair_hits, pair_digits, distance)
    pair_digits = pair_digits.astype(jnp.int32)
    pair_truth = pair_digits[:, 0] * 256 + pair_digits[:, 1] - 1
    logits = lax.dot_general(
        mask_embed, pair_hits, (((1,), (1,)), ((), ())), preferred_element_type=jnp.float32
    ) * model_width ** (-0.5)
    sigma = jax.nn.sigmoid(logits)
    matched_flag = match < track_count
    matched = matched_flag.astype(jnp.float32)
    target = jnp.logical_and(match[:, None] == pair_truth[None, :], matched_flag[:, None]).astype(
        jnp.float32
    )
    intersection, predicted, truth_count = butterfly(
        jnp.stack(
            [jnp.sum(sigma * target, axis=1), jnp.sum(sigma, axis=1), jnp.sum(target, axis=1)]
        ),
        "phi",
        add_trees,
        distance=4,
    )
    mask_fill = predicted / hits_total
    coef = loss_coefficients(
        sigma, target, matched, intersection, predicted, truth_count, hits_total, model_width
    )
    mask_grad = narrow_butterfly(
        jnp.dot(coef, pair_hits, preferred_element_type=jnp.float32), "phi", distance=4
    )
    group_count = group_hits.shape[0]
    own_coef = lax.dynamic_slice_in_dim(
        coef, (lax.axis_index("phi") % 4) * group_count, group_count, axis=1
    )
    hit_grad = reduce_scatter_rows(
        lax.dot_general(
            own_coef, mask_embed, (((0,), (0,)), ((), ())), preferred_element_type=jnp.float32
        ),
        "query",
    )
    return (encoded, mask_embed, hit_grad, mask_grad, mask_fill)


def solution(mesh):
    return jax.shard_map(
        body,
        mesh=mesh,
        in_specs=(
            P(("event", "phi", "query"), None),
            P(),
            P(),
            P(),
            P(),
            P("query", None),
            P(),
            P(),
            P(),
            P(),
            P(),
            P(("event", "phi", "query")),
            P(("event", "query")),
        ),
        out_specs=(
            P(("event", "phi", "query"), None),
            P(("event", "query"), None),
            P(("event", "phi", "query"), None),
            P(("event", "query"), None),
            P(("event", "query")),
        ),
        check_vma=False,
    )
```

```python
import jax
import jax.numpy as jnp
from jax import lax
from jax.sharding import PartitionSpec as P

HEADS = 8
WIN = 512


def extended_2(block, sides, width):
    for axis, dim in sides:
        count = lax.axis_size(axis)
        forward = [(i, i + 1) for i in range(count - 1)]
        forward.append((count - 1, 0))
        backward = [(target, source) for source, target in forward]
        low = lax.ppermute(
            lax.slice_in_dim(block, block.shape[dim] - width, None, axis=dim), axis, forward
        )
        high = lax.ppermute(lax.slice_in_dim(block, 0, width, axis=dim), axis, backward)
        block = jnp.concatenate([low, block, high], axis=dim)
    return block


def partner_pairs(count, distance):
    return [(i, i ^ distance) for i in range(count)]


def butterfly(tree, axis, combine, ordered=False, distance=1):
    count = lax.axis_size(axis)
    assert count & (count - 1) == 0
    index = lax.axis_index(axis)
    while distance < count:
        other = lax.ppermute(tree, axis, partner_pairs(count, distance))
        if ordered:
            upper = (index // distance) % 2 == 1
            first = jax.tree.map(lambda a, b: jnp.where(upper, b, a), tree, other)
            second = jax.tree.map(lambda a, b: jnp.where(upper, a, b), tree, other)
            tree = combine(first, second)
        else:
            tree = combine(tree, other)
        distance *= 2
    return tree


def add_trees(a, b):
    return jax.tree.map(jnp.add, a, b)


def narrow_butterfly(block, axis, distance=1):
    count = lax.axis_size(axis)
    while distance < count:
        sent = block.astype(jnp.bfloat16)
        other = lax.ppermute(sent, axis, partner_pairs(count, distance))
        block = sent.astype(jnp.float32) + other.astype(jnp.float32)
        distance *= 2
    return block


def softmax_combine(a, b):
    (max_a, total_a), mixed_a = a
    (max_b, total_b), mixed_b = b
    mixed_a = mixed_a.astype(jnp.float32)
    mixed_b = mixed_b.astype(jnp.float32)
    top = jnp.maximum(max_a, max_b)
    factor_a = jnp.exp(max_a - top)
    factor_b = jnp.exp(max_b - top)
    return (
        jnp.stack([top, total_a * factor_a + total_b * factor_b]),
        (scale_heads(mixed_a, factor_a) + scale_heads(mixed_b, factor_b)).astype(jnp.bfloat16),
    )


def pack_softmax(stats, mixed):
    width = mixed.shape[1]
    flat = stats.reshape(-1)
    high = flat.astype(jnp.bfloat16)
    rest = flat - high.astype(jnp.float32)
    middle = rest.astype(jnp.bfloat16)
    low = (rest - middle.astype(jnp.float32)).astype(jnp.bfloat16)
    pieces = jnp.concatenate([high, middle, low]).reshape(-1, width)
    return jnp.concatenate([mixed.astype(jnp.bfloat16), pieces])


def unpack_softmax(packed, query_count):
    pieces = packed[query_count:].reshape(3, -1).astype(jnp.float32)
    stats = (pieces[0] + pieces[1] + pieces[2]).reshape(2, HEADS, query_count)
    return stats, packed[:query_count].astype(jnp.float32)


def packed_combine(a, b):
    query_count = a.shape[0] * a.shape[1] // (a.shape[1] + 6 * HEADS)
    (max_a, total_a), mixed_a = unpack_softmax(a, query_count)
    (max_b, total_b), mixed_b = unpack_softmax(b, query_count)
    top = jnp.maximum(max_a, max_b)
    factor_a = jnp.exp(max_a - top)
    factor_b = jnp.exp(max_b - top)
    return pack_softmax(
        jnp.stack([top, total_a * factor_a + total_b * factor_b]),
        scale_heads(mixed_a, factor_a) + scale_heads(mixed_b, factor_b),
    )


def reduce_scatter_rows(block, axis):
    count = lax.axis_size(axis)
    assert count & (count - 1) == 0
    index = lax.axis_index(axis)
    distance = count // 2
    while distance >= 1:
        half = block.shape[0] // 2
        upper = (index // distance) % 2 == 1
        low, high = block[:half], block[half:]
        keep = jnp.where(upper, high, low)
        send = jnp.where(upper, low, high)
        block = keep + lax.ppermute(send, axis, partner_pairs(count, distance))
        distance //= 2
    return block


def partner_rows(hits, digits, distance):
    count_rows, width = hits.shape
    digit_rows = digits.T.reshape(2 * count_rows // width, width)
    payload = jnp.concatenate(
        [hits, jnp.pad(digit_rows, ((0, (-digit_rows.shape[0]) % 16), (0, 0)))]
    )
    other = lax.ppermute(payload, "phi", partner_pairs(lax.axis_size("phi"), distance))
    other_hits = other[:count_rows]
    other_digits = other[count_rows : count_rows + digit_rows.shape[0]].reshape(2, count_rows).T
    upper = (lax.axis_index("phi") // distance) % 2 == 1
    hits = jnp.where(
        upper, jnp.concatenate([other_hits, hits]), jnp.concatenate([hits, other_hits])
    )
    digits = jnp.where(
        upper, jnp.concatenate([other_digits, digits]), jnp.concatenate([digits, other_digits])
    )
    return hits, digits


def norm_rows(entries):
    widened = entries.astype(jnp.float32)
    centred = widened - jnp.mean(widened, axis=-1, keepdims=True)
    spread = jnp.mean(centred * centred, axis=-1, keepdims=True)
    return centred * lax.rsqrt(spread + 1e-05)


def window_attend(query_rows, kv_ext):
    row_count, model_width = query_rows.shape
    head_size = model_width // HEADS
    key_count = kv_ext.shape[0]
    key_span = key_count - row_count
    query_heads = query_rows.reshape(row_count, HEADS, head_size)
    key_heads = kv_ext[:, :model_width].reshape(key_count, HEADS, head_size)
    value_heads = kv_ext[:, model_width:].reshape(key_count, HEADS, head_size)
    scores = jnp.einsum(
        "qhd,khd->hqk", query_heads, key_heads, preferred_element_type=jnp.float32
    ) * head_size ** (-0.5)
    offset = lax.broadcasted_iota(jnp.int32, (row_count, key_count), 1) - lax.broadcasted_iota(
        jnp.int32, (row_count, key_count), 0
    )
    inside = jnp.logical_and(offset >= 0, offset < key_span)
    scores = jnp.where(inside[None, :, :], scores, -1e30)
    raised = jnp.exp(scores - jnp.max(scores, axis=-1, keepdims=True))
    weights = (raised / jnp.sum(raised, axis=-1, keepdims=True)).astype(jnp.bfloat16)
    attended = jnp.einsum("hqk,khd->qhd", weights, value_heads, preferred_element_type=jnp.float32)
    return attended.reshape(row_count, model_width).astype(jnp.bfloat16)


def split_heads(matrix):
    row_count, model_width = matrix.shape
    return matrix.reshape(row_count, HEADS, model_width // HEADS).transpose(1, 0, 2)


def head_partial(operands):
    query_head, key_head, value_head = operands
    scores = lax.dot_general(
        query_head, key_head, (((1,), (1,)), ((), ())), preferred_element_type=jnp.float32
    ) * query_head.shape[1] ** (-0.5)
    local_max = jnp.max(scores, axis=1)
    raised = jnp.exp(scores - local_max[:, None]).astype(jnp.bfloat16)
    total = jnp.sum(raised.astype(jnp.float32), axis=1)
    mixed = jnp.dot(raised, value_head, preferred_element_type=jnp.float32)
    return (local_max, total, mixed)


def scale_heads(mixed, factor):
    query_count, model_width = mixed.shape
    head_count = factor.shape[0]
    shaped = mixed.reshape(query_count, head_count, model_width // head_count)
    return (shaped * factor.T[:, :, None]).reshape(query_count, model_width)


def loss_coefficients(
    sigma, target, matched, intersection, predicted, truth_count, hits_total, model_width
):
    denom = predicted + truth_count + 1.0
    slope = -2.0 / denom
    level = (2.0 * intersection + 1.0) / (denom * denom)
    dice_part = hits_total * (slope[:, None] * target + level[:, None]) * sigma * (1.0 - sigma)
    return (matched[:, None] * (sigma - target + dice_part) * model_width ** (-0.5)).astype(
        jnp.bfloat16
    )


def body(
    hits,
    enc_qkv,
    enc_out,
    enc_up,
    enc_down,
    queries,
    cross_q,
    cross_kv,
    cross_out,
    mask_first,
    mask_second,
    truth,
    match,
):
    model_width = hits.shape[1]
    local_hits = hits.shape[0]
    query_count = queries.shape[0]
    hits_total = float(local_hits * lax.axis_size("phi") * lax.axis_size("query"))
    track_count = query_count * lax.axis_size("query") // 2
    normed = norm_rows(hits).astype(jnp.bfloat16)
    projected = jnp.dot(normed, enc_qkv, preferred_element_type=jnp.float32).astype(jnp.bfloat16)
    extended = extended_2(projected[:, model_width:], ((("phi", "query"), 0),), WIN // 2)
    block_rows = local_hits // 2
    span = extended.shape[0] - local_hits
    attended = jnp.concatenate(
        [
            window_attend(
                projected[b * block_rows : (b + 1) * block_rows, :model_width],
                extended[b * block_rows : b * block_rows + block_rows + span],
            )
            for b in range(2)
        ]
    )
    residual = hits.astype(jnp.float32) + jnp.dot(
        attended, enc_out, preferred_element_type=jnp.float32
    )
    upper = jax.nn.gelu(
        jnp.dot(
            norm_rows(residual).astype(jnp.bfloat16), enc_up, preferred_element_type=jnp.float32
        ),
        approximate=True,
    ).astype(jnp.bfloat16)
    encoded = (residual + jnp.dot(upper, enc_down, preferred_element_type=jnp.float32)).astype(
        jnp.bfloat16
    )
    local_kv = jnp.dot(
        norm_rows(encoded).astype(jnp.bfloat16), cross_kv, preferred_element_type=jnp.float32
    ).astype(jnp.bfloat16)
    shifted = truth + 1
    digits = jnp.stack([shifted // 256, shifted % 256], axis=1).astype(jnp.bfloat16)
    digits = jnp.pad(digits, ((0, 0), (0, 126)))
    gathered = lax.all_gather(
        jnp.concatenate([local_kv, encoded, digits], axis=1), "query", axis=0, tiled=True
    )
    group_kv = gathered[:, : 2 * model_width]
    group_hits = gathered[:, 2 * model_width : 3 * model_width]
    group_digits = gathered[:, 3 * model_width :].astype(jnp.int32)
    group_truth = group_digits[:, 0] * 256 + group_digits[:, 1] - 1
    query_proj = jnp.dot(queries, cross_q, preferred_element_type=jnp.float32).astype(jnp.bfloat16)
    head_size = model_width // HEADS
    group_count = group_kv.shape[0]
    query_heads = query_proj.reshape(query_count, HEADS, head_size)
    key_heads = group_kv[:, :model_width].reshape(group_count, HEADS, head_size)
    value_heads = group_kv[:, model_width:].reshape(group_count, HEADS, head_size)
    scores = jnp.einsum(
        "qhd,khd->hqk", query_heads, key_heads, preferred_element_type=jnp.float32
    ) * head_size ** (-0.5)
    local_max = jnp.max(scores, axis=-1)
    raised = jnp.exp(scores - local_max[..., None]).astype(jnp.bfloat16)
    local_total = jnp.sum(raised.astype(jnp.float32), axis=-1)
    local_mixed = jnp.einsum(
        "hqk,khd->qhd", raised, value_heads, preferred_element_type=jnp.float32
    ).reshape(query_count, model_width)
    packed = butterfly(
        pack_softmax(jnp.stack([local_max, local_total]), local_mixed),
        "phi",
        packed_combine,
        ordered=True,
    )
    (_, total), mixed = unpack_softmax(packed, query_count)
    context = scale_heads(mixed, 1.0 / total).astype(jnp.bfloat16)
    mixed_queries = queries.astype(jnp.float32) + jnp.dot(
        context, cross_out, preferred_element_type=jnp.float32
    )
    mask_hidden = jax.nn.relu(
        jnp.dot(
            norm_rows(mixed_queries).astype(jnp.bfloat16),
            mask_first,
            preferred_element_type=jnp.float32,
        )
    ).astype(jnp.bfloat16)
    mask_embed = jnp.dot(mask_hidden, mask_second, preferred_element_type=jnp.float32).astype(
        jnp.bfloat16
    )
    pair_hits = group_hits
    pair_digits = gathered[:, 3 * model_width : 3 * model_width + 2]
    for distance in (1, 2):
        pair_hits, pair_digits = partner_rows(pair_hits, pair_digits, distance)
    pair_digits = pair_digits.astype(jnp.int32)
    pair_truth = pair_digits[:, 0] * 256 + pair_digits[:, 1] - 1
    logits = lax.dot_general(
        mask_embed, pair_hits, (((1,), (1,)), ((), ())), preferred_element_type=jnp.float32
    ) * model_width ** (-0.5)
    sigma = jax.nn.sigmoid(logits)
    matched_flag = match < track_count
    matched = matched_flag.astype(jnp.float32)
    target = jnp.logical_and(match[:, None] == pair_truth[None, :], matched_flag[:, None]).astype(
        jnp.float32
    )
    intersection, predicted, truth_count = butterfly(
        jnp.stack(
            [jnp.sum(sigma * target, axis=1), jnp.sum(sigma, axis=1), jnp.sum(target, axis=1)]
        ),
        "phi",
        add_trees,
        distance=4,
    )
    mask_fill = predicted / hits_total
    coef = loss_coefficients(
        sigma, target, matched, intersection, predicted, truth_count, hits_total, model_width
    )
    mask_grad = narrow_butterfly(
        jnp.dot(coef, pair_hits, preferred_element_type=jnp.float32), "phi", distance=4
    )
    group_count = group_hits.shape[0]
    own_coef = lax.dynamic_slice_in_dim(
        coef, (lax.axis_index("phi") % 4) * group_count, group_count, axis=1
    )
    hit_grad = reduce_scatter_rows(
        lax.dot_general(
            own_coef, mask_embed, (((0,), (0,)), ((), ())), preferred_element_type=jnp.float32
        ),
        "query",
    )
    return (encoded, mask_embed, hit_grad, mask_grad, mask_fill)


def solution(mesh):
    return jax.shard_map(
        body,
        mesh=mesh,
        in_specs=(
            P(("event", "phi", "query"), None),
            P(),
            P(),
            P(),
            P(),
            P("query", None),
            P(),
            P(),
            P(),
            P(),
            P(),
            P(("event", "phi", "query")),
            P(("event", "query")),
        ),
        out_specs=(
            P(("event", "phi", "query"), None),
            P(("event", "query"), None),
            P(("event", "phi", "query"), None),
            P(("event", "query"), None),
            P(("event", "query")),
        ),
        check_vma=False,
    )
```

```python
import jax
import jax.numpy as jnp
from jax import lax
from jax.sharding import PartitionSpec as P

HEADS = 8
WIN = 512


def extended_2(block, sides, width):
    for axis, dim in sides:
        count = lax.axis_size(axis)
        forward = [(i, i + 1) for i in range(count - 1)]
        forward.append((count - 1, 0))
        backward = [(target, source) for source, target in forward]
        low = lax.ppermute(
            lax.slice_in_dim(block, block.shape[dim] - width, None, axis=dim), axis, forward
        )
        high = lax.ppermute(lax.slice_in_dim(block, 0, width, axis=dim), axis, backward)
        block = jnp.concatenate([low, block, high], axis=dim)
    return block


def partner_pairs(count, distance):
    return [(i, i ^ distance) for i in range(count)]


def butterfly(tree, axis, combine, ordered=False, distance=1):
    count = lax.axis_size(axis)
    assert count & (count - 1) == 0
    index = lax.axis_index(axis)
    while distance < count:
        other = lax.ppermute(tree, axis, partner_pairs(count, distance))
        if ordered:
            upper = (index // distance) % 2 == 1
            first = jax.tree.map(lambda a, b: jnp.where(upper, b, a), tree, other)
            second = jax.tree.map(lambda a, b: jnp.where(upper, a, b), tree, other)
            tree = combine(first, second)
        else:
            tree = combine(tree, other)
        distance *= 2
    return tree


def add_trees(a, b):
    return jax.tree.map(jnp.add, a, b)


def narrow_butterfly(block, axis, distance=1):
    count = lax.axis_size(axis)
    while distance < count:
        sent = block.astype(jnp.bfloat16)
        other = lax.ppermute(sent, axis, partner_pairs(count, distance))
        block = sent.astype(jnp.float32) + other.astype(jnp.float32)
        distance *= 2
    return block


def softmax_combine(a, b):
    (max_a, total_a), mixed_a = a
    (max_b, total_b), mixed_b = b
    mixed_a = mixed_a.astype(jnp.float32)
    mixed_b = mixed_b.astype(jnp.float32)
    top = jnp.maximum(max_a, max_b)
    factor_a = jnp.exp(max_a - top)
    factor_b = jnp.exp(max_b - top)
    return (
        jnp.stack([top, total_a * factor_a + total_b * factor_b]),
        (scale_heads(mixed_a, factor_a) + scale_heads(mixed_b, factor_b)).astype(jnp.bfloat16),
    )


def reduce_scatter_rows(block, axis):
    count = lax.axis_size(axis)
    assert count & (count - 1) == 0
    index = lax.axis_index(axis)
    distance = count // 2
    while distance >= 1:
        half = block.shape[0] // 2
        upper = (index // distance) % 2 == 1
        low, high = block[:half], block[half:]
        keep = jnp.where(upper, high, low)
        send = jnp.where(upper, low, high)
        block = keep + lax.ppermute(send, axis, partner_pairs(count, distance))
        distance //= 2
    return block


def partner_rows(hits, digits, distance):
    count_rows, width = hits.shape
    digit_rows = digits.T.reshape(2 * count_rows // width, width)
    payload = jnp.concatenate(
        [hits, jnp.pad(digit_rows, ((0, (-digit_rows.shape[0]) % 16), (0, 0)))]
    )
    other = lax.ppermute(payload, "phi", partner_pairs(lax.axis_size("phi"), distance))
    other_hits = other[:count_rows]
    other_digits = other[count_rows : count_rows + digit_rows.shape[0]].reshape(2, count_rows).T
    upper = (lax.axis_index("phi") // distance) % 2 == 1
    hits = jnp.where(
        upper, jnp.concatenate([other_hits, hits]), jnp.concatenate([hits, other_hits])
    )
    digits = jnp.where(
        upper, jnp.concatenate([other_digits, digits]), jnp.concatenate([digits, other_digits])
    )
    return hits, digits


def norm_rows(entries):
    widened = entries.astype(jnp.float32)
    centred = widened - jnp.mean(widened, axis=-1, keepdims=True)
    spread = jnp.mean(centred * centred, axis=-1, keepdims=True)
    return centred * lax.rsqrt(spread + 1e-05)


def window_attend(query_rows, kv_ext):
    row_count, model_width = query_rows.shape
    head_size = model_width // HEADS
    key_count = kv_ext.shape[0]
    key_span = key_count - row_count
    query_heads = query_rows.reshape(row_count, HEADS, head_size)
    key_heads = kv_ext[:, :model_width].reshape(key_count, HEADS, head_size)
    value_heads = kv_ext[:, model_width:].reshape(key_count, HEADS, head_size)
    scores = jnp.einsum(
        "qhd,khd->hqk", query_heads, key_heads, preferred_element_type=jnp.float32
    ) * head_size ** (-0.5)
    offset = lax.broadcasted_iota(jnp.int32, (row_count, key_count), 1) - lax.broadcasted_iota(
        jnp.int32, (row_count, key_count), 0
    )
    inside = jnp.logical_and(offset >= 0, offset < key_span)
    scores = jnp.where(inside[None, :, :], scores, -1e30)
    raised = jnp.exp(scores - jnp.max(scores, axis=-1, keepdims=True))
    weights = (raised / jnp.sum(raised, axis=-1, keepdims=True)).astype(jnp.bfloat16)
    attended = jnp.einsum("hqk,khd->qhd", weights, value_heads, preferred_element_type=jnp.float32)
    return attended.reshape(row_count, model_width).astype(jnp.bfloat16)


def split_heads(matrix):
    row_count, model_width = matrix.shape
    return matrix.reshape(row_count, HEADS, model_width // HEADS).transpose(1, 0, 2)


def head_partial(operands):
    query_head, key_head, value_head = operands
    scores = lax.dot_general(
        query_head, key_head, (((1,), (1,)), ((), ())), preferred_element_type=jnp.float32
    ) * query_head.shape[1] ** (-0.5)
    local_max = jnp.max(scores, axis=1)
    raised = jnp.exp(scores - local_max[:, None]).astype(jnp.bfloat16)
    total = jnp.sum(raised.astype(jnp.float32), axis=1)
    mixed = jnp.dot(raised, value_head, preferred_element_type=jnp.float32)
    return (local_max, total, mixed)


def scale_heads(mixed, factor):
    query_count, model_width = mixed.shape
    head_count = factor.shape[0]
    shaped = mixed.reshape(query_count, head_count, model_width // head_count)
    return (shaped * factor.T[:, :, None]).reshape(query_count, model_width)


def loss_coefficients(
    sigma, target, matched, intersection, predicted, truth_count, hits_total, model_width
):
    denom = predicted + truth_count + 1.0
    weight = matched * model_width ** (-0.5)
    slope = weight * hits_total * (-2.0 / denom)
    level = weight * hits_total * ((2.0 * intersection + 1.0) / (denom * denom))
    dice_part = (slope[:, None] * target + level[:, None]) * (sigma * (1.0 - sigma))
    return (weight[:, None] * (sigma - target) + dice_part).astype(jnp.bfloat16)


def body(
    hits,
    enc_qkv,
    enc_out,
    enc_up,
    enc_down,
    queries,
    cross_q,
    cross_kv,
    cross_out,
    mask_first,
    mask_second,
    truth,
    match,
):
    model_width = hits.shape[1]
    local_hits = hits.shape[0]
    query_count = queries.shape[0]
    hits_total = float(local_hits * lax.axis_size("phi") * lax.axis_size("query"))
    track_count = query_count * lax.axis_size("query") // 2
    normed = norm_rows(hits).astype(jnp.bfloat16)
    projected = jnp.dot(normed, enc_qkv, preferred_element_type=jnp.float32).astype(jnp.bfloat16)
    extended = extended_2(projected[:, model_width:], ((("phi", "query"), 0),), WIN // 2)
    block_rows = local_hits // 2
    span = extended.shape[0] - local_hits
    attended = jnp.concatenate(
        [
            window_attend(
                projected[b * block_rows : (b + 1) * block_rows, :model_width],
                extended[b * block_rows : b * block_rows + block_rows + span],
            )
            for b in range(2)
        ]
    )
    residual = hits.astype(jnp.float32) + jnp.dot(
        attended, enc_out, preferred_element_type=jnp.float32
    )
    upper = jax.nn.gelu(
        jnp.dot(
            norm_rows(residual).astype(jnp.bfloat16), enc_up, preferred_element_type=jnp.float32
        ),
        approximate=True,
    ).astype(jnp.bfloat16)
    encoded = (residual + jnp.dot(upper, enc_down, preferred_element_type=jnp.float32)).astype(
        jnp.bfloat16
    )
    local_kv = jnp.dot(
        norm_rows(encoded).astype(jnp.bfloat16), cross_kv, preferred_element_type=jnp.float32
    ).astype(jnp.bfloat16)
    shifted = truth + 1
    digits = jnp.stack([shifted // 256, shifted % 256], axis=1).astype(jnp.bfloat16)
    digits = jnp.pad(digits, ((0, 0), (0, 126)))
    gathered = lax.all_gather(
        jnp.concatenate([local_kv, encoded, digits], axis=1), "query", axis=0, tiled=True
    )
    group_kv = gathered[:, : 2 * model_width]
    group_hits = gathered[:, 2 * model_width : 3 * model_width]
    group_digits = gathered[:, 3 * model_width :].astype(jnp.int32)
    group_truth = group_digits[:, 0] * 256 + group_digits[:, 1] - 1
    query_proj = jnp.dot(queries, cross_q, preferred_element_type=jnp.float32).astype(jnp.bfloat16)
    head_size = model_width // HEADS
    group_count = group_kv.shape[0]
    query_heads = query_proj.reshape(query_count, HEADS, head_size)
    key_heads = group_kv[:, :model_width].reshape(group_count, HEADS, head_size)
    value_heads = group_kv[:, model_width:].reshape(group_count, HEADS, head_size)
    scores = jnp.einsum(
        "qhd,khd->hqk", query_heads, key_heads, preferred_element_type=jnp.float32
    ) * head_size ** (-0.5)
    local_max = jnp.max(scores, axis=-1)
    raised = jnp.exp(scores - local_max[..., None]).astype(jnp.bfloat16)
    local_total = jnp.sum(raised.astype(jnp.float32), axis=-1)
    local_mixed = jnp.einsum(
        "hqk,khd->qhd", raised, value_heads, preferred_element_type=jnp.float32
    ).reshape(query_count, model_width)
    (_, total), mixed = butterfly(
        (jnp.stack([local_max, local_total]), local_mixed.astype(jnp.bfloat16)),
        "phi",
        softmax_combine,
        ordered=True,
    )
    mixed = mixed.astype(jnp.float32)
    context = scale_heads(mixed, 1.0 / total).astype(jnp.bfloat16)
    mixed_queries = queries.astype(jnp.float32) + jnp.dot(
        context, cross_out, preferred_element_type=jnp.float32
    )
    mask_hidden = jax.nn.relu(
        jnp.dot(
            norm_rows(mixed_queries).astype(jnp.bfloat16),
            mask_first,
            preferred_element_type=jnp.float32,
        )
    ).astype(jnp.bfloat16)
    mask_embed = jnp.dot(mask_hidden, mask_second, preferred_element_type=jnp.float32).astype(
        jnp.bfloat16
    )
    pair_hits = group_hits
    pair_digits = gathered[:, 3 * model_width : 3 * model_width + 2]
    for distance in (1, 2):
        pair_hits, pair_digits = partner_rows(pair_hits, pair_digits, distance)
    pair_digits = pair_digits.astype(jnp.int32)
    pair_truth = pair_digits[:, 0] * 256 + pair_digits[:, 1] - 1
    logits = lax.dot_general(
        mask_embed, pair_hits, (((1,), (1,)), ((), ())), preferred_element_type=jnp.float32
    ) * model_width ** (-0.5)
    sigma = jax.nn.sigmoid(logits)
    matched_flag = match < track_count
    matched = matched_flag.astype(jnp.float32)
    target = jnp.logical_and(match[:, None] == pair_truth[None, :], matched_flag[:, None]).astype(
        jnp.float32
    )
    intersection, predicted, truth_count = butterfly(
        jnp.stack(
            [jnp.sum(sigma * target, axis=1), jnp.sum(sigma, axis=1), jnp.sum(target, axis=1)]
        ),
        "phi",
        add_trees,
        distance=4,
    )
    mask_fill = predicted / hits_total
    coef = loss_coefficients(
        sigma, target, matched, intersection, predicted, truth_count, hits_total, model_width
    )
    mask_grad = narrow_butterfly(
        jnp.dot(coef, pair_hits, preferred_element_type=jnp.float32), "phi", distance=4
    )
    group_count = group_hits.shape[0]
    own_coef = lax.dynamic_slice_in_dim(
        coef, (lax.axis_index("phi") % 4) * group_count, group_count, axis=1
    )
    hit_grad = reduce_scatter_rows(
        lax.dot_general(
            own_coef, mask_embed, (((0,), (0,)), ((), ())), preferred_element_type=jnp.float32
        ),
        "query",
    )
    return (encoded, mask_embed, hit_grad, mask_grad, mask_fill)


def solution(mesh):
    return jax.shard_map(
        body,
        mesh=mesh,
        in_specs=(
            P(("event", "phi", "query"), None),
            P(),
            P(),
            P(),
            P(),
            P("query", None),
            P(),
            P(),
            P(),
            P(),
            P(),
            P(("event", "phi", "query")),
            P(("event", "query")),
        ),
        out_specs=(
            P(("event", "phi", "query"), None),
            P(("event", "query"), None),
            P(("event", "phi", "query"), None),
            P(("event", "query"), None),
            P(("event", "query")),
        ),
        check_vma=False,
    )
```

```python
import jax
import jax.numpy as jnp
from jax import lax
from jax.sharding import PartitionSpec as P

HEADS = 8
WIN = 512


def extended_2(block, sides, width):
    for axis, dim in sides:
        count = lax.axis_size(axis)
        forward = [(i, i + 1) for i in range(count - 1)]
        forward.append((count - 1, 0))
        backward = [(target, source) for source, target in forward]
        low = lax.ppermute(
            lax.slice_in_dim(block, block.shape[dim] - width, None, axis=dim), axis, forward
        )
        high = lax.ppermute(lax.slice_in_dim(block, 0, width, axis=dim), axis, backward)
        block = jnp.concatenate([low, block, high], axis=dim)
    return block


def partner_pairs(count, distance):
    return [(i, i ^ distance) for i in range(count)]


def butterfly(tree, axis, combine, ordered=False, distance=1, order=None):
    count = lax.axis_size(axis)
    assert count & (count - 1) == 0
    index = lax.axis_index(axis)
    distances = []
    while distance < count:
        distances.append(distance)
        distance *= 2
    if order is not None and len(distances) >= 2:
        distances[0], distances[1] = distances[1], distances[0]
    for distance in distances:
        other = lax.ppermute(tree, axis, partner_pairs(count, distance))
        if ordered:
            upper = (index // distance) % 2 == 1
            first = jax.tree.map(lambda a, b: jnp.where(upper, b, a), tree, other)
            second = jax.tree.map(lambda a, b: jnp.where(upper, a, b), tree, other)
            tree = combine(first, second)
        else:
            tree = combine(tree, other)
    return tree


def add_trees(a, b):
    return jax.tree.map(jnp.add, a, b)


def narrow_butterfly(block, axis, distance=1):
    count = lax.axis_size(axis)
    while distance < count:
        sent = block.astype(jnp.bfloat16)
        other = lax.ppermute(sent, axis, partner_pairs(count, distance))
        block = sent.astype(jnp.float32) + other.astype(jnp.float32)
        distance *= 2
    return block


def softmax_combine(a, b):
    (max_a, total_a), mixed_a = a
    (max_b, total_b), mixed_b = b
    mixed_a = mixed_a.astype(jnp.float32)
    mixed_b = mixed_b.astype(jnp.float32)
    top = jnp.maximum(max_a, max_b)
    factor_a = jnp.exp(max_a - top)
    factor_b = jnp.exp(max_b - top)
    return (
        jnp.stack([top, total_a * factor_a + total_b * factor_b]),
        (scale_heads(mixed_a, factor_a) + scale_heads(mixed_b, factor_b)).astype(jnp.bfloat16),
    )


def reduce_scatter_rows(block, axis):
    count = lax.axis_size(axis)
    assert count & (count - 1) == 0
    index = lax.axis_index(axis)
    distance = count // 2
    while distance >= 1:
        half = block.shape[0] // 2
        upper = (index // distance) % 2 == 1
        low, high = block[:half], block[half:]
        keep = jnp.where(upper, high, low)
        send = jnp.where(upper, low, high)
        block = keep + lax.ppermute(send, axis, partner_pairs(count, distance))
        distance //= 2
    return block


def partner_rows(hits, digits, distance):
    count_rows, width = hits.shape
    digit_rows = digits.T.reshape(2 * count_rows // width, width)
    payload = jnp.concatenate(
        [hits, jnp.pad(digit_rows, ((0, (-digit_rows.shape[0]) % 16), (0, 0)))]
    )
    other = lax.ppermute(payload, "phi", partner_pairs(lax.axis_size("phi"), distance))
    other_hits = other[:count_rows]
    other_digits = other[count_rows : count_rows + digit_rows.shape[0]].reshape(2, count_rows).T
    upper = (lax.axis_index("phi") // distance) % 2 == 1
    hits = jnp.where(
        upper, jnp.concatenate([other_hits, hits]), jnp.concatenate([hits, other_hits])
    )
    digits = jnp.where(
        upper, jnp.concatenate([other_digits, digits]), jnp.concatenate([digits, other_digits])
    )
    return hits, digits


def norm_rows(entries):
    widened = entries.astype(jnp.float32)
    centred = widened - jnp.mean(widened, axis=-1, keepdims=True)
    spread = jnp.mean(centred * centred, axis=-1, keepdims=True)
    return centred * lax.rsqrt(spread + 1e-05)


def window_attend(query_rows, kv_ext):
    row_count, model_width = query_rows.shape
    head_size = model_width // HEADS
    key_count = kv_ext.shape[0]
    key_span = key_count - row_count
    query_heads = query_rows.reshape(row_count, HEADS, head_size)
    key_heads = kv_ext[:, :model_width].reshape(key_count, HEADS, head_size)
    value_heads = kv_ext[:, model_width:].reshape(key_count, HEADS, head_size)
    scores = jnp.einsum(
        "qhd,khd->hqk", query_heads, key_heads, preferred_element_type=jnp.float32
    ) * head_size ** (-0.5)
    offset = lax.broadcasted_iota(jnp.int32, (row_count, key_count), 1) - lax.broadcasted_iota(
        jnp.int32, (row_count, key_count), 0
    )
    inside = jnp.logical_and(offset >= 0, offset < key_span)
    scores = jnp.where(inside[None, :, :], scores, -1e30)
    raised = jnp.exp(scores - jnp.max(scores, axis=-1, keepdims=True))
    weights = (raised / jnp.sum(raised, axis=-1, keepdims=True)).astype(jnp.bfloat16)
    attended = jnp.einsum("hqk,khd->qhd", weights, value_heads, preferred_element_type=jnp.float32)
    return attended.reshape(row_count, model_width).astype(jnp.bfloat16)


def split_heads(matrix):
    row_count, model_width = matrix.shape
    return matrix.reshape(row_count, HEADS, model_width // HEADS).transpose(1, 0, 2)


def head_partial(operands):
    query_head, key_head, value_head = operands
    scores = lax.dot_general(
        query_head, key_head, (((1,), (1,)), ((), ())), preferred_element_type=jnp.float32
    ) * query_head.shape[1] ** (-0.5)
    local_max = jnp.max(scores, axis=1)
    raised = jnp.exp(scores - local_max[:, None]).astype(jnp.bfloat16)
    total = jnp.sum(raised.astype(jnp.float32), axis=1)
    mixed = jnp.dot(raised, value_head, preferred_element_type=jnp.float32)
    return (local_max, total, mixed)


def scale_heads(mixed, factor):
    query_count, model_width = mixed.shape
    head_count = factor.shape[0]
    shaped = mixed.reshape(query_count, head_count, model_width // head_count)
    return (shaped * factor.T[:, :, None]).reshape(query_count, model_width)


def loss_coefficients(
    sigma, target, matched, intersection, predicted, truth_count, hits_total, model_width
):
    denom = predicted + truth_count + 1.0
    slope = -2.0 / denom
    level = (2.0 * intersection + 1.0) / (denom * denom)
    dice_part = hits_total * (slope[:, None] * target + level[:, None]) * sigma * (1.0 - sigma)
    return (matched[:, None] * (sigma - target + dice_part) * model_width ** (-0.5)).astype(
        jnp.bfloat16
    )


def body(
    hits,
    enc_qkv,
    enc_out,
    enc_up,
    enc_down,
    queries,
    cross_q,
    cross_kv,
    cross_out,
    mask_first,
    mask_second,
    truth,
    match,
):
    model_width = hits.shape[1]
    local_hits = hits.shape[0]
    query_count = queries.shape[0]
    hits_total = float(local_hits * lax.axis_size("phi") * lax.axis_size("query"))
    track_count = query_count * lax.axis_size("query") // 2
    normed = norm_rows(hits).astype(jnp.bfloat16)
    projected = jnp.dot(normed, enc_qkv, preferred_element_type=jnp.float32).astype(jnp.bfloat16)
    extended = extended_2(projected[:, model_width:], ((("phi", "query"), 0),), WIN // 2)
    block_rows = local_hits // 2
    span = extended.shape[0] - local_hits
    attended = jnp.concatenate(
        [
            window_attend(
                projected[b * block_rows : (b + 1) * block_rows, :model_width],
                extended[b * block_rows : b * block_rows + block_rows + span],
            )
            for b in range(2)
        ]
    )
    residual = hits.astype(jnp.float32) + jnp.dot(
        attended, enc_out, preferred_element_type=jnp.float32
    )
    upper = jax.nn.gelu(
        jnp.dot(
            norm_rows(residual).astype(jnp.bfloat16), enc_up, preferred_element_type=jnp.float32
        ),
        approximate=True,
    ).astype(jnp.bfloat16)
    encoded = (residual + jnp.dot(upper, enc_down, preferred_element_type=jnp.float32)).astype(
        jnp.bfloat16
    )
    local_kv = jnp.dot(
        norm_rows(encoded).astype(jnp.bfloat16), cross_kv, preferred_element_type=jnp.float32
    ).astype(jnp.bfloat16)
    shifted = truth + 1
    digits = jnp.stack([shifted // 256, shifted % 256], axis=1).astype(jnp.bfloat16)
    digits = jnp.pad(digits, ((0, 0), (0, 126)))
    gathered = lax.all_gather(
        jnp.concatenate([local_kv, encoded, digits], axis=1), "query", axis=0, tiled=True
    )
    group_kv = gathered[:, : 2 * model_width]
    group_hits = gathered[:, 2 * model_width : 3 * model_width]
    group_digits = gathered[:, 3 * model_width :].astype(jnp.int32)
    group_truth = group_digits[:, 0] * 256 + group_digits[:, 1] - 1
    query_proj = jnp.dot(queries, cross_q, preferred_element_type=jnp.float32).astype(jnp.bfloat16)
    head_size = model_width // HEADS
    group_count = group_kv.shape[0]
    query_heads = query_proj.reshape(query_count, HEADS, head_size)
    key_heads = group_kv[:, :model_width].reshape(group_count, HEADS, head_size)
    value_heads = group_kv[:, model_width:].reshape(group_count, HEADS, head_size)
    scores = jnp.einsum(
        "qhd,khd->hqk", query_heads, key_heads, preferred_element_type=jnp.float32
    ) * head_size ** (-0.5)
    local_max = jnp.max(scores, axis=-1)
    raised = jnp.exp(scores - local_max[..., None]).astype(jnp.bfloat16)
    local_total = jnp.sum(raised.astype(jnp.float32), axis=-1)
    local_mixed = jnp.einsum(
        "hqk,khd->qhd", raised, value_heads, preferred_element_type=jnp.float32
    ).reshape(query_count, model_width)
    (_, total), mixed = butterfly(
        (jnp.stack([local_max, local_total]), local_mixed.astype(jnp.bfloat16)),
        "phi",
        softmax_combine,
        ordered=True,
        order="near_first",
    )
    mixed = mixed.astype(jnp.float32)
    context = scale_heads(mixed, 1.0 / total).astype(jnp.bfloat16)
    mixed_queries = queries.astype(jnp.float32) + jnp.dot(
        context, cross_out, preferred_element_type=jnp.float32
    )
    mask_hidden = jax.nn.relu(
        jnp.dot(
            norm_rows(mixed_queries).astype(jnp.bfloat16),
            mask_first,
            preferred_element_type=jnp.float32,
        )
    ).astype(jnp.bfloat16)
    mask_embed = jnp.dot(mask_hidden, mask_second, preferred_element_type=jnp.float32).astype(
        jnp.bfloat16
    )
    pair_hits = group_hits
    pair_digits = gathered[:, 3 * model_width : 3 * model_width + 2]
    for distance in (1, 2):
        pair_hits, pair_digits = partner_rows(pair_hits, pair_digits, distance)
    pair_digits = pair_digits.astype(jnp.int32)
    pair_truth = pair_digits[:, 0] * 256 + pair_digits[:, 1] - 1
    logits = lax.dot_general(
        mask_embed, pair_hits, (((1,), (1,)), ((), ())), preferred_element_type=jnp.float32
    ) * model_width ** (-0.5)
    sigma = jax.nn.sigmoid(logits)
    matched_flag = match < track_count
    matched = matched_flag.astype(jnp.float32)
    target = jnp.logical_and(match[:, None] == pair_truth[None, :], matched_flag[:, None]).astype(
        jnp.float32
    )
    intersection, predicted, truth_count = butterfly(
        jnp.stack(
            [jnp.sum(sigma * target, axis=1), jnp.sum(sigma, axis=1), jnp.sum(target, axis=1)]
        ),
        "phi",
        add_trees,
        distance=4,
    )
    mask_fill = predicted / hits_total
    coef = loss_coefficients(
        sigma, target, matched, intersection, predicted, truth_count, hits_total, model_width
    )
    mask_grad = narrow_butterfly(
        jnp.dot(coef, pair_hits, preferred_element_type=jnp.float32), "phi", distance=4
    )
    group_count = group_hits.shape[0]
    own_coef = lax.dynamic_slice_in_dim(
        coef, (lax.axis_index("phi") % 4) * group_count, group_count, axis=1
    )
    hit_grad = reduce_scatter_rows(
        lax.dot_general(
            own_coef, mask_embed, (((0,), (0,)), ((), ())), preferred_element_type=jnp.float32
        ),
        "query",
    )
    return (encoded, mask_embed, hit_grad, mask_grad, mask_fill)


def solution(mesh):
    return jax.shard_map(
        body,
        mesh=mesh,
        in_specs=(
            P(("event", "phi", "query"), None),
            P(),
            P(),
            P(),
            P(),
            P("query", None),
            P(),
            P(),
            P(),
            P(),
            P(),
            P(("event", "phi", "query")),
            P(("event", "query")),
        ),
        out_specs=(
            P(("event", "phi", "query"), None),
            P(("event", "query"), None),
            P(("event", "phi", "query"), None),
            P(("event", "query"), None),
            P(("event", "query")),
        ),
        check_vma=False,
    )
```

```python
import jax
import jax.numpy as jnp
from jax import lax
from jax.sharding import PartitionSpec as P

HEADS = 8
WIN = 512


def extended_2(block, sides, width):
    for axis, dim in sides:
        count = lax.axis_size(axis)
        forward = [(i, i + 1) for i in range(count - 1)]
        forward.append((count - 1, 0))
        backward = [(target, source) for source, target in forward]
        low = lax.ppermute(
            lax.slice_in_dim(block, block.shape[dim] - width, None, axis=dim), axis, forward
        )
        high = lax.ppermute(lax.slice_in_dim(block, 0, width, axis=dim), axis, backward)
        block = jnp.concatenate([low, block, high], axis=dim)
    return block


def partner_pairs(count, distance):
    return [(i, i ^ distance) for i in range(count)]


def butterfly(tree, axis, combine, ordered=False, distance=1, order=None):
    count = lax.axis_size(axis)
    assert count & (count - 1) == 0
    index = lax.axis_index(axis)
    distances = []
    while distance < count:
        distances.append(distance)
        distance *= 2
    if order is not None and len(distances) >= 2:
        distances = distances[1:] + distances[:1]
    for distance in distances:
        other = lax.ppermute(tree, axis, partner_pairs(count, distance))
        if ordered:
            upper = (index // distance) % 2 == 1
            first = jax.tree.map(lambda a, b: jnp.where(upper, b, a), tree, other)
            second = jax.tree.map(lambda a, b: jnp.where(upper, a, b), tree, other)
            tree = combine(first, second)
        else:
            tree = combine(tree, other)
    return tree


def add_trees(a, b):
    return jax.tree.map(jnp.add, a, b)


def narrow_butterfly(block, axis, distance=1):
    count = lax.axis_size(axis)
    while distance < count:
        sent = block.astype(jnp.bfloat16)
        other = lax.ppermute(sent, axis, partner_pairs(count, distance))
        block = sent.astype(jnp.float32) + other.astype(jnp.float32)
        distance *= 2
    return block


def softmax_combine(a, b):
    (max_a, total_a), mixed_a = a
    (max_b, total_b), mixed_b = b
    mixed_a = mixed_a.astype(jnp.float32)
    mixed_b = mixed_b.astype(jnp.float32)
    top = jnp.maximum(max_a, max_b)
    factor_a = jnp.exp(max_a - top)
    factor_b = jnp.exp(max_b - top)
    return (
        jnp.stack([top, total_a * factor_a + total_b * factor_b]),
        (scale_heads(mixed_a, factor_a) + scale_heads(mixed_b, factor_b)).astype(jnp.bfloat16),
    )


def reduce_scatter_rows(block, axis):
    count = lax.axis_size(axis)
    assert count & (count - 1) == 0
    index = lax.axis_index(axis)
    distance = count // 2
    while distance >= 1:
        half = block.shape[0] // 2
        upper = (index // distance) % 2 == 1
        low, high = block[:half], block[half:]
        keep = jnp.where(upper, high, low)
        send = jnp.where(upper, low, high)
        block = keep + lax.ppermute(send, axis, partner_pairs(count, distance))
        distance //= 2
    return block


def partner_rows(hits, digits, distance):
    count_rows, width = hits.shape
    digit_rows = digits.T.reshape(2 * count_rows // width, width)
    payload = jnp.concatenate(
        [hits, jnp.pad(digit_rows, ((0, (-digit_rows.shape[0]) % 16), (0, 0)))]
    )
    other = lax.ppermute(payload, "phi", partner_pairs(lax.axis_size("phi"), distance))
    other_hits = other[:count_rows]
    other_digits = other[count_rows : count_rows + digit_rows.shape[0]].reshape(2, count_rows).T
    upper = (lax.axis_index("phi") // distance) % 2 == 1
    hits = jnp.where(
        upper, jnp.concatenate([other_hits, hits]), jnp.concatenate([hits, other_hits])
    )
    digits = jnp.where(
        upper, jnp.concatenate([other_digits, digits]), jnp.concatenate([digits, other_digits])
    )
    return hits, digits


def norm_rows(entries):
    widened = entries.astype(jnp.float32)
    centred = widened - jnp.mean(widened, axis=-1, keepdims=True)
    spread = jnp.mean(centred * centred, axis=-1, keepdims=True)
    return centred * lax.rsqrt(spread + 1e-05)


def window_attend(query_rows, kv_ext):
    row_count, model_width = query_rows.shape
    head_size = model_width // HEADS
    key_count = kv_ext.shape[0]
    key_span = key_count - row_count
    query_heads = query_rows.reshape(row_count, HEADS, head_size)
    key_heads = kv_ext[:, :model_width].reshape(key_count, HEADS, head_size)
    value_heads = kv_ext[:, model_width:].reshape(key_count, HEADS, head_size)
    scores = jnp.einsum(
        "qhd,khd->hqk", query_heads, key_heads, preferred_element_type=jnp.float32
    ) * head_size ** (-0.5)
    offset = lax.broadcasted_iota(jnp.int32, (row_count, key_count), 1) - lax.broadcasted_iota(
        jnp.int32, (row_count, key_count), 0
    )
    inside = jnp.logical_and(offset >= 0, offset < key_span)
    scores = jnp.where(inside[None, :, :], scores, -1e30)
    raised = jnp.exp(scores - jnp.max(scores, axis=-1, keepdims=True))
    weights = (raised / jnp.sum(raised, axis=-1, keepdims=True)).astype(jnp.bfloat16)
    attended = jnp.einsum("hqk,khd->qhd", weights, value_heads, preferred_element_type=jnp.float32)
    return attended.reshape(row_count, model_width).astype(jnp.bfloat16)


def split_heads(matrix):
    row_count, model_width = matrix.shape
    return matrix.reshape(row_count, HEADS, model_width // HEADS).transpose(1, 0, 2)


def head_partial(operands):
    query_head, key_head, value_head = operands
    scores = lax.dot_general(
        query_head, key_head, (((1,), (1,)), ((), ())), preferred_element_type=jnp.float32
    ) * query_head.shape[1] ** (-0.5)
    local_max = jnp.max(scores, axis=1)
    raised = jnp.exp(scores - local_max[:, None]).astype(jnp.bfloat16)
    total = jnp.sum(raised.astype(jnp.float32), axis=1)
    mixed = jnp.dot(raised, value_head, preferred_element_type=jnp.float32)
    return (local_max, total, mixed)


def scale_heads(mixed, factor):
    query_count, model_width = mixed.shape
    head_count = factor.shape[0]
    shaped = mixed.reshape(query_count, head_count, model_width // head_count)
    return (shaped * factor.T[:, :, None]).reshape(query_count, model_width)


def loss_coefficients(
    sigma, target, matched, intersection, predicted, truth_count, hits_total, model_width
):
    denom = predicted + truth_count + 1.0
    slope = -2.0 / denom
    level = (2.0 * intersection + 1.0) / (denom * denom)
    dice_part = hits_total * (slope[:, None] * target + level[:, None]) * sigma * (1.0 - sigma)
    return (matched[:, None] * (sigma - target + dice_part) * model_width ** (-0.5)).astype(
        jnp.bfloat16
    )


def body(
    hits,
    enc_qkv,
    enc_out,
    enc_up,
    enc_down,
    queries,
    cross_q,
    cross_kv,
    cross_out,
    mask_first,
    mask_second,
    truth,
    match,
):
    model_width = hits.shape[1]
    local_hits = hits.shape[0]
    query_count = queries.shape[0]
    hits_total = float(local_hits * lax.axis_size("phi") * lax.axis_size("query"))
    track_count = query_count * lax.axis_size("query") // 2
    normed = norm_rows(hits).astype(jnp.bfloat16)
    projected = jnp.dot(normed, enc_qkv, preferred_element_type=jnp.float32).astype(jnp.bfloat16)
    extended = extended_2(projected[:, model_width:], ((("phi", "query"), 0),), WIN // 2)
    block_rows = local_hits // 2
    span = extended.shape[0] - local_hits
    attended = jnp.concatenate(
        [
            window_attend(
                projected[b * block_rows : (b + 1) * block_rows, :model_width],
                extended[b * block_rows : b * block_rows + block_rows + span],
            )
            for b in range(2)
        ]
    )
    residual = hits.astype(jnp.float32) + jnp.dot(
        attended, enc_out, preferred_element_type=jnp.float32
    )
    upper = jax.nn.gelu(
        jnp.dot(
            norm_rows(residual).astype(jnp.bfloat16), enc_up, preferred_element_type=jnp.float32
        ),
        approximate=True,
    ).astype(jnp.bfloat16)
    encoded = (residual + jnp.dot(upper, enc_down, preferred_element_type=jnp.float32)).astype(
        jnp.bfloat16
    )
    local_kv = jnp.dot(
        norm_rows(encoded).astype(jnp.bfloat16), cross_kv, preferred_element_type=jnp.float32
    ).astype(jnp.bfloat16)
    shifted = truth + 1
    digits = jnp.stack([shifted // 256, shifted % 256], axis=1).astype(jnp.bfloat16)
    digits = jnp.pad(digits, ((0, 0), (0, 126)))
    gathered = lax.all_gather(
        jnp.concatenate([local_kv, encoded, digits], axis=1), "query", axis=0, tiled=True
    )
    group_kv = gathered[:, : 2 * model_width]
    group_hits = gathered[:, 2 * model_width : 3 * model_width]
    group_digits = gathered[:, 3 * model_width :].astype(jnp.int32)
    group_truth = group_digits[:, 0] * 256 + group_digits[:, 1] - 1
    query_proj = jnp.dot(queries, cross_q, preferred_element_type=jnp.float32).astype(jnp.bfloat16)
    head_size = model_width // HEADS
    group_count = group_kv.shape[0]
    query_heads = query_proj.reshape(query_count, HEADS, head_size)
    key_heads = group_kv[:, :model_width].reshape(group_count, HEADS, head_size)
    value_heads = group_kv[:, model_width:].reshape(group_count, HEADS, head_size)
    scores = jnp.einsum(
        "qhd,khd->hqk", query_heads, key_heads, preferred_element_type=jnp.float32
    ) * head_size ** (-0.5)
    local_max = jnp.max(scores, axis=-1)
    raised = jnp.exp(scores - local_max[..., None]).astype(jnp.bfloat16)
    local_total = jnp.sum(raised.astype(jnp.float32), axis=-1)
    local_mixed = jnp.einsum(
        "hqk,khd->qhd", raised, value_heads, preferred_element_type=jnp.float32
    ).reshape(query_count, model_width)
    (_, total), mixed = butterfly(
        (jnp.stack([local_max, local_total]), local_mixed.astype(jnp.bfloat16)),
        "phi",
        softmax_combine,
        ordered=True,
        order="near_first",
    )
    mixed = mixed.astype(jnp.float32)
    context = scale_heads(mixed, 1.0 / total).astype(jnp.bfloat16)
    mixed_queries = queries.astype(jnp.float32) + jnp.dot(
        context, cross_out, preferred_element_type=jnp.float32
    )
    mask_hidden = jax.nn.relu(
        jnp.dot(
            norm_rows(mixed_queries).astype(jnp.bfloat16),
            mask_first,
            preferred_element_type=jnp.float32,
        )
    ).astype(jnp.bfloat16)
    mask_embed = jnp.dot(mask_hidden, mask_second, preferred_element_type=jnp.float32).astype(
        jnp.bfloat16
    )
    pair_hits = group_hits
    pair_digits = gathered[:, 3 * model_width : 3 * model_width + 2]
    for distance in (1, 2):
        pair_hits, pair_digits = partner_rows(pair_hits, pair_digits, distance)
    pair_digits = pair_digits.astype(jnp.int32)
    pair_truth = pair_digits[:, 0] * 256 + pair_digits[:, 1] - 1
    logits = lax.dot_general(
        mask_embed, pair_hits, (((1,), (1,)), ((), ())), preferred_element_type=jnp.float32
    ) * model_width ** (-0.5)
    sigma = jax.nn.sigmoid(logits)
    matched_flag = match < track_count
    matched = matched_flag.astype(jnp.float32)
    target = jnp.logical_and(match[:, None] == pair_truth[None, :], matched_flag[:, None]).astype(
        jnp.float32
    )
    intersection, predicted, truth_count = butterfly(
        jnp.stack(
            [jnp.sum(sigma * target, axis=1), jnp.sum(sigma, axis=1), jnp.sum(target, axis=1)]
        ),
        "phi",
        add_trees,
        distance=4,
    )
    mask_fill = predicted / hits_total
    coef = loss_coefficients(
        sigma, target, matched, intersection, predicted, truth_count, hits_total, model_width
    )
    mask_grad = narrow_butterfly(
        jnp.dot(coef, pair_hits, preferred_element_type=jnp.float32), "phi", distance=4
    )
    group_count = group_hits.shape[0]
    own_coef = lax.dynamic_slice_in_dim(
        coef, (lax.axis_index("phi") % 4) * group_count, group_count, axis=1
    )
    hit_grad = reduce_scatter_rows(
        lax.dot_general(
            own_coef, mask_embed, (((0,), (0,)), ((), ())), preferred_element_type=jnp.float32
        ),
        "query",
    )
    return (encoded, mask_embed, hit_grad, mask_grad, mask_fill)


def solution(mesh):
    return jax.shard_map(
        body,
        mesh=mesh,
        in_specs=(
            P(("event", "phi", "query"), None),
            P(),
            P(),
            P(),
            P(),
            P("query", None),
            P(),
            P(),
            P(),
            P(),
            P(),
            P(("event", "phi", "query")),
            P(("event", "query")),
        ),
        out_specs=(
            P(("event", "phi", "query"), None),
            P(("event", "query"), None),
            P(("event", "phi", "query"), None),
            P(("event", "query"), None),
            P(("event", "query")),
        ),
        check_vma=False,
    )
```

```python
import jax
import jax.numpy as jnp
from jax import lax
from jax.sharding import PartitionSpec as P

HEADS = 8
WIN = 512


def extended_2(block, sides, width):
    for axis, dim in sides:
        count = lax.axis_size(axis)
        forward = [(i, i + 1) for i in range(count - 1)]
        forward.append((count - 1, 0))
        backward = [(target, source) for source, target in forward]
        low = lax.ppermute(
            lax.slice_in_dim(block, block.shape[dim] - width, None, axis=dim), axis, forward
        )
        high = lax.ppermute(lax.slice_in_dim(block, 0, width, axis=dim), axis, backward)
        block = jnp.concatenate([low, block, high], axis=dim)
    return block


def partner_pairs(count, distance):
    return [(i, i ^ distance) for i in range(count)]


def butterfly(tree, axis, combine, ordered=False, distance=1, order=None):
    count = lax.axis_size(axis)
    assert count & (count - 1) == 0
    index = lax.axis_index(axis)
    distances = []
    while distance < count:
        distances.append(distance)
        distance *= 2
    if order is not None and len(distances) >= 2:
        distances[0], distances[1] = distances[1], distances[0]
    for distance in distances:
        other = lax.ppermute(tree, axis, partner_pairs(count, distance))
        if ordered:
            upper = (index // distance) % 2 == 1
            first = jax.tree.map(lambda a, b: jnp.where(upper, b, a), tree, other)
            second = jax.tree.map(lambda a, b: jnp.where(upper, a, b), tree, other)
            tree = combine(first, second)
        else:
            tree = combine(tree, other)
    return tree


def add_trees(a, b):
    return jax.tree.map(jnp.add, a, b)


def narrow_butterfly(block, axis, distance=1):
    count = lax.axis_size(axis)
    while distance < count:
        sent = block.astype(jnp.bfloat16)
        other = lax.ppermute(sent, axis, partner_pairs(count, distance))
        block = sent.astype(jnp.float32) + other.astype(jnp.float32)
        distance *= 2
    return block


def softmax_combine(a, b):
    (max_a, total_a), mixed_a = a
    (max_b, total_b), mixed_b = b
    mixed_a = mixed_a.astype(jnp.float32)
    mixed_b = mixed_b.astype(jnp.float32)
    top = jnp.maximum(max_a, max_b)
    factor_a = jnp.exp(max_a - top)
    factor_b = jnp.exp(max_b - top)
    return (
        jnp.stack([top, total_a * factor_a + total_b * factor_b]),
        (scale_heads(mixed_a, factor_a) + scale_heads(mixed_b, factor_b)).astype(jnp.bfloat16),
    )


def reduce_scatter_rows(block, axis):
    count = lax.axis_size(axis)
    assert count & (count - 1) == 0
    index = lax.axis_index(axis)
    distance = count // 2
    while distance >= 1:
        half = block.shape[0] // 2
        upper = (index // distance) % 2 == 1
        low, high = block[:half], block[half:]
        keep = jnp.where(upper, high, low)
        send = jnp.where(upper, low, high)
        block = keep + lax.ppermute(send, axis, partner_pairs(count, distance))
        distance //= 2
    return block


def partner_rows(hits, digits, distance):
    count_rows, width = hits.shape
    digit_rows = digits.T.reshape(2 * count_rows // width, width)
    payload = jnp.concatenate(
        [hits, jnp.pad(digit_rows, ((0, (-digit_rows.shape[0]) % 16), (0, 0)))]
    )
    other = lax.ppermute(payload, "phi", partner_pairs(lax.axis_size("phi"), distance))
    other_hits = other[:count_rows]
    other_digits = other[count_rows : count_rows + digit_rows.shape[0]].reshape(2, count_rows).T
    upper = (lax.axis_index("phi") // distance) % 2 == 1
    hits = jnp.where(
        upper, jnp.concatenate([other_hits, hits]), jnp.concatenate([hits, other_hits])
    )
    digits = jnp.where(
        upper, jnp.concatenate([other_digits, digits]), jnp.concatenate([digits, other_digits])
    )
    return hits, digits


def fetch_rows(hits, digits, mask):
    count_rows, width = hits.shape
    digit_rows = digits.T.reshape(2 * count_rows // width, width)
    payload = jnp.concatenate(
        [hits, jnp.pad(digit_rows, ((0, (-digit_rows.shape[0]) % 16), (0, 0)))]
    )
    count = lax.axis_size("phi")
    other = lax.ppermute(payload, "phi", [(i, i ^ mask) for i in range(count)])
    other_digits = other[count_rows : count_rows + digit_rows.shape[0]].reshape(2, count_rows).T
    return other[:count_rows], other_digits


def norm_rows(entries):
    widened = entries.astype(jnp.float32)
    centred = widened - jnp.mean(widened, axis=-1, keepdims=True)
    spread = jnp.mean(centred * centred, axis=-1, keepdims=True)
    return centred * lax.rsqrt(spread + 1e-05)


def window_attend(query_rows, kv_ext):
    row_count, model_width = query_rows.shape
    head_size = model_width // HEADS
    key_count = kv_ext.shape[0]
    key_span = key_count - row_count
    query_heads = query_rows.reshape(row_count, HEADS, head_size)
    key_heads = kv_ext[:, :model_width].reshape(key_count, HEADS, head_size)
    value_heads = kv_ext[:, model_width:].reshape(key_count, HEADS, head_size)
    scores = jnp.einsum(
        "qhd,khd->hqk", query_heads, key_heads, preferred_element_type=jnp.float32
    ) * head_size ** (-0.5)
    offset = lax.broadcasted_iota(jnp.int32, (row_count, key_count), 1) - lax.broadcasted_iota(
        jnp.int32, (row_count, key_count), 0
    )
    inside = jnp.logical_and(offset >= 0, offset < key_span)
    scores = jnp.where(inside[None, :, :], scores, -1e30)
    raised = jnp.exp(scores - jnp.max(scores, axis=-1, keepdims=True))
    weights = (raised / jnp.sum(raised, axis=-1, keepdims=True)).astype(jnp.bfloat16)
    attended = jnp.einsum("hqk,khd->qhd", weights, value_heads, preferred_element_type=jnp.float32)
    return attended.reshape(row_count, model_width).astype(jnp.bfloat16)


def split_heads(matrix):
    row_count, model_width = matrix.shape
    return matrix.reshape(row_count, HEADS, model_width // HEADS).transpose(1, 0, 2)


def head_partial(operands):
    query_head, key_head, value_head = operands
    scores = lax.dot_general(
        query_head, key_head, (((1,), (1,)), ((), ())), preferred_element_type=jnp.float32
    ) * query_head.shape[1] ** (-0.5)
    local_max = jnp.max(scores, axis=1)
    raised = jnp.exp(scores - local_max[:, None]).astype(jnp.bfloat16)
    total = jnp.sum(raised.astype(jnp.float32), axis=1)
    mixed = jnp.dot(raised, value_head, preferred_element_type=jnp.float32)
    return (local_max, total, mixed)


def scale_heads(mixed, factor):
    query_count, model_width = mixed.shape
    head_count = factor.shape[0]
    shaped = mixed.reshape(query_count, head_count, model_width // head_count)
    return (shaped * factor.T[:, :, None]).reshape(query_count, model_width)


def loss_coefficients(
    sigma, target, matched, intersection, predicted, truth_count, hits_total, model_width
):
    denom = predicted + truth_count + 1.0
    slope = -2.0 / denom
    level = (2.0 * intersection + 1.0) / (denom * denom)
    dice_part = hits_total * (slope[:, None] * target + level[:, None]) * sigma * (1.0 - sigma)
    return (matched[:, None] * (sigma - target + dice_part) * model_width ** (-0.5)).astype(
        jnp.bfloat16
    )


def body(
    hits,
    enc_qkv,
    enc_out,
    enc_up,
    enc_down,
    queries,
    cross_q,
    cross_kv,
    cross_out,
    mask_first,
    mask_second,
    truth,
    match,
):
    model_width = hits.shape[1]
    local_hits = hits.shape[0]
    query_count = queries.shape[0]
    hits_total = float(local_hits * lax.axis_size("phi") * lax.axis_size("query"))
    track_count = query_count * lax.axis_size("query") // 2
    normed = norm_rows(hits).astype(jnp.bfloat16)
    projected = jnp.dot(normed, enc_qkv, preferred_element_type=jnp.float32).astype(jnp.bfloat16)
    extended = extended_2(projected[:, model_width:], ((("phi", "query"), 0),), WIN // 2)
    block_rows = local_hits // 2
    span = extended.shape[0] - local_hits
    attended = jnp.concatenate(
        [
            window_attend(
                projected[b * block_rows : (b + 1) * block_rows, :model_width],
                extended[b * block_rows : b * block_rows + block_rows + span],
            )
            for b in range(2)
        ]
    )
    residual = hits.astype(jnp.float32) + jnp.dot(
        attended, enc_out, preferred_element_type=jnp.float32
    )
    upper = jax.nn.gelu(
        jnp.dot(
            norm_rows(residual).astype(jnp.bfloat16), enc_up, preferred_element_type=jnp.float32
        ),
        approximate=True,
    ).astype(jnp.bfloat16)
    encoded = (residual + jnp.dot(upper, enc_down, preferred_element_type=jnp.float32)).astype(
        jnp.bfloat16
    )
    local_kv = jnp.dot(
        norm_rows(encoded).astype(jnp.bfloat16), cross_kv, preferred_element_type=jnp.float32
    ).astype(jnp.bfloat16)
    shifted = truth + 1
    digits = jnp.stack([shifted // 256, shifted % 256], axis=1).astype(jnp.bfloat16)
    digits = jnp.pad(digits, ((0, 0), (0, 126)))
    gathered = lax.all_gather(
        jnp.concatenate([local_kv, encoded, digits], axis=1), "query", axis=0, tiled=True
    )
    group_kv = gathered[:, : 2 * model_width]
    group_hits = gathered[:, 2 * model_width : 3 * model_width]
    group_digits = gathered[:, 3 * model_width :].astype(jnp.int32)
    group_truth = group_digits[:, 0] * 256 + group_digits[:, 1] - 1
    query_proj = jnp.dot(queries, cross_q, preferred_element_type=jnp.float32).astype(jnp.bfloat16)
    head_size = model_width // HEADS
    group_count = group_kv.shape[0]
    query_heads = query_proj.reshape(query_count, HEADS, head_size)
    key_heads = group_kv[:, :model_width].reshape(group_count, HEADS, head_size)
    value_heads = group_kv[:, model_width:].reshape(group_count, HEADS, head_size)
    scores = jnp.einsum(
        "qhd,khd->hqk", query_heads, key_heads, preferred_element_type=jnp.float32
    ) * head_size ** (-0.5)
    local_max = jnp.max(scores, axis=-1)
    raised = jnp.exp(scores - local_max[..., None]).astype(jnp.bfloat16)
    local_total = jnp.sum(raised.astype(jnp.float32), axis=-1)
    local_mixed = jnp.einsum(
        "hqk,khd->qhd", raised, value_heads, preferred_element_type=jnp.float32
    ).reshape(query_count, model_width)
    (_, total), mixed = butterfly(
        (jnp.stack([local_max, local_total]), local_mixed.astype(jnp.bfloat16)),
        "phi",
        softmax_combine,
        ordered=True,
        order="near_first",
    )
    mixed = mixed.astype(jnp.float32)
    context = scale_heads(mixed, 1.0 / total).astype(jnp.bfloat16)
    mixed_queries = queries.astype(jnp.float32) + jnp.dot(
        context, cross_out, preferred_element_type=jnp.float32
    )
    mask_hidden = jax.nn.relu(
        jnp.dot(
            norm_rows(mixed_queries).astype(jnp.bfloat16),
            mask_first,
            preferred_element_type=jnp.float32,
        )
    ).astype(jnp.bfloat16)
    mask_embed = jnp.dot(mask_hidden, mask_second, preferred_element_type=jnp.float32).astype(
        jnp.bfloat16
    )
    own_digits = gathered[:, 3 * model_width : 3 * model_width + 2]
    pieces = [(group_hits, own_digits)] + [
        fetch_rows(group_hits, own_digits, mask) for mask in (1, 2, 3)
    ]
    position = jnp.bitwise_xor(jnp.arange(4), lax.axis_index("phi") % 4)
    pair_hits = jnp.take(jnp.stack([p[0] for p in pieces]), position, axis=0)
    pair_digits = jnp.take(jnp.stack([p[1] for p in pieces]), position, axis=0)
    pair_hits = pair_hits.reshape(-1, model_width)
    pair_digits = pair_digits.reshape(-1, 2).astype(jnp.int32)
    pair_truth = pair_digits[:, 0] * 256 + pair_digits[:, 1] - 1
    logits = lax.dot_general(
        mask_embed, pair_hits, (((1,), (1,)), ((), ())), preferred_element_type=jnp.float32
    ) * model_width ** (-0.5)
    sigma = jax.nn.sigmoid(logits)
    matched_flag = match < track_count
    matched = matched_flag.astype(jnp.float32)
    target = jnp.logical_and(match[:, None] == pair_truth[None, :], matched_flag[:, None]).astype(
        jnp.float32
    )
    intersection, predicted, truth_count = butterfly(
        jnp.stack(
            [jnp.sum(sigma * target, axis=1), jnp.sum(sigma, axis=1), jnp.sum(target, axis=1)]
        ),
        "phi",
        add_trees,
        distance=4,
    )
    mask_fill = predicted / hits_total
    coef = loss_coefficients(
        sigma, target, matched, intersection, predicted, truth_count, hits_total, model_width
    )
    mask_grad = narrow_butterfly(
        jnp.dot(coef, pair_hits, preferred_element_type=jnp.float32), "phi", distance=4
    )
    group_count = group_hits.shape[0]
    own_coef = lax.dynamic_slice_in_dim(
        coef, (lax.axis_index("phi") % 4) * group_count, group_count, axis=1
    )
    hit_grad = reduce_scatter_rows(
        lax.dot_general(
            own_coef, mask_embed, (((0,), (0,)), ((), ())), preferred_element_type=jnp.float32
        ),
        "query",
    )
    return (encoded, mask_embed, hit_grad, mask_grad, mask_fill)


def solution(mesh):
    return jax.shard_map(
        body,
        mesh=mesh,
        in_specs=(
            P(("event", "phi", "query"), None),
            P(),
            P(),
            P(),
            P(),
            P("query", None),
            P(),
            P(),
            P(),
            P(),
            P(),
            P(("event", "phi", "query")),
            P(("event", "query")),
        ),
        out_specs=(
            P(("event", "phi", "query"), None),
            P(("event", "query"), None),
            P(("event", "phi", "query"), None),
            P(("event", "query"), None),
            P(("event", "query")),
        ),
        check_vma=False,
    )
```

```python
import jax
import jax.numpy as jnp
from jax import lax
from jax.sharding import PartitionSpec as P

HEADS = 8
WIN = 512


def extended_2(block, sides, width):
    for axis, dim in sides:
        count = lax.axis_size(axis)
        forward = [(i, i + 1) for i in range(count - 1)]
        forward.append((count - 1, 0))
        backward = [(target, source) for source, target in forward]
        low = lax.ppermute(
            lax.slice_in_dim(block, block.shape[dim] - width, None, axis=dim), axis, forward
        )
        high = lax.ppermute(lax.slice_in_dim(block, 0, width, axis=dim), axis, backward)
        block = jnp.concatenate([low, block, high], axis=dim)
    return block


def partner_pairs(count, distance):
    return [(i, i ^ distance) for i in range(count)]


def butterfly(tree, axis, combine, ordered=False, distance=1, order=None):
    count = lax.axis_size(axis)
    assert count & (count - 1) == 0
    index = lax.axis_index(axis)
    distances = []
    while distance < count:
        distances.append(distance)
        distance *= 2
    if order is not None and len(distances) >= 2:
        distances[0], distances[1] = distances[1], distances[0]
    for distance in distances:
        other = lax.ppermute(tree, axis, partner_pairs(count, distance))
        if ordered:
            upper = (index // distance) % 2 == 1
            first = jax.tree.map(lambda a, b: jnp.where(upper, b, a), tree, other)
            second = jax.tree.map(lambda a, b: jnp.where(upper, a, b), tree, other)
            tree = combine(first, second)
        else:
            tree = combine(tree, other)
    return tree


def add_trees(a, b):
    return jax.tree.map(jnp.add, a, b)


def narrow_butterfly(block, axis, distance=1):
    count = lax.axis_size(axis)
    while distance < count:
        sent = block.astype(jnp.bfloat16)
        other = lax.ppermute(sent, axis, partner_pairs(count, distance))
        block = sent.astype(jnp.float32) + other.astype(jnp.float32)
        distance *= 2
    return block


def softmax_combine(a, b):
    (max_a, total_a), mixed_a = a
    (max_b, total_b), mixed_b = b
    mixed_a = mixed_a.astype(jnp.float32)
    mixed_b = mixed_b.astype(jnp.float32)
    top = jnp.maximum(max_a, max_b)
    factor_a = jnp.exp(max_a - top)
    factor_b = jnp.exp(max_b - top)
    return (
        jnp.stack([top, total_a * factor_a + total_b * factor_b]),
        (scale_heads(mixed_a, factor_a) + scale_heads(mixed_b, factor_b)).astype(jnp.bfloat16),
    )


def reduce_scatter_rows(block, axis):
    count = lax.axis_size(axis)
    assert count & (count - 1) == 0
    index = lax.axis_index(axis)
    distance = count // 2
    while distance >= 1:
        half = block.shape[0] // 2
        upper = (index // distance) % 2 == 1
        low, high = block[:half], block[half:]
        keep = jnp.where(upper, high, low)
        send = jnp.where(upper, low, high)
        block = keep + lax.ppermute(send, axis, partner_pairs(count, distance))
        distance //= 2
    return block


def partner_rows(hits, digits, distance):
    count_rows, width = hits.shape
    digit_rows = digits.T.reshape(2 * count_rows // width, width)
    payload = jnp.concatenate(
        [hits, jnp.pad(digit_rows, ((0, (-digit_rows.shape[0]) % 16), (0, 0)))]
    )
    other = lax.ppermute(payload, "phi", partner_pairs(lax.axis_size("phi"), distance))
    other_hits = other[:count_rows]
    other_digits = other[count_rows : count_rows + digit_rows.shape[0]].reshape(2, count_rows).T
    upper = (lax.axis_index("phi") // distance) % 2 == 1
    hits = jnp.where(
        upper, jnp.concatenate([other_hits, hits]), jnp.concatenate([hits, other_hits])
    )
    digits = jnp.where(
        upper, jnp.concatenate([other_digits, digits]), jnp.concatenate([digits, other_digits])
    )
    return hits, digits


def norm_rows(entries):
    widened = entries.astype(jnp.float32)
    centred = widened - jnp.mean(widened, axis=-1, keepdims=True)
    spread = jnp.mean(centred * centred, axis=-1, keepdims=True)
    return centred * lax.rsqrt(spread + 1e-05)


def window_attend(query_rows, kv_ext):
    row_count, model_width = query_rows.shape
    head_size = model_width // HEADS
    key_count = kv_ext.shape[0]
    key_span = key_count - row_count
    query_heads = query_rows.reshape(row_count, HEADS, head_size)
    key_heads = kv_ext[:, :model_width].reshape(key_count, HEADS, head_size)
    value_heads = kv_ext[:, model_width:].reshape(key_count, HEADS, head_size)
    scores = jnp.einsum(
        "qhd,khd->hqk", query_heads, key_heads, preferred_element_type=jnp.float32
    ) * head_size ** (-0.5)
    offset = lax.broadcasted_iota(jnp.int32, (row_count, key_count), 1) - lax.broadcasted_iota(
        jnp.int32, (row_count, key_count), 0
    )
    inside = jnp.logical_and(offset >= 0, offset < key_span)
    scores = jnp.where(inside[None, :, :], scores, -1e30)
    raised = jnp.exp(scores - jnp.max(scores, axis=-1, keepdims=True))
    weights = (raised / jnp.sum(raised, axis=-1, keepdims=True)).astype(jnp.bfloat16)
    attended = jnp.einsum("hqk,khd->qhd", weights, value_heads, preferred_element_type=jnp.float32)
    return attended.reshape(row_count, model_width).astype(jnp.bfloat16)


def split_heads(matrix):
    row_count, model_width = matrix.shape
    return matrix.reshape(row_count, HEADS, model_width // HEADS).transpose(1, 0, 2)


def head_partial(operands):
    query_head, key_head, value_head = operands
    scores = lax.dot_general(
        query_head, key_head, (((1,), (1,)), ((), ())), preferred_element_type=jnp.float32
    ) * query_head.shape[1] ** (-0.5)
    local_max = jnp.max(scores, axis=1)
    raised = jnp.exp(scores - local_max[:, None]).astype(jnp.bfloat16)
    total = jnp.sum(raised.astype(jnp.float32), axis=1)
    mixed = jnp.dot(raised, value_head, preferred_element_type=jnp.float32)
    return (local_max, total, mixed)


def scale_heads(mixed, factor):
    query_count, model_width = mixed.shape
    head_count = factor.shape[0]
    shaped = mixed.reshape(query_count, head_count, model_width // head_count)
    return (shaped * factor.T[:, :, None]).reshape(query_count, model_width)


def loss_coefficients(
    sigma, target, matched, intersection, predicted, truth_count, hits_total, model_width
):
    denom = predicted + truth_count + 1.0
    slope = -2.0 / denom
    level = (2.0 * intersection + 1.0) / (denom * denom)
    dice_part = hits_total * (slope[:, None] * target + level[:, None]) * sigma * (1.0 - sigma)
    return (matched[:, None] * (sigma - target + dice_part) * model_width ** (-0.5)).astype(
        jnp.bfloat16
    )


def body(
    hits,
    enc_qkv,
    enc_out,
    enc_up,
    enc_down,
    queries,
    cross_q,
    cross_kv,
    cross_out,
    mask_first,
    mask_second,
    truth,
    match,
):
    model_width = hits.shape[1]
    local_hits = hits.shape[0]
    query_count = queries.shape[0]
    hits_total = float(local_hits * lax.axis_size("phi") * lax.axis_size("query"))
    track_count = query_count * lax.axis_size("query") // 2
    normed = norm_rows(hits).astype(jnp.bfloat16)
    projected = jnp.dot(normed, enc_qkv, preferred_element_type=jnp.float32).astype(jnp.bfloat16)
    extended = extended_2(projected[:, model_width:], ((("phi", "query"), 0),), WIN // 2)
    block_rows = local_hits // 2
    span = extended.shape[0] - local_hits
    attended = jnp.concatenate(
        [
            window_attend(
                projected[b * block_rows : (b + 1) * block_rows, :model_width],
                extended[b * block_rows : b * block_rows + block_rows + span],
            )
            for b in range(2)
        ]
    )
    residual = hits.astype(jnp.float32) + jnp.dot(
        attended, enc_out, preferred_element_type=jnp.float32
    )
    upper = jax.nn.gelu(
        jnp.dot(
            norm_rows(residual).astype(jnp.bfloat16), enc_up, preferred_element_type=jnp.float32
        ),
        approximate=True,
    ).astype(jnp.bfloat16)
    encoded = (residual + jnp.dot(upper, enc_down, preferred_element_type=jnp.float32)).astype(
        jnp.bfloat16
    )
    local_kv = jnp.dot(
        norm_rows(encoded).astype(jnp.bfloat16), cross_kv, preferred_element_type=jnp.float32
    ).astype(jnp.bfloat16)
    shifted = truth + 1
    digits = jnp.stack([shifted // 256, shifted % 256], axis=1).astype(jnp.bfloat16)
    digits = jnp.pad(digits, ((0, 0), (0, 126)))
    gathered = lax.all_gather(
        jnp.concatenate([local_kv, encoded, digits], axis=1), "query", axis=0, tiled=True
    )
    group_kv = gathered[:, : 2 * model_width]
    group_hits = gathered[:, 2 * model_width : 3 * model_width]
    group_digits = gathered[:, 3 * model_width :].astype(jnp.int32)
    group_truth = group_digits[:, 0] * 256 + group_digits[:, 1] - 1
    query_proj = jnp.dot(queries, cross_q, preferred_element_type=jnp.float32).astype(jnp.bfloat16)
    head_size = model_width // HEADS
    group_count = group_kv.shape[0]
    query_heads = query_proj.reshape(query_count, HEADS, head_size)
    key_heads = group_kv[:, :model_width].reshape(group_count, HEADS, head_size)
    value_heads = group_kv[:, model_width:].reshape(group_count, HEADS, head_size)
    scores = jnp.einsum(
        "qhd,khd->hqk", query_heads, key_heads, preferred_element_type=jnp.float32
    ) * head_size ** (-0.5)
    local_max = jnp.max(scores, axis=-1)
    raised = jnp.exp(scores - local_max[..., None]).astype(jnp.bfloat16)
    local_total = jnp.sum(raised.astype(jnp.float32), axis=-1)
    local_mixed = jnp.einsum(
        "hqk,khd->qhd", raised, value_heads, preferred_element_type=jnp.float32
    ).reshape(query_count, model_width)
    (_, total), mixed = butterfly(
        (jnp.stack([local_max, local_total]), local_mixed.astype(jnp.bfloat16)),
        "phi",
        softmax_combine,
        order="near_first",
    )
    mixed = mixed.astype(jnp.float32)
    context = scale_heads(mixed, 1.0 / total).astype(jnp.bfloat16)
    mixed_queries = queries.astype(jnp.float32) + jnp.dot(
        context, cross_out, preferred_element_type=jnp.float32
    )
    mask_hidden = jax.nn.relu(
        jnp.dot(
            norm_rows(mixed_queries).astype(jnp.bfloat16),
            mask_first,
            preferred_element_type=jnp.float32,
        )
    ).astype(jnp.bfloat16)
    mask_embed = jnp.dot(mask_hidden, mask_second, preferred_element_type=jnp.float32).astype(
        jnp.bfloat16
    )
    pair_hits = group_hits
    pair_digits = gathered[:, 3 * model_width : 3 * model_width + 2]
    for distance in (1, 2):
        pair_hits, pair_digits = partner_rows(pair_hits, pair_digits, distance)
    pair_digits = pair_digits.astype(jnp.int32)
    pair_truth = pair_digits[:, 0] * 256 + pair_digits[:, 1] - 1
    logits = lax.dot_general(
        mask_embed, pair_hits, (((1,), (1,)), ((), ())), preferred_element_type=jnp.float32
    ) * model_width ** (-0.5)
    sigma = jax.nn.sigmoid(logits)
    matched_flag = match < track_count
    matched = matched_flag.astype(jnp.float32)
    target = jnp.logical_and(match[:, None] == pair_truth[None, :], matched_flag[:, None]).astype(
        jnp.float32
    )
    intersection, predicted, truth_count = butterfly(
        jnp.stack(
            [jnp.sum(sigma * target, axis=1), jnp.sum(sigma, axis=1), jnp.sum(target, axis=1)]
        ),
        "phi",
        add_trees,
        distance=4,
    )
    mask_fill = predicted / hits_total
    coef = loss_coefficients(
        sigma, target, matched, intersection, predicted, truth_count, hits_total, model_width
    )
    mask_grad = narrow_butterfly(
        jnp.dot(coef, pair_hits, preferred_element_type=jnp.float32), "phi", distance=4
    )
    group_count = group_hits.shape[0]
    own_coef = lax.dynamic_slice_in_dim(
        coef, (lax.axis_index("phi") % 4) * group_count, group_count, axis=1
    )
    hit_grad = reduce_scatter_rows(
        lax.dot_general(
            own_coef, mask_embed, (((0,), (0,)), ((), ())), preferred_element_type=jnp.float32
        ),
        "query",
    )
    return (encoded, mask_embed, hit_grad, mask_grad, mask_fill)


def solution(mesh):
    return jax.shard_map(
        body,
        mesh=mesh,
        in_specs=(
            P(("event", "phi", "query"), None),
            P(),
            P(),
            P(),
            P(),
            P("query", None),
            P(),
            P(),
            P(),
            P(),
            P(),
            P(("event", "phi", "query")),
            P(("event", "query")),
        ),
        out_specs=(
            P(("event", "phi", "query"), None),
            P(("event", "query"), None),
            P(("event", "phi", "query"), None),
            P(("event", "query"), None),
            P(("event", "query")),
        ),
        check_vma=False,
    )
```

```python
import jax
import jax.numpy as jnp
from jax import lax
from jax.sharding import PartitionSpec as P

HEADS = 8
WIN = 512


def extended_2(block, sides, width):
    for axis, dim in sides:
        count = lax.axis_size(axis)
        forward = [(i, i + 1) for i in range(count - 1)]
        forward.append((count - 1, 0))
        backward = [(target, source) for source, target in forward]
        low = lax.ppermute(
            lax.slice_in_dim(block, block.shape[dim] - width, None, axis=dim), axis, forward
        )
        high = lax.ppermute(lax.slice_in_dim(block, 0, width, axis=dim), axis, backward)
        block = jnp.concatenate([low, block, high], axis=dim)
    return block


def partner_pairs(count, distance):
    return [(i, i ^ distance) for i in range(count)]


def butterfly(tree, axis, combine, ordered=False, distance=1, order=None):
    count = lax.axis_size(axis)
    assert count & (count - 1) == 0
    index = lax.axis_index(axis)
    distances = []
    while distance < count:
        distances.append(distance)
        distance *= 2
    if order is not None and len(distances) >= 2:
        distances[0], distances[1] = distances[1], distances[0]
    for distance in distances:
        other = lax.ppermute(tree, axis, partner_pairs(count, distance))
        if ordered:
            upper = (index // distance) % 2 == 1
            first = jax.tree.map(lambda a, b: jnp.where(upper, b, a), tree, other)
            second = jax.tree.map(lambda a, b: jnp.where(upper, a, b), tree, other)
            tree = combine(first, second)
        else:
            tree = combine(tree, other)
    return tree


def add_trees(a, b):
    return jax.tree.map(jnp.add, a, b)


def narrow_butterfly(block, axis, distance=1):
    count = lax.axis_size(axis)
    while distance < count:
        sent = block.astype(jnp.bfloat16)
        other = lax.ppermute(sent, axis, partner_pairs(count, distance))
        block = sent.astype(jnp.float32) + other.astype(jnp.float32)
        distance *= 2
    return block


def softmax_combine(a, b):
    (max_a, total_a), mixed_a = a
    (max_b, total_b), mixed_b = b
    mixed_a = mixed_a.astype(jnp.float32)
    mixed_b = mixed_b.astype(jnp.float32)
    top = jnp.maximum(max_a, max_b)
    factor_a = jnp.exp(max_a - top)
    factor_b = jnp.exp(max_b - top)
    return (
        jnp.stack([top, total_a * factor_a + total_b * factor_b]),
        (scale_heads(mixed_a, factor_a) + scale_heads(mixed_b, factor_b)).astype(jnp.bfloat16),
    )


def reduce_scatter_rows(block, axis):
    count = lax.axis_size(axis)
    assert count & (count - 1) == 0
    index = lax.axis_index(axis)
    distance = count // 2
    while distance >= 1:
        half = block.shape[0] // 2
        upper = (index // distance) % 2 == 1
        low, high = block[:half], block[half:]
        keep = jnp.where(upper, high, low)
        send = jnp.where(upper, low, high)
        block = keep + lax.ppermute(send, axis, partner_pairs(count, distance))
        distance //= 2
    return block


def partner_rows(hits, digits, distance):
    count_rows, width = hits.shape
    digit_rows = digits.T.reshape(2 * count_rows // width, width)
    payload = jnp.concatenate(
        [hits, jnp.pad(digit_rows, ((0, (-digit_rows.shape[0]) % 16), (0, 0)))]
    )
    other = lax.ppermute(payload, "phi", partner_pairs(lax.axis_size("phi"), distance))
    other_hits = other[:count_rows]
    other_digits = other[count_rows : count_rows + digit_rows.shape[0]].reshape(2, count_rows).T
    upper = (lax.axis_index("phi") // distance) % 2 == 1
    hits = jnp.where(
        upper, jnp.concatenate([other_hits, hits]), jnp.concatenate([hits, other_hits])
    )
    digits = jnp.where(
        upper, jnp.concatenate([other_digits, digits]), jnp.concatenate([digits, other_digits])
    )
    return hits, digits


def norm_rows(entries):
    widened = entries.astype(jnp.float32)
    centred = widened - jnp.mean(widened, axis=-1, keepdims=True)
    spread = jnp.mean(centred * centred, axis=-1, keepdims=True)
    return centred * lax.rsqrt(spread + 1e-05)


def window_attend(query_rows, kv_ext):
    row_count, model_width = query_rows.shape
    head_size = model_width // HEADS
    key_count = kv_ext.shape[0]
    key_span = key_count - row_count
    query_heads = query_rows.reshape(row_count, HEADS, head_size)
    key_heads = kv_ext[:, :model_width].reshape(key_count, HEADS, head_size)
    value_heads = kv_ext[:, model_width:].reshape(key_count, HEADS, head_size)
    scores = jnp.einsum(
        "qhd,khd->hqk", query_heads, key_heads, preferred_element_type=jnp.float32
    ) * head_size ** (-0.5)
    offset = lax.broadcasted_iota(jnp.int32, (row_count, key_count), 1) - lax.broadcasted_iota(
        jnp.int32, (row_count, key_count), 0
    )
    inside = jnp.logical_and(offset >= 0, offset < key_span)
    scores = jnp.where(inside[None, :, :], scores, -1e30)
    raised = jnp.exp(scores - jnp.max(scores, axis=-1, keepdims=True))
    weights = (raised / jnp.sum(raised, axis=-1, keepdims=True)).astype(jnp.bfloat16)
    attended = jnp.einsum("hqk,khd->qhd", weights, value_heads, preferred_element_type=jnp.float32)
    return attended.reshape(row_count, model_width).astype(jnp.bfloat16)


def split_heads(matrix):
    row_count, model_width = matrix.shape
    return matrix.reshape(row_count, HEADS, model_width // HEADS).transpose(1, 0, 2)


def head_partial(operands):
    query_head, key_head, value_head = operands
    scores = lax.dot_general(
        query_head, key_head, (((1,), (1,)), ((), ())), preferred_element_type=jnp.float32
    ) * query_head.shape[1] ** (-0.5)
    local_max = jnp.max(scores, axis=1)
    raised = jnp.exp(scores - local_max[:, None]).astype(jnp.bfloat16)
    total = jnp.sum(raised.astype(jnp.float32), axis=1)
    mixed = jnp.dot(raised, value_head, preferred_element_type=jnp.float32)
    return (local_max, total, mixed)


def scale_heads(mixed, factor):
    query_count, model_width = mixed.shape
    head_count = factor.shape[0]
    shaped = mixed.reshape(query_count, head_count, model_width // head_count)
    return (shaped * factor.T[:, :, None]).reshape(query_count, model_width)


def loss_coefficients(
    sigma, target, matched, intersection, predicted, truth_count, hits_total, model_width
):
    denom = predicted + truth_count + 1.0
    slope = -2.0 / denom
    level = (2.0 * intersection + 1.0) / (denom * denom)
    dice_part = hits_total * (slope[:, None] * target + level[:, None]) * sigma * (1.0 - sigma)
    return (matched[:, None] * (sigma - target + dice_part) * model_width ** (-0.5)).astype(
        jnp.bfloat16
    )


def body(
    hits,
    enc_qkv,
    enc_out,
    enc_up,
    enc_down,
    queries,
    cross_q,
    cross_kv,
    cross_out,
    mask_first,
    mask_second,
    truth,
    match,
):
    model_width = hits.shape[1]
    local_hits = hits.shape[0]
    query_count = queries.shape[0]
    hits_total = float(local_hits * lax.axis_size("phi") * lax.axis_size("query"))
    track_count = query_count * lax.axis_size("query") // 2
    normed = norm_rows(hits).astype(jnp.bfloat16)
    projected = jnp.dot(normed, enc_qkv, preferred_element_type=jnp.float32).astype(jnp.bfloat16)
    extended = extended_2(projected[:, model_width:], ((("phi", "query"), 0),), WIN // 2)
    block_rows = local_hits // 2
    span = extended.shape[0] - local_hits
    attended = jnp.concatenate(
        [
            window_attend(
                projected[b * block_rows : (b + 1) * block_rows, :model_width],
                extended[b * block_rows : b * block_rows + block_rows + span],
            )
            for b in range(2)
        ]
    )
    residual = hits.astype(jnp.float32) + jnp.dot(
        attended, enc_out, preferred_element_type=jnp.float32
    )
    upper = jax.nn.gelu(
        jnp.dot(
            norm_rows(residual).astype(jnp.bfloat16), enc_up, preferred_element_type=jnp.float32
        ),
        approximate=True,
    ).astype(jnp.bfloat16)
    encoded = (residual + jnp.dot(upper, enc_down, preferred_element_type=jnp.float32)).astype(
        jnp.bfloat16
    )
    local_kv = jnp.dot(
        norm_rows(encoded).astype(jnp.bfloat16), cross_kv, preferred_element_type=jnp.float32
    ).astype(jnp.bfloat16)
    shifted = truth + 1
    digits = jnp.stack([shifted // 256, shifted % 256], axis=1).astype(jnp.bfloat16)
    digits = jnp.pad(digits, ((0, 0), (0, 126)))
    gathered = lax.all_gather(
        jnp.concatenate([local_kv, encoded, digits], axis=1), "query", axis=0, tiled=True
    )
    group_kv = gathered[:, : 2 * model_width]
    group_hits = gathered[:, 2 * model_width : 3 * model_width]
    group_digits = gathered[:, 3 * model_width :].astype(jnp.int32)
    group_truth = group_digits[:, 0] * 256 + group_digits[:, 1] - 1
    query_proj = jnp.dot(queries, cross_q, preferred_element_type=jnp.float32).astype(jnp.bfloat16)
    head_size = model_width // HEADS
    group_count = group_kv.shape[0]
    query_heads = query_proj.reshape(query_count, HEADS, head_size)
    key_heads = group_kv[:, :model_width].reshape(group_count, HEADS, head_size)
    value_heads = group_kv[:, model_width:].reshape(group_count, HEADS, head_size)
    scores = jnp.einsum(
        "qhd,khd->hqk", query_heads, key_heads, preferred_element_type=jnp.float32
    ) * head_size ** (-0.5)
    local_max = jnp.max(scores, axis=-1)
    raised = jnp.exp(scores - local_max[..., None]).astype(jnp.bfloat16)
    local_total = jnp.sum(raised.astype(jnp.float32), axis=-1)
    local_mixed = jnp.einsum(
        "hqk,khd->qhd", raised, value_heads, preferred_element_type=jnp.float32
    ).reshape(query_count, model_width)
    (_, total), mixed = butterfly(
        (jnp.stack([local_max, local_total]), local_mixed.astype(jnp.bfloat16)),
        "phi",
        softmax_combine,
        ordered=True,
        order="near_first",
    )
    mixed = mixed.astype(jnp.float32)
    context = scale_heads(mixed, 1.0 / total).astype(jnp.bfloat16)
    mixed_queries = queries.astype(jnp.float32) + jnp.dot(
        context, cross_out, preferred_element_type=jnp.float32
    )
    mask_hidden = jax.nn.relu(
        jnp.dot(
            norm_rows(mixed_queries).astype(jnp.bfloat16),
            mask_first,
            preferred_element_type=jnp.float32,
        )
    ).astype(jnp.bfloat16)
    mask_embed = jnp.dot(mask_hidden, mask_second, preferred_element_type=jnp.float32).astype(
        jnp.bfloat16
    )
    pair_hits = group_hits
    pair_digits = gathered[:, 3 * model_width : 3 * model_width + 2]
    for distance in (2, 1):
        pair_hits, pair_digits = partner_rows(pair_hits, pair_digits, distance)
    pair_digits = pair_digits.astype(jnp.int32)
    pair_truth = pair_digits[:, 0] * 256 + pair_digits[:, 1] - 1
    logits = lax.dot_general(
        mask_embed, pair_hits, (((1,), (1,)), ((), ())), preferred_element_type=jnp.float32
    ) * model_width ** (-0.5)
    sigma = jax.nn.sigmoid(logits)
    matched_flag = match < track_count
    matched = matched_flag.astype(jnp.float32)
    target = jnp.logical_and(match[:, None] == pair_truth[None, :], matched_flag[:, None]).astype(
        jnp.float32
    )
    intersection, predicted, truth_count = butterfly(
        jnp.stack(
            [jnp.sum(sigma * target, axis=1), jnp.sum(sigma, axis=1), jnp.sum(target, axis=1)]
        ),
        "phi",
        add_trees,
        distance=4,
    )
    mask_fill = predicted / hits_total
    coef = loss_coefficients(
        sigma, target, matched, intersection, predicted, truth_count, hits_total, model_width
    )
    mask_grad = narrow_butterfly(
        jnp.dot(coef, pair_hits, preferred_element_type=jnp.float32), "phi", distance=4
    )
    group_count = group_hits.shape[0]
    own_coef = lax.dynamic_slice_in_dim(
        coef,
        ((lax.axis_index("phi") % 2) * 2 + (lax.axis_index("phi") // 2) % 2) * group_count,
        group_count,
        axis=1,
    )
    hit_grad = reduce_scatter_rows(
        lax.dot_general(
            own_coef, mask_embed, (((0,), (0,)), ((), ())), preferred_element_type=jnp.float32
        ),
        "query",
    )
    return (encoded, mask_embed, hit_grad, mask_grad, mask_fill)


def solution(mesh):
    return jax.shard_map(
        body,
        mesh=mesh,
        in_specs=(
            P(("event", "phi", "query"), None),
            P(),
            P(),
            P(),
            P(),
            P("query", None),
            P(),
            P(),
            P(),
            P(),
            P(),
            P(("event", "phi", "query")),
            P(("event", "query")),
        ),
        out_specs=(
            P(("event", "phi", "query"), None),
            P(("event", "query"), None),
            P(("event", "phi", "query"), None),
            P(("event", "query"), None),
            P(("event", "query")),
        ),
        check_vma=False,
    )
```

```python
import jax
import jax.numpy as jnp
from jax import lax
from jax.sharding import PartitionSpec as P

HEADS = 8
WIN = 512


def extended_2(block, sides, width):
    for axis, dim in sides:
        count = lax.axis_size(axis)
        forward = [(i, i + 1) for i in range(count - 1)]
        forward.append((count - 1, 0))
        backward = [(target, source) for source, target in forward]
        low = lax.ppermute(
            lax.slice_in_dim(block, block.shape[dim] - width, None, axis=dim), axis, forward
        )
        high = lax.ppermute(lax.slice_in_dim(block, 0, width, axis=dim), axis, backward)
        block = jnp.concatenate([low, block, high], axis=dim)
    return block


def partner_pairs(count, distance):
    return [(i, i ^ distance) for i in range(count)]


def butterfly(tree, axis, combine, ordered=False, distance=1, order=None):
    count = lax.axis_size(axis)
    assert count & (count - 1) == 0
    index = lax.axis_index(axis)
    distances = []
    while distance < count:
        distances.append(distance)
        distance *= 2
    if order is not None and len(distances) >= 2:
        distances[0], distances[1] = distances[1], distances[0]
    for distance in distances:
        other = lax.ppermute(tree, axis, partner_pairs(count, distance))
        if ordered:
            upper = (index // distance) % 2 == 1
            first = jax.tree.map(lambda a, b: jnp.where(upper, b, a), tree, other)
            second = jax.tree.map(lambda a, b: jnp.where(upper, a, b), tree, other)
            tree = combine(first, second)
        else:
            tree = combine(tree, other)
    return tree


def add_trees(a, b):
    return jax.tree.map(jnp.add, a, b)


def narrow_butterfly(block, axis, distance=1):
    count = lax.axis_size(axis)
    while distance < count:
        sent = block.astype(jnp.bfloat16)
        other = lax.ppermute(sent, axis, partner_pairs(count, distance))
        block = sent.astype(jnp.float32) + other.astype(jnp.float32)
        distance *= 2
    return block


def softmax_combine(a, b):
    (max_a, total_a), mixed_a = a
    (max_b, total_b), mixed_b = b
    mixed_a = mixed_a.astype(jnp.float32)
    mixed_b = mixed_b.astype(jnp.float32)
    top = jnp.maximum(max_a, max_b)
    factor_a = jnp.exp(max_a - top)
    factor_b = jnp.exp(max_b - top)
    return (
        jnp.stack([top, total_a * factor_a + total_b * factor_b]),
        (scale_heads(mixed_a, factor_a) + scale_heads(mixed_b, factor_b)).astype(jnp.bfloat16),
    )


def reduce_scatter_rows(block, axis):
    count = lax.axis_size(axis)
    assert count & (count - 1) == 0
    index = lax.axis_index(axis)
    distance = count // 2
    while distance >= 1:
        half = block.shape[0] // 2
        upper = (index // distance) % 2 == 1
        low, high = block[:half], block[half:]
        keep = jnp.where(upper, high, low)
        send = jnp.where(upper, low, high)
        block = keep + lax.ppermute(send, axis, partner_pairs(count, distance))
        distance //= 2
    return block


def partner_rows(hits, digits, distance):
    count_rows, width = hits.shape
    digit_rows = digits.T.reshape(2 * count_rows // width, width)
    payload = jnp.concatenate(
        [hits, jnp.pad(digit_rows, ((0, (-digit_rows.shape[0]) % 16), (0, 0)))]
    )
    other = lax.ppermute(payload, "phi", partner_pairs(lax.axis_size("phi"), distance))
    other_hits = other[:count_rows]
    other_digits = other[count_rows : count_rows + digit_rows.shape[0]].reshape(2, count_rows).T
    upper = (lax.axis_index("phi") // distance) % 2 == 1
    hits = jnp.where(
        upper, jnp.concatenate([other_hits, hits]), jnp.concatenate([hits, other_hits])
    )
    digits = jnp.where(
        upper, jnp.concatenate([other_digits, digits]), jnp.concatenate([digits, other_digits])
    )
    return hits, digits


def norm_rows(entries):
    widened = entries.astype(jnp.float32)
    centred = widened - jnp.mean(widened, axis=-1, keepdims=True)
    spread = jnp.mean(centred * centred, axis=-1, keepdims=True)
    return centred * lax.rsqrt(spread + 1e-05)


def window_attend(query_rows, kv_ext):
    row_count, model_width = query_rows.shape
    head_size = model_width // HEADS
    key_count = kv_ext.shape[0]
    key_span = key_count - row_count
    query_heads = query_rows.reshape(row_count, HEADS, head_size)
    key_heads = kv_ext[:, :model_width].reshape(key_count, HEADS, head_size)
    value_heads = kv_ext[:, model_width:].reshape(key_count, HEADS, head_size)
    scores = jnp.einsum(
        "qhd,khd->hqk", query_heads, key_heads, preferred_element_type=jnp.float32
    ) * head_size ** (-0.5)
    offset = lax.broadcasted_iota(jnp.int32, (row_count, key_count), 1) - lax.broadcasted_iota(
        jnp.int32, (row_count, key_count), 0
    )
    inside = jnp.logical_and(offset >= 0, offset < key_span)
    scores = jnp.where(inside[None, :, :], scores, -1e30)
    raised = jnp.exp(scores - jnp.max(scores, axis=-1, keepdims=True))
    weights = (raised / jnp.sum(raised, axis=-1, keepdims=True)).astype(jnp.bfloat16)
    attended = jnp.einsum("hqk,khd->qhd", weights, value_heads, preferred_element_type=jnp.float32)
    return attended.reshape(row_count, model_width).astype(jnp.bfloat16)


def split_heads(matrix):
    row_count, model_width = matrix.shape
    return matrix.reshape(row_count, HEADS, model_width // HEADS).transpose(1, 0, 2)


def head_partial(operands):
    query_head, key_head, value_head = operands
    scores = lax.dot_general(
        query_head, key_head, (((1,), (1,)), ((), ())), preferred_element_type=jnp.float32
    ) * query_head.shape[1] ** (-0.5)
    local_max = jnp.max(scores, axis=1)
    raised = jnp.exp(scores - local_max[:, None]).astype(jnp.bfloat16)
    total = jnp.sum(raised.astype(jnp.float32), axis=1)
    mixed = jnp.dot(raised, value_head, preferred_element_type=jnp.float32)
    return (local_max, total, mixed)


def scale_heads(mixed, factor):
    query_count, model_width = mixed.shape
    head_count = factor.shape[0]
    shaped = mixed.reshape(query_count, head_count, model_width // head_count)
    return (shaped * factor.T[:, :, None]).reshape(query_count, model_width)


def loss_coefficients(
    sigma, target, matched, intersection, predicted, truth_count, hits_total, model_width
):
    denom = predicted + truth_count + 1.0
    slope = -2.0 / denom
    level = (2.0 * intersection + 1.0) / (denom * denom)
    dice_part = hits_total * (slope[:, None] * target + level[:, None]) * sigma * (1.0 - sigma)
    return (matched[:, None] * (sigma - target + dice_part) * model_width ** (-0.5)).astype(
        jnp.bfloat16
    )


def body(
    hits,
    enc_qkv,
    enc_out,
    enc_up,
    enc_down,
    queries,
    cross_q,
    cross_kv,
    cross_out,
    mask_first,
    mask_second,
    truth,
    match,
):
    model_width = hits.shape[1]
    local_hits = hits.shape[0]
    query_count = queries.shape[0]
    hits_total = float(local_hits * lax.axis_size("phi") * lax.axis_size("query"))
    track_count = query_count * lax.axis_size("query") // 2
    normed = norm_rows(hits).astype(jnp.bfloat16)
    projected = jnp.dot(normed, enc_qkv, preferred_element_type=jnp.float32).astype(jnp.bfloat16)
    extended = extended_2(projected[:, model_width:], ((("phi", "query"), 0),), WIN // 2)
    block_rows = local_hits // 2
    span = extended.shape[0] - local_hits
    attended = jnp.concatenate(
        [
            window_attend(
                projected[b * block_rows : (b + 1) * block_rows, :model_width],
                extended[b * block_rows : b * block_rows + block_rows + span],
            )
            for b in range(2)
        ]
    )
    residual = hits.astype(jnp.float32) + jnp.dot(
        attended, enc_out, preferred_element_type=jnp.float32
    )
    upper = jax.nn.gelu(
        jnp.dot(
            norm_rows(residual).astype(jnp.bfloat16), enc_up, preferred_element_type=jnp.float32
        ),
        approximate=True,
    ).astype(jnp.bfloat16)
    encoded = (residual + jnp.dot(upper, enc_down, preferred_element_type=jnp.float32)).astype(
        jnp.bfloat16
    )
    local_kv = jnp.dot(
        norm_rows(encoded).astype(jnp.bfloat16), cross_kv, preferred_element_type=jnp.float32
    ).astype(jnp.bfloat16)
    shifted = truth + 1
    digits = jnp.stack([shifted // 256, shifted % 256], axis=1).astype(jnp.bfloat16)
    digits = jnp.pad(digits, ((0, 0), (0, 126)))
    gathered = lax.all_gather(
        jnp.concatenate([local_kv, encoded, digits], axis=1), "query", axis=0, tiled=True
    )
    group_kv = gathered[:, : 2 * model_width]
    group_hits = gathered[:, 2 * model_width : 3 * model_width]
    group_digits = gathered[:, 3 * model_width :].astype(jnp.int32)
    group_truth = group_digits[:, 0] * 256 + group_digits[:, 1] - 1
    query_proj = jnp.dot(queries, cross_q, preferred_element_type=jnp.float32).astype(jnp.bfloat16)
    head_size = model_width // HEADS
    group_count = group_kv.shape[0]
    query_heads = query_proj.reshape(query_count, HEADS, head_size)
    key_heads = group_kv[:, :model_width].reshape(group_count, HEADS, head_size)
    value_heads = group_kv[:, model_width:].reshape(group_count, HEADS, head_size)
    scores = jnp.einsum(
        "qhd,khd->hqk", query_heads, key_heads, preferred_element_type=jnp.float32
    ) * head_size ** (-0.5)
    local_max = jnp.max(scores, axis=-1)
    raised = jnp.exp(scores - local_max[..., None]).astype(jnp.bfloat16)
    local_total = jnp.sum(raised.astype(jnp.float32), axis=-1)
    local_mixed = jnp.einsum(
        "hqk,khd->qhd", raised, value_heads, preferred_element_type=jnp.float32
    ).reshape(query_count, model_width)
    (_, total), mixed = butterfly(
        (jnp.stack([local_max, local_total]), local_mixed.astype(jnp.bfloat16)),
        "phi",
        softmax_combine,
        ordered=True,
    )
    mixed = mixed.astype(jnp.float32)
    context = scale_heads(mixed, 1.0 / total).astype(jnp.bfloat16)
    mixed_queries = queries.astype(jnp.float32) + jnp.dot(
        context, cross_out, preferred_element_type=jnp.float32
    )
    mask_hidden = jax.nn.relu(
        jnp.dot(
            norm_rows(mixed_queries).astype(jnp.bfloat16),
            mask_first,
            preferred_element_type=jnp.float32,
        )
    ).astype(jnp.bfloat16)
    mask_embed = jnp.dot(mask_hidden, mask_second, preferred_element_type=jnp.float32).astype(
        jnp.bfloat16
    )
    pair_hits = group_hits
    pair_digits = gathered[:, 3 * model_width : 3 * model_width + 2]
    for distance in (2, 1):
        pair_hits, pair_digits = partner_rows(pair_hits, pair_digits, distance)
    pair_digits = pair_digits.astype(jnp.int32)
    pair_truth = pair_digits[:, 0] * 256 + pair_digits[:, 1] - 1
    logits = lax.dot_general(
        mask_embed, pair_hits, (((1,), (1,)), ((), ())), preferred_element_type=jnp.float32
    ) * model_width ** (-0.5)
    sigma = jax.nn.sigmoid(logits)
    matched_flag = match < track_count
    matched = matched_flag.astype(jnp.float32)
    target = jnp.logical_and(match[:, None] == pair_truth[None, :], matched_flag[:, None]).astype(
        jnp.float32
    )
    intersection, predicted, truth_count = butterfly(
        jnp.stack(
            [jnp.sum(sigma * target, axis=1), jnp.sum(sigma, axis=1), jnp.sum(target, axis=1)]
        ),
        "phi",
        add_trees,
        distance=4,
    )
    mask_fill = predicted / hits_total
    coef = loss_coefficients(
        sigma, target, matched, intersection, predicted, truth_count, hits_total, model_width
    )
    mask_grad = narrow_butterfly(
        jnp.dot(coef, pair_hits, preferred_element_type=jnp.float32), "phi", distance=4
    )
    group_count = group_hits.shape[0]
    own_coef = lax.dynamic_slice_in_dim(
        coef,
        ((lax.axis_index("phi") % 2) * 2 + (lax.axis_index("phi") // 2) % 2) * group_count,
        group_count,
        axis=1,
    )
    hit_grad = reduce_scatter_rows(
        lax.dot_general(
            own_coef, mask_embed, (((0,), (0,)), ((), ())), preferred_element_type=jnp.float32
        ),
        "query",
    )
    return (encoded, mask_embed, hit_grad, mask_grad, mask_fill)


def solution(mesh):
    return jax.shard_map(
        body,
        mesh=mesh,
        in_specs=(
            P(("event", "phi", "query"), None),
            P(),
            P(),
            P(),
            P(),
            P("query", None),
            P(),
            P(),
            P(),
            P(),
            P(),
            P(("event", "phi", "query")),
            P(("event", "query")),
        ),
        out_specs=(
            P(("event", "phi", "query"), None),
            P(("event", "query"), None),
            P(("event", "phi", "query"), None),
            P(("event", "query"), None),
            P(("event", "query")),
        ),
        check_vma=False,
    )
```
